256 devices in a mesh: gz: 32 (over y_lo, z, core), gy: 8 (over x, y_hi).
Axes of the slice: x: 4, y: 4 (y_hi: 2, y_lo: 2; y = y_hi * 2 + y_lo), z: 8, core: 2. Of those that a mesh axis runs over, the one named last changes fastest.
Arguments:
- density: float32 [320, 128, 2048], P('gz', 'gy'), may hold values from -6 to 6
- dilations: int32 [3], replicated, may hold values from 1 to 4, as said below
- owner_rank: int32 [65536, 1], P(('gz', 'gy')), may hold values from 0 to 7; in each aligned block of 256 rows (0 to 255, 256 to 511, ...) at most 128 rows name the same one
- owner_slot: int32 [65536], P(('gz', 'gy')), may hold values from 0 to 255
- base_cell: int32 [65536], P(('gz', 'gy')), may hold values from 0 to 276479
- corner_weights: float32 [8, 65536], P(None, ('gz', 'gy')), may hold values from 0.05 to 1
Outputs:
- response: float32 [320, 128, 2048], P('gz', 'gy')
- catalogue: float32 [3, 65536], P(None, ('gz', 'gy'))
The draws below stay inside these ranges and needn't reach their ends.
Inputs may be any that keep to these rules, and one draw needn't show every extreme that they name: `dilations`: one level has dilation 4 and another has dilation 1. `owner_rank`: the entries listed on one device name one owner at most 128 times; some owner is named exactly 128 times by some device.
All inputs are finite; a program needn't handle non-finite values.
Results may differ from the reference program's by a relative error of at most 0.00014.
Values sent between devices are 32-bit elements; how exact they have to be, the bound alone decides.
No kernel may reach another device: no remote copies, remote signals or barrier semaphores. Data moves between devices by JAX's collectives and lax.ppermute only.
A program may use at most 192 MiB of HBM per device.

```python
import math
import jax
import jax.numpy as jnp
import numpy as np

SCALES = 3
DMAX = 4
CZ = 10
CY = 16
NX = 2048
NZ = 320
NY = 128
HSLOT = 256
CAP = 128
HOWN = 256
SLOTS = 65536
N_GZ = 32
N_GY = 8


def draw_dilations(key, part):
    key_values, key_pick = jax.random.split(key)
    spacing = jax.random.randint(key_values, (SCALES,), 1, DMAX + 1)
    chosen = jax.random.randint(key_pick, (), 0, SCALES)
    levels = jnp.arange(SCALES)
    spacing = jnp.where(levels == chosen, DMAX, spacing)
    spacing = jnp.where(levels == (chosen + 1) % SCALES, 1, spacing)
    return spacing.astype(jnp.int32)


def set_ends(drawn, rng, least, top_value):
    spot = [jax.random.randint(jax.random.fold_in(rng, axis), (), 0, length) for axis, length in enumerate(drawn.shape)]
    widest = drawn.shape.index(max(drawn.shape))
    next_to = spot[:widest] + [(spot[widest] + 1) % drawn.shape[widest]] + spot[widest + 1:]
    return drawn.at[tuple(spot)].set(least).at[tuple(next_to)].set(top_value)


def level_of(rng, dims, cuts, low, largest):
    def one(axis_at, parts):
        steps = jax.random.uniform(jax.random.fold_in(jax.random.fold_in(rng, 6), axis_at), (parts,), jnp.float32, low / len(cuts), largest / len(cuts))
        return jnp.repeat(jnp.exp(steps), dims[axis_at] // parts).reshape((-1,) + (1,) * (len(dims) - axis_at - 1))

    loudness = one(*cuts[0])
    for cut in cuts[1:]:
        loudness = loudness * one(*cut)
    return loudness


def routed_block(rng, own, number, rows, number_of, top, limit, slope):
    order = jax.random.permutation(rng, number_of)
    packed, common = shares(number_of, rows * top, limit, slope, True), shares(number_of, rows * top, limit, slope, False)
    places = jnp.arange(number_of)

    def named(lengths, rotation):
        used = int((lengths > 0).sum())
        fixed = max(1, used // 4)
        moved = fixed + (places - fixed + rotation * (used - fixed)) % max(1, number_of - fixed)
        return jnp.zeros((number_of,), jnp.int32).at[order[jnp.where(places < fixed, places, moved)]].set(jnp.asarray(lengths, jnp.int32))

    lengths = jnp.where(number % 4 == 0, named(packed, number // 4), named(common, number - number // 4 - 1))
    mixed = jax.random.permutation(jax.random.fold_in(own, 3), number_of)
    giver, sink = mixed[0:number_of // 2 * 2:2], mixed[1:number_of // 2 * 2:2]
    room = jnp.minimum(lengths[giver] - 1, limit - lengths[sink]) // 2
    room = jnp.where((giver == order[0]) | (sink == order[0]) | (lengths[sink] == 0), 0, jnp.maximum(room, 0))
    moved = jax.random.randint(jax.random.fold_in(own, 4), (number_of // 2,), 0, 1 << 20) % (room + 1)
    lengths = lengths.at[giver].add(-moved).at[sink].add(moved)
    items = jnp.searchsorted(jnp.cumsum(lengths), jnp.arange(rows * top), side="right").astype(jnp.int32)
    listing = items.reshape(top, rows).T
    listing = listing[jax.random.permutation(jax.random.fold_in(own, 1), rows)]
    rotation = jax.random.randint(jax.random.fold_in(own, 2), (rows, 1), 0, top)
    return jnp.take_along_axis(listing, (jnp.arange(top)[None, :] + rotation) % top, axis=1)


def shares(number_of, total, bound, lean, full):
    portions = [(1 << 20) // math.isqrt(grade ** lean) + 1 for grade in range(1, number_of + 1)]
    largest = bound if full else min(bound, max(-(-total // number_of), total * portions[0] // sum(portions)))
    least = 1 if total - largest >= number_of - 1 else 0
    holding, surplus = [largest] + [least] * (number_of - 1), total - largest - least * (number_of - 1)
    while surplus > 0:
        movable = [i for i in range(1, number_of) if holding[i] < largest] or [i for i in range(1, number_of) if holding[i] < bound]
        whole, budget = sum([portions[i] for i in movable]), surplus
        for i in movable:
            addition = min(bound - holding[i], max(1, budget * portions[i] // whole), surplus)
            holding[i] = holding[i] + addition
            surplus = surplus - addition
    return np.array(holding)


def noise(own_key, dims, deviation, reach, pieces=(), held_as=jnp.bfloat16):
    gain = level_of(own_key, dims, pieces, -0.22, 0.18) if pieces else 1.0
    drawn = jax.random.normal(own_key, dims, jnp.float32) * deviation * gain
    return jnp.minimum(jnp.maximum(drawn, -reach), reach).astype(held_as)


def setup_inputs(seed: int = 0) -> dict:
    arg_keys = jax.random.split(jax.random.key(seed), 7)
    density = noise(arg_keys[0], (NZ, NY, NX), 1.0, 6.0, ((0, 32), (1, 8)), jnp.float32)
    dilations = draw_dilations(jax.random.fold_in(arg_keys[6], 71), 0)
    owner_rank_keys = jax.random.split(jax.random.fold_in(arg_keys[2], 1), SLOTS // HSLOT)
    owner_rank_turns = jax.random.permutation(jax.random.fold_in(arg_keys[2], 3), SLOTS // HSLOT)
    owner_rank = jax.vmap(lambda own, number: routed_block(jax.random.fold_in(arg_keys[2], 2), own, number, HSLOT, N_GY, 1, CAP, 2))(owner_rank_keys, owner_rank_turns).reshape((SLOTS, 1))
    owner_slot = set_ends(jax.random.randint(arg_keys[3], (SLOTS,), 0, HOWN), jax.random.fold_in(arg_keys[3], 1), 0, HOWN - 1).astype(jnp.int32)
    base_cell = set_ends(jax.random.randint(arg_keys[4], (SLOTS,), 0, (CZ - 1) * (CY - 1) * NX), jax.random.fold_in(arg_keys[4], 1), 0, ((CZ - 1) * (CY - 1) * NX) - 1).astype(jnp.int32)
    corner_weights = jnp.clip(0.05 + 0.95 * jax.random.uniform(arg_keys[5], (8, SLOTS), jnp.float32) ** level_of(arg_keys[5], (8, SLOTS), ((1, 256),), -0.2, 0.2), 0.05, 1.0)
    return {"density": density, "dilations": dilations, "owner_rank": owner_rank, "owner_slot": owner_slot, "base_cell": base_cell, "corner_weights": corner_weights}


tap_weights = (0.0625, 0.25, 0.375, 0.25, 0.0625)
hessian_scale = 4.0


def smooth_cycle(field_data, dilation, along_dim):
    running = None
    for offset in range(5):
        summand = tap_weights[offset] * jnp.roll(field_data, -(offset - 2) * dilation, axis=along_dim)
        running = summand if running is None else running + summand
    return running


def invariants(curve_zz, curve_yy, curve_xx, curve_zy, curve_zx, curve_yx):
    trace_sum = curve_xx + curve_yy + curve_zz
    minor_sum = curve_xx * curve_yy + curve_xx * curve_zz + curve_yy * curve_zz - curve_zy * curve_zy - curve_zx * curve_zx - curve_yx * curve_yx
    return (trace_sum * trace_sum / 3.0 - minor_sum) * jax.nn.sigmoid(-trace_sum)


def signature(smoothed):
    centre = smoothed
    above_z = jnp.roll(smoothed, -1, 0)
    below_z = jnp.roll(smoothed, 1, 0)
    above_y = jnp.roll(smoothed, -1, 1)
    below_y = jnp.roll(smoothed, 1, 1)
    curve_zz = hessian_scale * (above_z - 2.0 * centre + below_z)
    curve_yy = hessian_scale * (above_y - 2.0 * centre + below_y)
    curve_xx = hessian_scale * (jnp.roll(centre, -1, 2) - 2.0 * centre + jnp.roll(centre, 1, 2))
    curve_zy = hessian_scale * 0.25 * (jnp.roll(above_z, -1, 1) - jnp.roll(above_z, 1, 1) - jnp.roll(below_z, -1, 1) + jnp.roll(below_z, 1, 1))
    curve_zx = hessian_scale * 0.25 * (jnp.roll(above_z, -1, 2) - jnp.roll(above_z, 1, 2) - jnp.roll(below_z, -1, 2) + jnp.roll(below_z, 1, 2))
    curve_yx = hessian_scale * 0.25 * (jnp.roll(above_y, -1, 2) - jnp.roll(above_y, 1, 2) - jnp.roll(below_y, -1, 2) + jnp.roll(below_y, 1, 2))
    return invariants(curve_zz, curve_yy, curve_xx, curve_zy, curve_zx, curve_yx)


def reference(density, dilations, owner_rank, owner_slot, base_cell, corner_weights):
    response = None
    levels = []
    for level_index in range(SCALES):
        dilation = dilations[level_index]
        smoothed = smooth_cycle(density, dilation, 1)
        smoothed = smooth_cycle(smoothed, dilation, 0)
        smoothed = smooth_cycle(smoothed, dilation, 2)
        feature = signature(smoothed)
        response = feature if response is None else jnp.maximum(response, feature)
        levels.append(feature)
    feature_table = jnp.stack(levels)
    slot_rows = jnp.arange(SLOTS, dtype=jnp.int32)
    device = slot_rows // HSLOT
    z_group = device // N_GY
    y_group = device % N_GY
    plane = (CY - 1) * NX
    z_index = base_cell // plane
    remainder = base_cell % plane
    y_index = remainder // NX
    x_index = remainder % NX
    partial_value = None
    corner = 0
    for step_z in (0, 1):
        for step_y in (0, 1):
            for step_x in (0, 1):
                picked = feature_table[:, z_group * CZ + z_index + step_z, y_group * CY + y_index + step_y, (x_index + step_x) % NX]
                summand = corner_weights[corner] * picked
                partial_value = summand if partial_value is None else partial_value + summand
                corner += 1
    column = z_group * (N_GY * HOWN) + owner_rank[:, 0] * HOWN + owner_slot
    catalogue = jnp.zeros((SCALES, N_GZ * N_GY * HOWN), jnp.float32).at[:, column].add(partial_value)
    return response, catalogue
```

```python
import jax
import jax.numpy as jnp
from jax import lax
from jax.sharding import PartitionSpec as P

SCALES = 3
HALO = 9
HOWN = 256


tap_weights = (0.0625, 0.25, 0.375, 0.25, 0.0625)
hessian_scale = 4.0


def with_halo(block, sides, width):
    for axis, dim in sides:
        count = lax.axis_size(axis)
        forward = [(i, i + 1) for i in range(count - 1)]
        forward.append((count - 1, 0))
        backward = [(target, source) for source, target in forward]
        low = lax.ppermute(
            lax.slice_in_dim(block, block.shape[dim] - width, None, axis=dim), axis, forward
        )
        high = lax.ppermute(lax.slice_in_dim(block, 0, width, axis=dim), axis, backward)
        block = jnp.concatenate([low, block, high], axis=dim)
    return block


def smooth_padded(field_data, dilation, along_dim, extent):
    running = None
    for offset in range(5):
        start_at = HALO - 1 + (offset - 2) * dilation
        summand = tap_weights[offset] * lax.dynamic_slice_in_dim(
            field_data, start_at, extent + 2, along_dim
        )
        running = summand if running is None else running + summand
    return running


def smooth_periodic(field_data, dilation):
    running = None
    for offset in range(5):
        summand = tap_weights[offset] * jnp.roll(field_data, -(offset - 2) * dilation, axis=2)
        running = summand if running is None else running + summand
    return running


def invariants(curve_zz, curve_yy, curve_xx, curve_zy, curve_zx, curve_yx):
    trace_sum = curve_xx + curve_yy + curve_zz
    minor_sum = (
        curve_xx * curve_yy
        + curve_xx * curve_zz
        + curve_yy * curve_zz
        - curve_zy * curve_zy
        - curve_zx * curve_zx
        - curve_yx * curve_yx
    )
    return (trace_sum * trace_sum / 3.0 - minor_sum) * jax.nn.sigmoid(-trace_sum)


def signature(smoothed):
    centre = smoothed[1:-1, 1:-1]
    above_z = smoothed[2:, 1:-1]
    below_z = smoothed[:-2, 1:-1]
    above_y = smoothed[1:-1, 2:]
    below_y = smoothed[1:-1, :-2]
    curve_zz = hessian_scale * (above_z - 2.0 * centre + below_z)
    curve_yy = hessian_scale * (above_y - 2.0 * centre + below_y)
    curve_xx = hessian_scale * (jnp.roll(centre, -1, 2) - 2.0 * centre + jnp.roll(centre, 1, 2))
    curve_zy = (
        hessian_scale
        * 0.25
        * (smoothed[2:, 2:] - smoothed[2:, :-2] - smoothed[:-2, 2:] + smoothed[:-2, :-2])
    )
    curve_zx = (
        hessian_scale
        * 0.25
        * (
            jnp.roll(above_z, -1, 2)
            - jnp.roll(above_z, 1, 2)
            - jnp.roll(below_z, -1, 2)
            + jnp.roll(below_z, 1, 2)
        )
    )
    curve_yx = (
        hessian_scale
        * 0.25
        * (
            jnp.roll(above_y, -1, 2)
            - jnp.roll(above_y, 1, 2)
            - jnp.roll(below_y, -1, 2)
            + jnp.roll(below_y, 1, 2)
        )
    )
    return invariants(curve_zz, curve_yy, curve_xx, curve_zy, curve_zx, curve_yx)


def per_device(density, dilations, owner_rank, owner_slot, base_cell, corner_weights):
    slab_depth = density.shape[0]
    band_rows = density.shape[1]
    row_length = density.shape[2]
    banded = with_halo(density, (("gy", 1),), HALO)
    response = None
    levels = []
    for level_index in range(SCALES):
        dilation = dilations[level_index]
        along_y = with_halo(smooth_padded(banded, dilation, 1, band_rows), (("gz", 0),), HALO)
        along_z = smooth_padded(along_y, dilation, 0, slab_depth)
        smoothed = smooth_periodic(along_z, dilation)
        feature = signature(smoothed)
        response = feature if response is None else jnp.maximum(response, feature)
        levels.append(feature.reshape(-1))
    feature_table = jnp.stack(levels)
    plane = (band_rows - 1) * row_length
    z_index = base_cell // plane
    remainder = base_cell % plane
    y_index = remainder // row_length
    x_index = remainder % row_length
    partial_value = None
    corner = 0
    for step_z in (0, 1):
        for step_y in (0, 1):
            for step_x in (0, 1):
                cell_index = (
                    (z_index + step_z) * (band_rows * row_length)
                    + (y_index + step_y) * row_length
                    + (x_index + step_x) % row_length
                )
                summand = corner_weights[corner] * feature_table[:, cell_index]
                partial_value = summand if partial_value is None else partial_value + summand
                corner += 1
    owner_group = owner_rank[:, 0]
    groups = lax.axis_size("gy")
    column = owner_group * HOWN + owner_slot
    onehot = (column[:, None] == jnp.arange(groups * HOWN, dtype=jnp.int32)[None, :]).astype(
        jnp.float32
    )
    spread = jnp.dot(
        partial_value, onehot, precision=lax.Precision.HIGHEST, preferred_element_type=jnp.float32
    )
    exchanged = lax.all_to_all(
        spread.reshape(SCALES, groups, HOWN), "gy", split_axis=1, concat_axis=1, tiled=True
    )
    catalogue = jnp.sum(exchanged, axis=1)
    return (response, catalogue)


def solution(mesh):
    placed = (
        P("gz", "gy", None),
        P(),
        P(("gz", "gy"), None),
        P(("gz", "gy")),
        P(("gz", "gy")),
        P(None, ("gz", "gy")),
    )
    return jax.shard_map(
        per_device,
        mesh=mesh,
        in_specs=placed,
        out_specs=(P("gz", "gy", None), P(None, ("gz", "gy"))),
        check_vma=False,
    )
```

```python
import jax
import jax.numpy as jnp
from jax import lax
from jax.experimental import pallas as pl
from jax.experimental.pallas import tpu as pltpu
from jax.sharding import PartitionSpec as P

SCALES = 3
HALO = 9
HOWN = 256
DMAX = 4


tap_weights = (0.0625, 0.25, 0.375, 0.25, 0.0625)
hessian_scale = 4.0


def with_halo(block, sides, width):
    for axis, dim in sides:
        count = lax.axis_size(axis)
        forward = [(i, i + 1) for i in range(count - 1)]
        forward.append((count - 1, 0))
        backward = [(target, source) for source, target in forward]
        low = lax.ppermute(
            lax.slice_in_dim(block, block.shape[dim] - width, None, axis=dim), axis, forward
        )
        high = lax.ppermute(lax.slice_in_dim(block, 0, width, axis=dim), axis, backward)
        block = jnp.concatenate([low, block, high], axis=dim)
    return block


def smooth_padded(field_data, dilation, along_dim, extent):
    running = None
    for offset in range(5):
        start_at = HALO - 1 + (offset - 2) * dilation
        summand = tap_weights[offset] * lax.dynamic_slice_in_dim(
            field_data, start_at, extent + 2, along_dim
        )
        running = summand if running is None else running + summand
    return running


def smooth_periodic(field_data, dilation):
    running = None
    for offset in range(5):
        summand = tap_weights[offset] * jnp.roll(field_data, -(offset - 2) * dilation, axis=2)
        running = summand if running is None else running + summand
    return running


def level_kernel(dilation, slab_depth, band_rows, row_length):
    planes = slab_depth + 2

    def kernel(along_y_ref, prev_ref, feature_ref, best_ref, smoothed_ref):
        def smooth_plane(plane, carry):
            along_z = None
            for offset in range(5):
                summand = tap_weights[offset] * along_y_ref[HALO - 1 + plane + (offset - 2) * dilation]
                along_z = summand if along_z is None else along_z + summand
            running = None
            for offset in range(5):
                shift = (-(offset - 2) * dilation) % row_length
                moved = along_z if shift == 0 else pltpu.roll(along_z, shift, 1)
                summand = tap_weights[offset] * moved
                running = summand if running is None else running + summand
            smoothed_ref[plane] = running
            return carry

        lax.fori_loop(0, planes, smooth_plane, 0)

        def feature_plane(z, carry):
            for half in range(band_rows // 8):
                y0 = half * 8

                def at(dz, dy):
                    return smoothed_ref[z + 1 + dz, pl.ds(1 + y0 + dy, 8), :]

                centre = at(0, 0)
                above_z = at(1, 0)
                below_z = at(-1, 0)
                above_y = at(0, 1)
                below_y = at(0, -1)

                def left(v):
                    return pltpu.roll(v, row_length - 1, 1)

                def right(v):
                    return pltpu.roll(v, 1, 1)

                curve_zz = hessian_scale * (above_z - 2.0 * centre + below_z)
                curve_yy = hessian_scale * (above_y - 2.0 * centre + below_y)
                curve_xx = hessian_scale * (left(centre) - 2.0 * centre + right(centre))
                curve_zy = (hessian_scale * 0.25) * (at(1, 1) - at(1, -1) - at(-1, 1) + at(-1, -1))
                curve_zx = (hessian_scale * 0.25) * (
                    left(above_z) - right(above_z) - left(below_z) + right(below_z)
                )
                curve_yx = (hessian_scale * 0.25) * (
                    left(above_y) - right(above_y) - left(below_y) + right(below_y)
                )
                trace_sum = curve_xx + curve_yy + curve_zz
                minor_sum = (
                    curve_xx * curve_yy
                    + curve_xx * curve_zz
                    + curve_yy * curve_zz
                    - curve_zy * curve_zy
                    - curve_zx * curve_zx
                    - curve_yx * curve_yx
                )
                value = (trace_sum * trace_sum / 3.0 - minor_sum) * (1.0 / (1.0 + jnp.exp(trace_sum)))
                feature_ref[z, pl.ds(y0, 8), :] = value
                best_ref[z, pl.ds(y0, 8), :] = jnp.maximum(prev_ref[z, pl.ds(y0, 8), :], value)
            return carry

        lax.fori_loop(0, slab_depth, feature_plane, 0)

    def run(along_y, prev):
        block = jax.ShapeDtypeStruct((slab_depth, band_rows, row_length), jnp.float32)
        return pl.pallas_call(
            kernel,
            out_shape=(block, block),
            scratch_shapes=[pltpu.VMEM((planes, band_rows + 2, row_length), jnp.float32)],
            compiler_params=pltpu.CompilerParams(vmem_limit_bytes=56 * 1024 * 1024),
        )(along_y, prev)

    return run


def level_feature(along_y, prev, dilation):
    slab_depth = prev.shape[0]
    band_rows = prev.shape[1]
    row_length = prev.shape[2]
    branches = [
        level_kernel(d, slab_depth, band_rows, row_length) for d in range(1, DMAX + 1)
    ]
    pick = jnp.clip(dilation - 1, 0, DMAX - 1)
    return lax.switch(pick, branches, along_y, prev)


def invariants(curve_zz, curve_yy, curve_xx, curve_zy, curve_zx, curve_yx):
    trace_sum = curve_xx + curve_yy + curve_zz
    minor_sum = (
        curve_xx * curve_yy
        + curve_xx * curve_zz
        + curve_yy * curve_zz
        - curve_zy * curve_zy
        - curve_zx * curve_zx
        - curve_yx * curve_yx
    )
    return (trace_sum * trace_sum / 3.0 - minor_sum) * jax.nn.sigmoid(-trace_sum)


def signature(smoothed):
    centre = smoothed[1:-1, 1:-1]
    above_z = smoothed[2:, 1:-1]
    below_z = smoothed[:-2, 1:-1]
    above_y = smoothed[1:-1, 2:]
    below_y = smoothed[1:-1, :-2]
    curve_zz = hessian_scale * (above_z - 2.0 * centre + below_z)
    curve_yy = hessian_scale * (above_y - 2.0 * centre + below_y)
    curve_xx = hessian_scale * (jnp.roll(centre, -1, 2) - 2.0 * centre + jnp.roll(centre, 1, 2))
    curve_zy = (
        hessian_scale
        * 0.25
        * (smoothed[2:, 2:] - smoothed[2:, :-2] - smoothed[:-2, 2:] + smoothed[:-2, :-2])
    )
    curve_zx = (
        hessian_scale
        * 0.25
        * (
            jnp.roll(above_z, -1, 2)
            - jnp.roll(above_z, 1, 2)
            - jnp.roll(below_z, -1, 2)
            + jnp.roll(below_z, 1, 2)
        )
    )
    curve_yx = (
        hessian_scale
        * 0.25
        * (
            jnp.roll(above_y, -1, 2)
            - jnp.roll(above_y, 1, 2)
            - jnp.roll(below_y, -1, 2)
            + jnp.roll(below_y, 1, 2)
        )
    )
    return invariants(curve_zz, curve_yy, curve_xx, curve_zy, curve_zx, curve_yx)


def per_device(density, dilations, owner_rank, owner_slot, base_cell, corner_weights):
    slab_depth = density.shape[0]
    band_rows = density.shape[1]
    row_length = density.shape[2]
    banded = with_halo(density, (("gy", 1),), HALO)
    response = jnp.full(density.shape, -jnp.inf, jnp.float32)
    levels = []
    for level_index in range(SCALES):
        dilation = dilations[level_index]
        along_y = with_halo(smooth_padded(banded, dilation, 1, band_rows), (("gz", 0),), HALO)
        feature, response = level_feature(along_y, response, dilation)
        levels.append(feature.reshape(-1))
    feature_table = jnp.stack(levels)
    plane = (band_rows - 1) * row_length
    z_index = base_cell // plane
    remainder = base_cell % plane
    y_index = remainder // row_length
    x_index = remainder % row_length
    partial_value = None
    corner = 0
    for step_z in (0, 1):
        for step_y in (0, 1):
            for step_x in (0, 1):
                cell_index = (
                    (z_index + step_z) * (band_rows * row_length)
                    + (y_index + step_y) * row_length
                    + (x_index + step_x) % row_length
                )
                summand = corner_weights[corner] * feature_table[:, cell_index]
                partial_value = summand if partial_value is None else partial_value + summand
                corner += 1
    owner_group = owner_rank[:, 0]
    groups = lax.axis_size("gy")
    column = owner_group * HOWN + owner_slot
    onehot = (column[:, None] == jnp.arange(groups * HOWN, dtype=jnp.int32)[None, :]).astype(
        jnp.float32
    )
    spread = jnp.dot(
        partial_value, onehot, precision=lax.Precision.HIGHEST, preferred_element_type=jnp.float32
    )
    exchanged = lax.all_to_all(
        spread.reshape(SCALES, groups, HOWN), "gy", split_axis=1, concat_axis=1, tiled=True
    )
    catalogue = jnp.sum(exchanged, axis=1)
    return (response, catalogue)


def solution(mesh):
    placed = (
        P("gz", "gy", None),
        P(),
        P(("gz", "gy"), None),
        P(("gz", "gy")),
        P(("gz", "gy")),
        P(None, ("gz", "gy")),
    )
    return jax.shard_map(
        per_device,
        mesh=mesh,
        in_specs=placed,
        out_specs=(P("gz", "gy", None), P(None, ("gz", "gy"))),
        check_vma=False,
    )
```

```python
import jax
import jax.numpy as jnp
from jax import lax
from jax.experimental import pallas as pl
from jax.experimental.pallas import tpu as pltpu
from jax.sharding import PartitionSpec as P

SCALES = 3
HALO = 9
HOWN = 256
DMAX = 4


tap_weights = (0.0625, 0.25, 0.375, 0.25, 0.0625)
hessian_scale = 4.0


def with_halo(block, sides, width):
    for axis, dim in sides:
        count = lax.axis_size(axis)
        forward = [(i, i + 1) for i in range(count - 1)]
        forward.append((count - 1, 0))
        backward = [(target, source) for source, target in forward]
        low = lax.ppermute(
            lax.slice_in_dim(block, block.shape[dim] - width, None, axis=dim), axis, forward
        )
        high = lax.ppermute(lax.slice_in_dim(block, 0, width, axis=dim), axis, backward)
        block = jnp.concatenate([low, block, high], axis=dim)
    return block


def smooth_padded(field_data, dilation, along_dim, extent):
    running = None
    for offset in range(5):
        start_at = HALO - 1 + (offset - 2) * dilation
        summand = tap_weights[offset] * lax.dynamic_slice_in_dim(
            field_data, start_at, extent + 2, along_dim
        )
        running = summand if running is None else running + summand
    return running


def smooth_periodic(field_data, dilation):
    running = None
    for offset in range(5):
        summand = tap_weights[offset] * jnp.roll(field_data, -(offset - 2) * dilation, axis=2)
        running = summand if running is None else running + summand
    return running


def level_kernel(level_index, first, slab_depth, band_rows, row_length):
    planes = slab_depth + 2

    def compute(dilation, a_scr, s_scr, feature_ref, prev_ref, best_ref):
        def smooth_plane(plane, carry):
            along_z = None
            for offset in range(5):
                summand = tap_weights[offset] * a_scr[HALO - 1 + plane + (offset - 2) * dilation]
                along_z = summand if along_z is None else along_z + summand
            running = None
            for offset in range(5):
                shift = (-(offset - 2) * dilation) % row_length
                moved = along_z if shift == 0 else pltpu.roll(along_z, shift, 1)
                summand = tap_weights[offset] * moved
                running = summand if running is None else running + summand
            s_scr[plane] = running
            return carry

        lax.fori_loop(0, planes, smooth_plane, 0)

        def feature_plane(z, carry):
            for half in range(band_rows // 8):
                y0 = half * 8

                def at(dz, dy):
                    return s_scr[z + 1 + dz, pl.ds(1 + y0 + dy, 8), :]

                centre = at(0, 0)
                above_z = at(1, 0)
                below_z = at(-1, 0)
                above_y = at(0, 1)
                below_y = at(0, -1)

                def left(v):
                    return pltpu.roll(v, row_length - 1, 1)

                def right(v):
                    return pltpu.roll(v, 1, 1)

                curve_zz = hessian_scale * (above_z - 2.0 * centre + below_z)
                curve_yy = hessian_scale * (above_y - 2.0 * centre + below_y)
                curve_xx = hessian_scale * (left(centre) - 2.0 * centre + right(centre))
                curve_zy = (hessian_scale * 0.25) * (at(1, 1) - at(1, -1) - at(-1, 1) + at(-1, -1))
                curve_zx = (hessian_scale * 0.25) * (
                    left(above_z) - right(above_z) - left(below_z) + right(below_z)
                )
                curve_yx = (hessian_scale * 0.25) * (
                    left(above_y) - right(above_y) - left(below_y) + right(below_y)
                )
                trace_sum = curve_xx + curve_yy + curve_zz
                minor_sum = (
                    curve_xx * curve_yy
                    + curve_xx * curve_zz
                    + curve_yy * curve_zz
                    - curve_zy * curve_zy
                    - curve_zx * curve_zx
                    - curve_yx * curve_yx
                )
                value = (trace_sum * trace_sum / 3.0 - minor_sum) * (1.0 / (1.0 + jnp.exp(trace_sum)))
                feature_ref[z, pl.ds(y0, 8), :] = value
                if first:
                    best_ref[z, pl.ds(y0, 8), :] = value
                else:
                    best_ref[z, pl.ds(y0, 8), :] = jnp.maximum(prev_ref[z, pl.ds(y0, 8), :], value)
            return carry

        lax.fori_loop(0, slab_depth, feature_plane, 0)

    def kernel(*refs):
        if first:
            dil_ref, lo_hbm, mid_hbm, hi_hbm, feature_ref, best_ref, a_scr, s_scr, sems = refs
            prev_ref = None
        else:
            (dil_ref, lo_hbm, mid_hbm, hi_hbm, prev_ref, feature_ref, best_ref,
             a_scr, s_scr, sems) = refs
        copies = [
            pltpu.make_async_copy(lo_hbm, a_scr.at[pl.ds(0, HALO)], sems.at[0]),
            pltpu.make_async_copy(mid_hbm, a_scr.at[pl.ds(HALO, slab_depth)], sems.at[1]),
            pltpu.make_async_copy(hi_hbm, a_scr.at[pl.ds(HALO + slab_depth, HALO)], sems.at[2]),
        ]
        for copy in copies:
            copy.start()
        for copy in copies:
            copy.wait()
        dilation = dil_ref[level_index]
        for value in range(1, DMAX + 1):

            @pl.when(dilation == value)
            def _():
                compute(value, a_scr, s_scr, feature_ref, prev_ref, best_ref)

    def run(dilations, low, middle, high, prev):
        block = jax.ShapeDtypeStruct((slab_depth, band_rows, row_length), jnp.float32)
        anywhere = pl.BlockSpec(memory_space=pl.ANY)
        in_vmem = pl.BlockSpec(memory_space=pltpu.VMEM)
        in_specs = [pl.BlockSpec(memory_space=pltpu.SMEM), anywhere, anywhere, anywhere]
        operands = [dilations, low, middle, high]
        if not first:
            in_specs.append(in_vmem)
            operands.append(prev)
        return pl.pallas_call(
            kernel,
            out_shape=(block, block),
            in_specs=in_specs,
            out_specs=(in_vmem, in_vmem),
            scratch_shapes=[
                pltpu.VMEM((planes + 2 * HALO - 2, band_rows + 2, row_length), jnp.float32),
                pltpu.VMEM((planes, band_rows + 2, row_length), jnp.float32),
                pltpu.SemaphoreType.DMA((3,)),
            ],
            compiler_params=pltpu.CompilerParams(vmem_limit_bytes=56 * 1024 * 1024),
        )(*operands)

    return run


def z_neighbours(block, width):
    count = lax.axis_size("gz")
    forward = [(i, i + 1) for i in range(count - 1)]
    forward.append((count - 1, 0))
    backward = [(target, source) for source, target in forward]
    low = lax.ppermute(lax.slice_in_dim(block, block.shape[0] - width, None, axis=0), "gz", forward)
    high = lax.ppermute(lax.slice_in_dim(block, 0, width, axis=0), "gz", backward)
    return low, high


def invariants(curve_zz, curve_yy, curve_xx, curve_zy, curve_zx, curve_yx):
    trace_sum = curve_xx + curve_yy + curve_zz
    minor_sum = (
        curve_xx * curve_yy
        + curve_xx * curve_zz
        + curve_yy * curve_zz
        - curve_zy * curve_zy
        - curve_zx * curve_zx
        - curve_yx * curve_yx
    )
    return (trace_sum * trace_sum / 3.0 - minor_sum) * jax.nn.sigmoid(-trace_sum)


def signature(smoothed):
    centre = smoothed[1:-1, 1:-1]
    above_z = smoothed[2:, 1:-1]
    below_z = smoothed[:-2, 1:-1]
    above_y = smoothed[1:-1, 2:]
    below_y = smoothed[1:-1, :-2]
    curve_zz = hessian_scale * (above_z - 2.0 * centre + below_z)
    curve_yy = hessian_scale * (above_y - 2.0 * centre + below_y)
    curve_xx = hessian_scale * (jnp.roll(centre, -1, 2) - 2.0 * centre + jnp.roll(centre, 1, 2))
    curve_zy = (
        hessian_scale
        * 0.25
        * (smoothed[2:, 2:] - smoothed[2:, :-2] - smoothed[:-2, 2:] + smoothed[:-2, :-2])
    )
    curve_zx = (
        hessian_scale
        * 0.25
        * (
            jnp.roll(above_z, -1, 2)
            - jnp.roll(above_z, 1, 2)
            - jnp.roll(below_z, -1, 2)
            + jnp.roll(below_z, 1, 2)
        )
    )
    curve_yx = (
        hessian_scale
        * 0.25
        * (
            jnp.roll(above_y, -1, 2)
            - jnp.roll(above_y, 1, 2)
            - jnp.roll(below_y, -1, 2)
            + jnp.roll(below_y, 1, 2)
        )
    )
    return invariants(curve_zz, curve_yy, curve_xx, curve_zy, curve_zx, curve_yx)


def per_device(density, dilations, owner_rank, owner_slot, base_cell, corner_weights):
    slab_depth = density.shape[0]
    band_rows = density.shape[1]
    row_length = density.shape[2]
    banded = with_halo(density, (("gy", 1),), HALO)
    response = None
    features = []
    for level_index in range(SCALES):
        dilation = dilations[level_index]
        along_y = smooth_padded(banded, dilation, 1, band_rows)
        low, high = z_neighbours(along_y, HALO)
        run = level_kernel(level_index, level_index == 0, slab_depth, band_rows, row_length)
        feature, response = run(dilations, low, along_y, high, response)
        features.append(feature.reshape(slab_depth * band_rows, row_length))
    plane = (band_rows - 1) * row_length
    z_index = base_cell // plane
    remainder = base_cell % plane
    y_index = remainder // row_length
    x_index = remainder % row_length
    entries = base_cell.shape[0]
    steps = jnp.arange(2, dtype=jnp.int32)
    target_x = ((x_index[:, None] + steps[None, :]) % row_length).reshape(-1)
    pick_x = (
        jnp.arange(row_length, dtype=jnp.int32)[:, None] == target_x[None, :]
    ).astype(jnp.float32)
    cells = jnp.arange(slab_depth * band_rows, dtype=jnp.int32)[:, None, None]
    weight_grid = None
    for step_z in (0, 1):
        for step_y in (0, 1):
            row = (z_index + step_z) * band_rows + y_index + step_y
            corner = 4 * step_z + 2 * step_y
            weights = jnp.stack([corner_weights[corner], corner_weights[corner + 1]], axis=1)
            term = jnp.where(cells == row[None, :, None], weights[None, :, :], 0.0)
            weight_grid = term if weight_grid is None else weight_grid + term
    weight_grid = weight_grid.reshape(slab_depth * band_rows, entries * 2)
    partials = []
    for feature in features:
        picked = jnp.dot(
            feature, pick_x, precision=lax.Precision.HIGHEST, preferred_element_type=jnp.float32
        )
        partials.append(jnp.sum((picked * weight_grid).reshape(-1, entries, 2), axis=(0, 2)))
    partial_value = jnp.stack(partials)
    owner_group = owner_rank[:, 0]
    groups = lax.axis_size("gy")
    column = owner_group * HOWN + owner_slot
    onehot = (column[:, None] == jnp.arange(groups * HOWN, dtype=jnp.int32)[None, :]).astype(
        jnp.float32
    )
    spread = jnp.dot(
        partial_value, onehot, precision=lax.Precision.HIGHEST, preferred_element_type=jnp.float32
    )
    exchanged = lax.all_to_all(
        spread.reshape(SCALES, groups, HOWN), "gy", split_axis=1, concat_axis=1, tiled=True
    )
    catalogue = jnp.sum(exchanged, axis=1)
    return (response, catalogue)


def solution(mesh):
    placed = (
        P("gz", "gy", None),
        P(),
        P(("gz", "gy"), None),
        P(("gz", "gy")),
        P(("gz", "gy")),
        P(None, ("gz", "gy")),
    )
    return jax.shard_map(
        per_device,
        mesh=mesh,
        in_specs=placed,
        out_specs=(P("gz", "gy", None), P(None, ("gz", "gy"))),
        check_vma=False,
    )
```

```python
import jax
import jax.numpy as jnp
from jax import lax
from jax.experimental import pallas as pl
from jax.experimental.pallas import tpu as pltpu
from jax.sharding import PartitionSpec as P

SCALES = 3
HALO = 9
HOWN = 256
DMAX = 4


tap_weights = (0.0625, 0.25, 0.375, 0.25, 0.0625)
hessian_scale = 4.0


def with_halo(block, sides, width):
    for axis, dim in sides:
        count = lax.axis_size(axis)
        forward = [(i, i + 1) for i in range(count - 1)]
        forward.append((count - 1, 0))
        backward = [(target, source) for source, target in forward]
        low = lax.ppermute(
            lax.slice_in_dim(block, block.shape[dim] - width, None, axis=dim), axis, forward
        )
        high = lax.ppermute(lax.slice_in_dim(block, 0, width, axis=dim), axis, backward)
        block = jnp.concatenate([low, block, high], axis=dim)
    return block


def smooth_padded(field_data, dilation, along_dim, extent):
    running = None
    for offset in range(5):
        start_at = HALO - 1 + (offset - 2) * dilation
        summand = tap_weights[offset] * lax.dynamic_slice_in_dim(
            field_data, start_at, extent + 2, along_dim
        )
        running = summand if running is None else running + summand
    return running


def smooth_periodic(field_data, dilation):
    running = None
    for offset in range(5):
        summand = tap_weights[offset] * jnp.roll(field_data, -(offset - 2) * dilation, axis=2)
        running = summand if running is None else running + summand
    return running


def level_kernel(level_index, first, slab_depth, band_rows, row_length):
    planes = slab_depth + 2

    def compute(dilation, a_scr, s_scr, feature_ref, prev_ref, best_ref):
        def smooth_plane(plane, carry):
            along_z = None
            for offset in range(5):
                summand = tap_weights[offset] * a_scr[HALO - 1 + plane + (offset - 2) * dilation]
                along_z = summand if along_z is None else along_z + summand
            running = None
            for offset in range(5):
                shift = (-(offset - 2) * dilation) % row_length
                moved = along_z if shift == 0 else pltpu.roll(along_z, shift, 1)
                summand = tap_weights[offset] * moved
                running = summand if running is None else running + summand
            s_scr[plane] = running
            return carry

        lax.fori_loop(0, planes, smooth_plane, 0)

        def feature_plane(z, carry):
            for half in range(band_rows // 8):
                y0 = half * 8

                def at(dz, dy):
                    return s_scr[z + 1 + dz, pl.ds(1 + y0 + dy, 8), :]

                centre = at(0, 0)
                above_z = at(1, 0)
                below_z = at(-1, 0)
                above_y = at(0, 1)
                below_y = at(0, -1)

                def left(v):
                    return pltpu.roll(v, row_length - 1, 1)

                def right(v):
                    return pltpu.roll(v, 1, 1)

                curve_zz = hessian_scale * (above_z - 2.0 * centre + below_z)
                curve_yy = hessian_scale * (above_y - 2.0 * centre + below_y)
                curve_xx = hessian_scale * (left(centre) - 2.0 * centre + right(centre))
                curve_zy = (hessian_scale * 0.25) * (at(1, 1) - at(1, -1) - at(-1, 1) + at(-1, -1))
                curve_zx = (hessian_scale * 0.25) * (
                    left(above_z) - right(above_z) - left(below_z) + right(below_z)
                )
                curve_yx = (hessian_scale * 0.25) * (
                    left(above_y) - right(above_y) - left(below_y) + right(below_y)
                )
                trace_sum = curve_xx + curve_yy + curve_zz
                minor_sum = (
                    curve_xx * curve_yy
                    + curve_xx * curve_zz
                    + curve_yy * curve_zz
                    - curve_zy * curve_zy
                    - curve_zx * curve_zx
                    - curve_yx * curve_yx
                )
                value = (trace_sum * trace_sum / 3.0 - minor_sum) * (1.0 / (1.0 + jnp.exp(trace_sum)))
                feature_ref[z, pl.ds(y0, 8), :] = value
                if first:
                    best_ref[z, pl.ds(y0, 8), :] = value
                else:
                    best_ref[z, pl.ds(y0, 8), :] = jnp.maximum(prev_ref[z, pl.ds(y0, 8), :], value)
            return carry

        lax.fori_loop(0, slab_depth, feature_plane, 0)

    def kernel(*refs):
        if first:
            dil_ref, lo_hbm, mid_hbm, hi_hbm, feature_ref, best_ref, a_scr, s_scr, sems = refs
            prev_ref = None
        else:
            (dil_ref, lo_hbm, mid_hbm, hi_hbm, prev_ref, feature_ref, best_ref,
             a_scr, s_scr, sems) = refs
        copies = [
            pltpu.make_async_copy(lo_hbm, a_scr.at[pl.ds(0, HALO)], sems.at[0]),
            pltpu.make_async_copy(mid_hbm, a_scr.at[pl.ds(HALO, slab_depth)], sems.at[1]),
            pltpu.make_async_copy(hi_hbm, a_scr.at[pl.ds(HALO + slab_depth, HALO)], sems.at[2]),
        ]
        for copy in copies:
            copy.start()
        for copy in copies:
            copy.wait()
        dilation = dil_ref[level_index]
        for value in range(1, DMAX + 1):

            @pl.when(dilation == value)
            def _():
                compute(value, a_scr, s_scr, feature_ref, prev_ref, best_ref)

    def run(dilations, low, middle, high, prev):
        block = jax.ShapeDtypeStruct((slab_depth, band_rows, row_length), jnp.float32)
        anywhere = pl.BlockSpec(memory_space=pl.ANY)
        in_vmem = pl.BlockSpec(memory_space=pltpu.VMEM)
        in_specs = [pl.BlockSpec(memory_space=pltpu.SMEM), anywhere, anywhere, anywhere]
        operands = [dilations, low, middle, high]
        if not first:
            in_specs.append(in_vmem)
            operands.append(prev)
        return pl.pallas_call(
            kernel,
            out_shape=(block, block),
            in_specs=in_specs,
            out_specs=(in_vmem, in_vmem),
            scratch_shapes=[
                pltpu.VMEM((planes + 2 * HALO - 2, band_rows + 2, row_length), jnp.float32),
                pltpu.VMEM((planes, band_rows + 2, row_length), jnp.float32),
                pltpu.SemaphoreType.DMA((3,)),
            ],
            compiler_params=pltpu.CompilerParams(vmem_limit_bytes=56 * 1024 * 1024),
        )(*operands)

    return run


def z_neighbours(block, width):
    count = lax.axis_size("gz")
    forward = [(i, i + 1) for i in range(count - 1)]
    forward.append((count - 1, 0))
    backward = [(target, source) for source, target in forward]
    low = lax.ppermute(lax.slice_in_dim(block, block.shape[0] - width, None, axis=0), "gz", forward)
    high = lax.ppermute(lax.slice_in_dim(block, 0, width, axis=0), "gz", backward)
    return low, high


def invariants(curve_zz, curve_yy, curve_xx, curve_zy, curve_zx, curve_yx):
    trace_sum = curve_xx + curve_yy + curve_zz
    minor_sum = (
        curve_xx * curve_yy
        + curve_xx * curve_zz
        + curve_yy * curve_zz
        - curve_zy * curve_zy
        - curve_zx * curve_zx
        - curve_yx * curve_yx
    )
    return (trace_sum * trace_sum / 3.0 - minor_sum) * jax.nn.sigmoid(-trace_sum)


def signature(smoothed):
    centre = smoothed[1:-1, 1:-1]
    above_z = smoothed[2:, 1:-1]
    below_z = smoothed[:-2, 1:-1]
    above_y = smoothed[1:-1, 2:]
    below_y = smoothed[1:-1, :-2]
    curve_zz = hessian_scale * (above_z - 2.0 * centre + below_z)
    curve_yy = hessian_scale * (above_y - 2.0 * centre + below_y)
    curve_xx = hessian_scale * (jnp.roll(centre, -1, 2) - 2.0 * centre + jnp.roll(centre, 1, 2))
    curve_zy = (
        hessian_scale
        * 0.25
        * (smoothed[2:, 2:] - smoothed[2:, :-2] - smoothed[:-2, 2:] + smoothed[:-2, :-2])
    )
    curve_zx = (
        hessian_scale
        * 0.25
        * (
            jnp.roll(above_z, -1, 2)
            - jnp.roll(above_z, 1, 2)
            - jnp.roll(below_z, -1, 2)
            + jnp.roll(below_z, 1, 2)
        )
    )
    curve_yx = (
        hessian_scale
        * 0.25
        * (
            jnp.roll(above_y, -1, 2)
            - jnp.roll(above_y, 1, 2)
            - jnp.roll(below_y, -1, 2)
            + jnp.roll(below_y, 1, 2)
        )
    )
    return invariants(curve_zz, curve_yy, curve_xx, curve_zy, curve_zx, curve_yx)


def per_device(density, dilations, owner_rank, owner_slot, base_cell, corner_weights):
    slab_depth = density.shape[0]
    band_rows = density.shape[1]
    row_length = density.shape[2]
    banded = with_halo(density, (("gy", 1),), HALO)
    response = None
    features = []
    for level_index in range(SCALES):
        dilation = dilations[level_index]
        along_y = smooth_padded(banded, dilation, 1, band_rows)
        low, high = z_neighbours(along_y, HALO)
        run = level_kernel(level_index, level_index == 0, slab_depth, band_rows, row_length)
        feature, response = run(dilations, low, along_y, high, response)
        features.append(feature.reshape(slab_depth * band_rows, row_length))
    plane = (band_rows - 1) * row_length
    z_index = base_cell // plane
    remainder = base_cell % plane
    y_index = remainder // row_length
    x_index = remainder % row_length
    entries = base_cell.shape[0]
    steps = jnp.arange(2, dtype=jnp.int32)
    target_x = ((x_index[:, None] + steps[None, :]) % row_length).reshape(-1)
    pick_x = (
        jnp.arange(row_length, dtype=jnp.int32)[:, None] == target_x[None, :]
    ).astype(jnp.float32)
    cells = jnp.arange(slab_depth * band_rows, dtype=jnp.int32)[:, None]
    weight_grid = None
    for step_z in (0, 1):
        for step_y in (0, 1):
            row = jnp.repeat((z_index + step_z) * band_rows + y_index + step_y, 2)
            corner = 4 * step_z + 2 * step_y
            weights = jnp.stack(
                [corner_weights[corner], corner_weights[corner + 1]], axis=1
            ).reshape(-1)
            term = jnp.where(cells == row[None, :], weights[None, :], 0.0)
            weight_grid = term if weight_grid is None else weight_grid + term
    partials = []
    for feature in features:
        picked = jnp.dot(
            feature, pick_x, precision=lax.Precision.HIGHEST, preferred_element_type=jnp.float32
        )
        per_column = jnp.sum(picked * weight_grid, axis=0)
        partials.append(jnp.sum(per_column.reshape(entries, 2), axis=1))
    partial_value = jnp.stack(partials)
    owner_group = owner_rank[:, 0]
    groups = lax.axis_size("gy")
    column = owner_group * HOWN + owner_slot
    onehot = (column[:, None] == jnp.arange(groups * HOWN, dtype=jnp.int32)[None, :]).astype(
        jnp.float32
    )
    spread = jnp.dot(
        partial_value, onehot, precision=lax.Precision.HIGHEST, preferred_element_type=jnp.float32
    )
    exchanged = lax.all_to_all(
        spread.reshape(SCALES, groups, HOWN), "gy", split_axis=1, concat_axis=1, tiled=True
    )
    catalogue = jnp.sum(exchanged, axis=1)
    return (response, catalogue)


def solution(mesh):
    placed = (
        P("gz", "gy", None),
        P(),
        P(("gz", "gy"), None),
        P(("gz", "gy")),
        P(("gz", "gy")),
        P(None, ("gz", "gy")),
    )
    return jax.shard_map(
        per_device,
        mesh=mesh,
        in_specs=placed,
        out_specs=(P("gz", "gy", None), P(None, ("gz", "gy"))),
        check_vma=False,
    )
```

```python
import jax
import jax.numpy as jnp
from jax import lax
from jax.experimental import pallas as pl
from jax.experimental.pallas import tpu as pltpu
from jax.sharding import PartitionSpec as P

SCALES = 3
HALO = 9
HOWN = 256
DMAX = 4


tap_weights = (0.0625, 0.25, 0.375, 0.25, 0.0625)
hessian_scale = 4.0


def with_halo(block, sides, width):
    for axis, dim in sides:
        count = lax.axis_size(axis)
        forward = [(i, i + 1) for i in range(count - 1)]
        forward.append((count - 1, 0))
        backward = [(target, source) for source, target in forward]
        low = lax.ppermute(
            lax.slice_in_dim(block, block.shape[dim] - width, None, axis=dim), axis, forward
        )
        high = lax.ppermute(lax.slice_in_dim(block, 0, width, axis=dim), axis, backward)
        block = jnp.concatenate([low, block, high], axis=dim)
    return block


def smooth_padded(field_data, dilation, along_dim, extent):
    running = None
    for offset in range(5):
        start_at = HALO - 1 + (offset - 2) * dilation
        summand = tap_weights[offset] * lax.dynamic_slice_in_dim(
            field_data, start_at, extent + 2, along_dim
        )
        running = summand if running is None else running + summand
    return running


def smooth_periodic(field_data, dilation):
    running = None
    for offset in range(5):
        summand = tap_weights[offset] * jnp.roll(field_data, -(offset - 2) * dilation, axis=2)
        running = summand if running is None else running + summand
    return running


def level_kernel(level_index, first, slab_depth, band_rows, row_length):
    planes = slab_depth + 2

    def compute(dilation, a_scr, s_scr, feature_ref, prev_ref, best_ref):
        def smooth_plane(plane, carry):
            along_z = None
            for offset in range(5):
                summand = tap_weights[offset] * a_scr[HALO - 1 + plane + (offset - 2) * dilation]
                along_z = summand if along_z is None else along_z + summand
            running = None
            for offset in range(5):
                shift = (-(offset - 2) * dilation) % row_length
                moved = along_z if shift == 0 else pltpu.roll(along_z, shift, 1)
                summand = tap_weights[offset] * moved
                running = summand if running is None else running + summand
            s_scr[plane] = running
            return carry

        lax.fori_loop(0, planes, smooth_plane, 0)

        def feature_plane(z, carry):
            for half in range(band_rows // 8):
                y0 = half * 8

                def at(dz, dy):
                    return s_scr[z + 1 + dz, pl.ds(1 + y0 + dy, 8), :]

                centre = at(0, 0)
                above_z = at(1, 0)
                below_z = at(-1, 0)
                above_y = at(0, 1)
                below_y = at(0, -1)

                def left(v):
                    return pltpu.roll(v, row_length - 1, 1)

                def right(v):
                    return pltpu.roll(v, 1, 1)

                curve_zz = hessian_scale * (above_z - 2.0 * centre + below_z)
                curve_yy = hessian_scale * (above_y - 2.0 * centre + below_y)
                curve_xx = hessian_scale * (left(centre) - 2.0 * centre + right(centre))
                curve_zy = (hessian_scale * 0.25) * (at(1, 1) - at(1, -1) - at(-1, 1) + at(-1, -1))
                curve_zx = (hessian_scale * 0.25) * (
                    left(above_z) - right(above_z) - left(below_z) + right(below_z)
                )
                curve_yx = (hessian_scale * 0.25) * (
                    left(above_y) - right(above_y) - left(below_y) + right(below_y)
                )
                trace_sum = curve_xx + curve_yy + curve_zz
                minor_sum = (
                    curve_xx * curve_yy
                    + curve_xx * curve_zz
                    + curve_yy * curve_zz
                    - curve_zy * curve_zy
                    - curve_zx * curve_zx
                    - curve_yx * curve_yx
                )
                value = (trace_sum * trace_sum / 3.0 - minor_sum) * (1.0 / (1.0 + jnp.exp(trace_sum)))
                feature_ref[z, pl.ds(y0, 8), :] = value
                if first:
                    best_ref[z, pl.ds(y0, 8), :] = value
                else:
                    best_ref[z, pl.ds(y0, 8), :] = jnp.maximum(prev_ref[z, pl.ds(y0, 8), :], value)
            return carry

        lax.fori_loop(0, slab_depth, feature_plane, 0)

    def kernel(*refs):
        if first:
            dil_ref, lo_hbm, mid_hbm, hi_hbm, feature_ref, best_ref, a_scr, s_scr, sems = refs
            prev_ref = None
        else:
            (dil_ref, lo_hbm, mid_hbm, hi_hbm, prev_ref, feature_ref, best_ref,
             a_scr, s_scr, sems) = refs
        copies = [
            pltpu.make_async_copy(lo_hbm, a_scr.at[pl.ds(0, HALO)], sems.at[0]),
            pltpu.make_async_copy(mid_hbm, a_scr.at[pl.ds(HALO, slab_depth)], sems.at[1]),
            pltpu.make_async_copy(hi_hbm, a_scr.at[pl.ds(HALO + slab_depth, HALO)], sems.at[2]),
        ]
        for copy in copies:
            copy.start()
        for copy in copies:
            copy.wait()
        dilation = dil_ref[level_index]
        for value in range(1, DMAX + 1):

            @pl.when(dilation == value)
            def _():
                compute(value, a_scr, s_scr, feature_ref, prev_ref, best_ref)

    def run(dilations, low, middle, high, prev):
        block = jax.ShapeDtypeStruct((slab_depth, band_rows, row_length), jnp.float32)
        anywhere = pl.BlockSpec(memory_space=pl.ANY)
        in_vmem = pl.BlockSpec(memory_space=pltpu.VMEM)
        in_specs = [pl.BlockSpec(memory_space=pltpu.SMEM), anywhere, anywhere, anywhere]
        operands = [dilations, low, middle, high]
        if not first:
            in_specs.append(in_vmem)
            operands.append(prev)
        return pl.pallas_call(
            kernel,
            out_shape=(block, block),
            in_specs=in_specs,
            out_specs=(in_vmem, in_vmem),
            scratch_shapes=[
                pltpu.VMEM((planes + 2 * HALO - 2, band_rows + 2, row_length), jnp.float32),
                pltpu.VMEM((planes, band_rows + 2, row_length), jnp.float32),
                pltpu.SemaphoreType.DMA((3,)),
            ],
            compiler_params=pltpu.CompilerParams(vmem_limit_bytes=56 * 1024 * 1024),
        )(*operands)

    return run


def z_neighbours(block, width):
    count = lax.axis_size("gz")
    forward = [(i, i + 1) for i in range(count - 1)]
    forward.append((count - 1, 0))
    backward = [(target, source) for source, target in forward]
    low = lax.ppermute(lax.slice_in_dim(block, block.shape[0] - width, None, axis=0), "gz", forward)
    high = lax.ppermute(lax.slice_in_dim(block, 0, width, axis=0), "gz", backward)
    return low, high


def invariants(curve_zz, curve_yy, curve_xx, curve_zy, curve_zx, curve_yx):
    trace_sum = curve_xx + curve_yy + curve_zz
    minor_sum = (
        curve_xx * curve_yy
        + curve_xx * curve_zz
        + curve_yy * curve_zz
        - curve_zy * curve_zy
        - curve_zx * curve_zx
        - curve_yx * curve_yx
    )
    return (trace_sum * trace_sum / 3.0 - minor_sum) * jax.nn.sigmoid(-trace_sum)


def signature(smoothed):
    centre = smoothed[1:-1, 1:-1]
    above_z = smoothed[2:, 1:-1]
    below_z = smoothed[:-2, 1:-1]
    above_y = smoothed[1:-1, 2:]
    below_y = smoothed[1:-1, :-2]
    curve_zz = hessian_scale * (above_z - 2.0 * centre + below_z)
    curve_yy = hessian_scale * (above_y - 2.0 * centre + below_y)
    curve_xx = hessian_scale * (jnp.roll(centre, -1, 2) - 2.0 * centre + jnp.roll(centre, 1, 2))
    curve_zy = (
        hessian_scale
        * 0.25
        * (smoothed[2:, 2:] - smoothed[2:, :-2] - smoothed[:-2, 2:] + smoothed[:-2, :-2])
    )
    curve_zx = (
        hessian_scale
        * 0.25
        * (
            jnp.roll(above_z, -1, 2)
            - jnp.roll(above_z, 1, 2)
            - jnp.roll(below_z, -1, 2)
            + jnp.roll(below_z, 1, 2)
        )
    )
    curve_yx = (
        hessian_scale
        * 0.25
        * (
            jnp.roll(above_y, -1, 2)
            - jnp.roll(above_y, 1, 2)
            - jnp.roll(below_y, -1, 2)
            + jnp.roll(below_y, 1, 2)
        )
    )
    return invariants(curve_zz, curve_yy, curve_xx, curve_zy, curve_zx, curve_yx)


def per_device(density, dilations, owner_rank, owner_slot, base_cell, corner_weights):
    slab_depth = density.shape[0]
    band_rows = density.shape[1]
    row_length = density.shape[2]
    banded = with_halo(density, (("gy", 1),), HALO)
    response = None
    features = []
    for level_index in range(SCALES):
        dilation = dilations[level_index]
        along_y = smooth_padded(banded, dilation, 1, band_rows)
        low, high = z_neighbours(along_y, HALO)
        run = level_kernel(level_index, level_index == 0, slab_depth, band_rows, row_length)
        feature, response = run(dilations, low, along_y, high, response)
        features.append(feature.reshape(slab_depth * band_rows, row_length))
    plane = (band_rows - 1) * row_length
    z_index = base_cell // plane
    remainder = base_cell % plane
    y_index = remainder // row_length
    x_index = remainder % row_length
    entries = base_cell.shape[0]
    target_x = jnp.concatenate([x_index, (x_index + 1) % row_length])
    pick_x = (
        jnp.arange(row_length, dtype=jnp.int32)[:, None] == target_x[None, :]
    ).astype(jnp.float32)
    cells = jnp.arange(slab_depth * band_rows, dtype=jnp.int32)[:, None]
    weight_grid = None
    for step_z in (0, 1):
        for step_y in (0, 1):
            row = (z_index + step_z) * band_rows + y_index + step_y
            corner = 4 * step_z + 2 * step_y
            weights = jnp.concatenate([corner_weights[corner], corner_weights[corner + 1]])
            term = jnp.where(cells == jnp.concatenate([row, row])[None, :], weights[None, :], 0.0)
            weight_grid = term if weight_grid is None else weight_grid + term
    partials = []
    for feature in features:
        picked = jnp.dot(
            feature, pick_x, precision=lax.Precision.HIGHEST, preferred_element_type=jnp.float32
        )
        per_column = jnp.sum(picked * weight_grid, axis=0)
        partials.append(per_column[:entries] + per_column[entries:])
    partial_value = jnp.stack(partials)
    owner_group = owner_rank[:, 0]
    groups = lax.axis_size("gy")
    column = owner_group * HOWN + owner_slot
    onehot = (column[:, None] == jnp.arange(groups * HOWN, dtype=jnp.int32)[None, :]).astype(
        jnp.float32
    )
    spread = jnp.dot(
        partial_value, onehot, precision=lax.Precision.HIGHEST, preferred_element_type=jnp.float32
    )
    exchanged = lax.all_to_all(
        spread.reshape(SCALES, groups, HOWN), "gy", split_axis=1, concat_axis=1, tiled=True
    )
    catalogue = jnp.sum(exchanged, axis=1)
    return (response, catalogue)


def solution(mesh):
    placed = (
        P("gz", "gy", None),
        P(),
        P(("gz", "gy"), None),
        P(("gz", "gy")),
        P(("gz", "gy")),
        P(None, ("gz", "gy")),
    )
    return jax.shard_map(
        per_device,
        mesh=mesh,
        in_specs=placed,
        out_specs=(P("gz", "gy", None), P(None, ("gz", "gy"))),
        check_vma=False,
    )
```

```python
import jax
import jax.numpy as jnp
from jax import lax
from jax.experimental import pallas as pl
from jax.experimental.pallas import tpu as pltpu
from jax.sharding import PartitionSpec as P

SCALES = 3
HALO = 9
HOWN = 256
DMAX = 4


tap_weights = (0.0625, 0.25, 0.375, 0.25, 0.0625)
hessian_scale = 4.0


def with_halo(block, sides, width):
    for axis, dim in sides:
        count = lax.axis_size(axis)
        forward = [(i, i + 1) for i in range(count - 1)]
        forward.append((count - 1, 0))
        backward = [(target, source) for source, target in forward]
        low = lax.ppermute(
            lax.slice_in_dim(block, block.shape[dim] - width, None, axis=dim), axis, forward
        )
        high = lax.ppermute(lax.slice_in_dim(block, 0, width, axis=dim), axis, backward)
        block = jnp.concatenate([low, block, high], axis=dim)
    return block


def smooth_padded(field_data, dilation, along_dim, extent):
    running = None
    for offset in range(5):
        start_at = HALO - 1 + (offset - 2) * dilation
        summand = tap_weights[offset] * lax.dynamic_slice_in_dim(
            field_data, start_at, extent + 2, along_dim
        )
        running = summand if running is None else running + summand
    return running


def smooth_periodic(field_data, dilation):
    running = None
    for offset in range(5):
        summand = tap_weights[offset] * jnp.roll(field_data, -(offset - 2) * dilation, axis=2)
        running = summand if running is None else running + summand
    return running


def level_kernel(level_index, first, slab_depth, band_rows, row_length):
    planes = slab_depth + 2

    def compute(dilation, a_scr, s_scr, feature_ref, prev_ref, best_ref):
        def smooth_plane(plane, carry):
            along_z = None
            for offset in range(5):
                summand = tap_weights[offset] * a_scr[HALO - 1 + plane + (offset - 2) * dilation]
                along_z = summand if along_z is None else along_z + summand
            running = None
            for offset in range(5):
                shift = (-(offset - 2) * dilation) % row_length
                moved = along_z if shift == 0 else pltpu.roll(along_z, shift, 1)
                summand = tap_weights[offset] * moved
                running = summand if running is None else running + summand
            s_scr[plane] = running
            return carry

        lax.fori_loop(0, planes, smooth_plane, 0)

        def feature_plane(z, carry):
            for half in range(band_rows // 8):
                y0 = half * 8

                def at(dz, dy):
                    return s_scr[z + 1 + dz, pl.ds(1 + y0 + dy, 8), :]

                centre = at(0, 0)
                above_z = at(1, 0)
                below_z = at(-1, 0)
                above_y = at(0, 1)
                below_y = at(0, -1)

                def left(v):
                    return pltpu.roll(v, row_length - 1, 1)

                def right(v):
                    return pltpu.roll(v, 1, 1)

                curve_zz = hessian_scale * (above_z - 2.0 * centre + below_z)
                curve_yy = hessian_scale * (above_y - 2.0 * centre + below_y)
                curve_xx = hessian_scale * (left(centre) - 2.0 * centre + right(centre))
                curve_zy = (hessian_scale * 0.25) * (at(1, 1) - at(1, -1) - at(-1, 1) + at(-1, -1))
                curve_zx = (hessian_scale * 0.25) * (
                    left(above_z) - right(above_z) - left(below_z) + right(below_z)
                )
                curve_yx = (hessian_scale * 0.25) * (
                    left(above_y) - right(above_y) - left(below_y) + right(below_y)
                )
                trace_sum = curve_xx + curve_yy + curve_zz
                minor_sum = (
                    curve_xx * curve_yy
                    + curve_xx * curve_zz
                    + curve_yy * curve_zz
                    - curve_zy * curve_zy
                    - curve_zx * curve_zx
                    - curve_yx * curve_yx
                )
                value = (trace_sum * trace_sum * (1.0 / 3.0) - minor_sum) / (1.0 + jnp.exp(trace_sum))
                feature_ref[z, pl.ds(y0, 8), :] = value
                if first:
                    best_ref[z, pl.ds(y0, 8), :] = value
                else:
                    best_ref[z, pl.ds(y0, 8), :] = jnp.maximum(prev_ref[z, pl.ds(y0, 8), :], value)
            return carry

        lax.fori_loop(0, slab_depth, feature_plane, 0)

    def kernel(*refs):
        if first:
            dil_ref, lo_hbm, mid_hbm, hi_hbm, feature_ref, best_ref, a_scr, s_scr, sems = refs
            prev_ref = None
        else:
            (dil_ref, lo_hbm, mid_hbm, hi_hbm, prev_ref, feature_ref, best_ref,
             a_scr, s_scr, sems) = refs
        copies = [
            pltpu.make_async_copy(lo_hbm, a_scr.at[pl.ds(0, HALO)], sems.at[0]),
            pltpu.make_async_copy(mid_hbm, a_scr.at[pl.ds(HALO, slab_depth)], sems.at[1]),
            pltpu.make_async_copy(hi_hbm, a_scr.at[pl.ds(HALO + slab_depth, HALO)], sems.at[2]),
        ]
        for copy in copies:
            copy.start()
        for copy in copies:
            copy.wait()
        dilation = dil_ref[level_index]
        for value in range(1, DMAX + 1):

            @pl.when(dilation == value)
            def _():
                compute(value, a_scr, s_scr, feature_ref, prev_ref, best_ref)

    def run(dilations, low, middle, high, prev):
        block = jax.ShapeDtypeStruct((slab_depth, band_rows, row_length), jnp.float32)
        anywhere = pl.BlockSpec(memory_space=pl.ANY)
        in_vmem = pl.BlockSpec(memory_space=pltpu.VMEM)
        in_specs = [pl.BlockSpec(memory_space=pltpu.SMEM), anywhere, anywhere, anywhere]
        operands = [dilations, low, middle, high]
        if not first:
            in_specs.append(in_vmem)
            operands.append(prev)
        return pl.pallas_call(
            kernel,
            out_shape=(block, block),
            in_specs=in_specs,
            out_specs=(in_vmem, in_vmem),
            scratch_shapes=[
                pltpu.VMEM((planes + 2 * HALO - 2, band_rows + 2, row_length), jnp.float32),
                pltpu.VMEM((planes, band_rows + 2, row_length), jnp.float32),
                pltpu.SemaphoreType.DMA((3,)),
            ],
            compiler_params=pltpu.CompilerParams(vmem_limit_bytes=56 * 1024 * 1024),
        )(*operands)

    return run


def z_neighbours(block, width):
    count = lax.axis_size("gz")
    forward = [(i, i + 1) for i in range(count - 1)]
    forward.append((count - 1, 0))
    backward = [(target, source) for source, target in forward]
    low = lax.ppermute(lax.slice_in_dim(block, block.shape[0] - width, None, axis=0), "gz", forward)
    high = lax.ppermute(lax.slice_in_dim(block, 0, width, axis=0), "gz", backward)
    return low, high


def invariants(curve_zz, curve_yy, curve_xx, curve_zy, curve_zx, curve_yx):
    trace_sum = curve_xx + curve_yy + curve_zz
    minor_sum = (
        curve_xx * curve_yy
        + curve_xx * curve_zz
        + curve_yy * curve_zz
        - curve_zy * curve_zy
        - curve_zx * curve_zx
        - curve_yx * curve_yx
    )
    return (trace_sum * trace_sum / 3.0 - minor_sum) * jax.nn.sigmoid(-trace_sum)


def signature(smoothed):
    centre = smoothed[1:-1, 1:-1]
    above_z = smoothed[2:, 1:-1]
    below_z = smoothed[:-2, 1:-1]
    above_y = smoothed[1:-1, 2:]
    below_y = smoothed[1:-1, :-2]
    curve_zz = hessian_scale * (above_z - 2.0 * centre + below_z)
    curve_yy = hessian_scale * (above_y - 2.0 * centre + below_y)
    curve_xx = hessian_scale * (jnp.roll(centre, -1, 2) - 2.0 * centre + jnp.roll(centre, 1, 2))
    curve_zy = (
        hessian_scale
        * 0.25
        * (smoothed[2:, 2:] - smoothed[2:, :-2] - smoothed[:-2, 2:] + smoothed[:-2, :-2])
    )
    curve_zx = (
        hessian_scale
        * 0.25
        * (
            jnp.roll(above_z, -1, 2)
            - jnp.roll(above_z, 1, 2)
            - jnp.roll(below_z, -1, 2)
            + jnp.roll(below_z, 1, 2)
        )
    )
    curve_yx = (
        hessian_scale
        * 0.25
        * (
            jnp.roll(above_y, -1, 2)
            - jnp.roll(above_y, 1, 2)
            - jnp.roll(below_y, -1, 2)
            + jnp.roll(below_y, 1, 2)
        )
    )
    return invariants(curve_zz, curve_yy, curve_xx, curve_zy, curve_zx, curve_yx)


def per_device(density, dilations, owner_rank, owner_slot, base_cell, corner_weights):
    slab_depth = density.shape[0]
    band_rows = density.shape[1]
    row_length = density.shape[2]
    banded = with_halo(density, (("gy", 1),), HALO)
    response = None
    features = []
    for level_index in range(SCALES):
        dilation = dilations[level_index]
        along_y = smooth_padded(banded, dilation, 1, band_rows)
        low, high = z_neighbours(along_y, HALO)
        run = level_kernel(level_index, level_index == 0, slab_depth, band_rows, row_length)
        feature, response = run(dilations, low, along_y, high, response)
        features.append(feature.reshape(slab_depth * band_rows, row_length))
    plane = (band_rows - 1) * row_length
    z_index = base_cell // plane
    remainder = base_cell % plane
    y_index = remainder // row_length
    x_index = remainder % row_length
    entries = base_cell.shape[0]
    target_x = jnp.concatenate([x_index, (x_index + 1) % row_length])
    pick_x = (
        jnp.arange(row_length, dtype=jnp.int32)[:, None] == target_x[None, :]
    ).astype(jnp.float32)
    cells = jnp.arange(slab_depth * band_rows, dtype=jnp.int32)[:, None]
    weight_grid = None
    for step_z in (0, 1):
        for step_y in (0, 1):
            row = (z_index + step_z) * band_rows + y_index + step_y
            corner = 4 * step_z + 2 * step_y
            weights = jnp.concatenate([corner_weights[corner], corner_weights[corner + 1]])
            term = jnp.where(cells == jnp.concatenate([row, row])[None, :], weights[None, :], 0.0)
            weight_grid = term if weight_grid is None else weight_grid + term
    partials = []
    for feature in features:
        picked = jnp.dot(
            feature, pick_x, precision=lax.Precision.HIGHEST, preferred_element_type=jnp.float32
        )
        per_column = jnp.sum(picked * weight_grid, axis=0)
        partials.append(per_column[:entries] + per_column[entries:])
    partial_value = jnp.stack(partials)
    groups = lax.axis_size("gy")
    me = lax.axis_index("gy")
    column = ((owner_rank[:, 0] - me) % groups) * HOWN + owner_slot
    onehot = (column[:, None] == jnp.arange(groups * HOWN, dtype=jnp.int32)[None, :]).astype(
        jnp.float32
    )
    spread = jnp.dot(
        partial_value, onehot, precision=lax.Precision.HIGHEST, preferred_element_type=jnp.float32
    )
    catalogue = spread[:, :HOWN]
    for shift in range(1, groups):
        chunk = spread[:, shift * HOWN:(shift + 1) * HOWN]
        pairs = [(i, (i + shift) % groups) for i in range(groups)]
        catalogue = catalogue + lax.ppermute(chunk, "gy", pairs)
    return (response, catalogue)


def solution(mesh):
    placed = (
        P("gz", "gy", None),
        P(),
        P(("gz", "gy"), None),
        P(("gz", "gy")),
        P(("gz", "gy")),
        P(None, ("gz", "gy")),
    )
    return jax.shard_map(
        per_device,
        mesh=mesh,
        in_specs=placed,
        out_specs=(P("gz", "gy", None), P(None, ("gz", "gy"))),
        check_vma=False,
    )
```

```python
import jax
import jax.numpy as jnp
from jax import lax
from jax.experimental import pallas as pl
from jax.experimental.pallas import tpu as pltpu
from jax.sharding import PartitionSpec as P

SCALES = 3
HALO = 9
HOWN = 256
DMAX = 4


tap_weights = (0.0625, 0.25, 0.375, 0.25, 0.0625)
hessian_scale = 4.0


def with_halo(block, sides, width):
    for axis, dim in sides:
        count = lax.axis_size(axis)
        forward = [(i, i + 1) for i in range(count - 1)]
        forward.append((count - 1, 0))
        backward = [(target, source) for source, target in forward]
        low = lax.ppermute(
            lax.slice_in_dim(block, block.shape[dim] - width, None, axis=dim), axis, forward
        )
        high = lax.ppermute(lax.slice_in_dim(block, 0, width, axis=dim), axis, backward)
        block = jnp.concatenate([low, block, high], axis=dim)
    return block


def smooth_padded(field_data, dilation, along_dim, extent):
    running = None
    for offset in range(5):
        start_at = HALO - 1 + (offset - 2) * dilation
        summand = tap_weights[offset] * lax.dynamic_slice_in_dim(
            field_data, start_at, extent + 2, along_dim
        )
        running = summand if running is None else running + summand
    return running


def smooth_periodic(field_data, dilation):
    running = None
    for offset in range(5):
        summand = tap_weights[offset] * jnp.roll(field_data, -(offset - 2) * dilation, axis=2)
        running = summand if running is None else running + summand
    return running


def level_kernel(level_index, first, slab_depth, band_rows, row_length):
    planes = slab_depth + 2

    def compute(dilation, a_scr, s_scr, feature_ref, prev_ref, best_ref):
        def smooth_plane(plane, carry):
            along_z = None
            for offset in range(5):
                summand = tap_weights[offset] * a_scr[HALO - 1 + plane + (offset - 2) * dilation]
                along_z = summand if along_z is None else along_z + summand
            running = None
            for offset in range(5):
                shift = (-(offset - 2) * dilation) % row_length
                moved = along_z if shift == 0 else pltpu.roll(along_z, shift, 1)
                summand = tap_weights[offset] * moved
                running = summand if running is None else running + summand
            s_scr[plane] = running
            return carry

        lax.fori_loop(0, planes, smooth_plane, 0)

        def feature_plane(z, carry):
            for half in range(band_rows // 8):
                y0 = half * 8

                def at(dz, dy):
                    return s_scr[z + 1 + dz, pl.ds(1 + y0 + dy, 8), :]

                centre = at(0, 0)
                above_z = at(1, 0)
                below_z = at(-1, 0)
                above_y = at(0, 1)
                below_y = at(0, -1)

                def left(v):
                    return pltpu.roll(v, row_length - 1, 1)

                def right(v):
                    return pltpu.roll(v, 1, 1)

                curve_zz = hessian_scale * (above_z - 2.0 * centre + below_z)
                curve_yy = hessian_scale * (above_y - 2.0 * centre + below_y)
                curve_xx = hessian_scale * (left(centre) - 2.0 * centre + right(centre))
                curve_zy = (hessian_scale * 0.25) * (at(1, 1) - at(1, -1) - at(-1, 1) + at(-1, -1))
                across_z = above_z - below_z
                across_y = above_y - below_y
                curve_zx = (hessian_scale * 0.25) * (left(across_z) - right(across_z))
                curve_yx = (hessian_scale * 0.25) * (left(across_y) - right(across_y))
                trace_sum = curve_xx + curve_yy + curve_zz
                minor_sum = (
                    curve_xx * curve_yy
                    + curve_xx * curve_zz
                    + curve_yy * curve_zz
                    - curve_zy * curve_zy
                    - curve_zx * curve_zx
                    - curve_yx * curve_yx
                )
                value = (trace_sum * trace_sum / 3.0 - minor_sum) * (1.0 / (1.0 + jnp.exp(trace_sum)))
                feature_ref[z, pl.ds(y0, 8), :] = value
                if first:
                    best_ref[z, pl.ds(y0, 8), :] = value
                else:
                    best_ref[z, pl.ds(y0, 8), :] = jnp.maximum(prev_ref[z, pl.ds(y0, 8), :], value)
            return carry

        lax.fori_loop(0, slab_depth, feature_plane, 0)

    def kernel(*refs):
        if first:
            dil_ref, lo_hbm, mid_hbm, hi_hbm, feature_ref, best_ref, a_scr, s_scr, sems = refs
            prev_ref = None
        else:
            (dil_ref, lo_hbm, mid_hbm, hi_hbm, prev_ref, feature_ref, best_ref,
             a_scr, s_scr, sems) = refs
        copies = [
            pltpu.make_async_copy(lo_hbm, a_scr.at[pl.ds(0, HALO)], sems.at[0]),
            pltpu.make_async_copy(mid_hbm, a_scr.at[pl.ds(HALO, slab_depth)], sems.at[1]),
            pltpu.make_async_copy(hi_hbm, a_scr.at[pl.ds(HALO + slab_depth, HALO)], sems.at[2]),
        ]
        for copy in copies:
            copy.start()
        for copy in copies:
            copy.wait()
        dilation = dil_ref[level_index]
        for value in range(1, DMAX + 1):

            @pl.when(dilation == value)
            def _():
                compute(value, a_scr, s_scr, feature_ref, prev_ref, best_ref)

    def run(dilations, low, middle, high, prev):
        block = jax.ShapeDtypeStruct((slab_depth, band_rows, row_length), jnp.float32)
        anywhere = pl.BlockSpec(memory_space=pl.ANY)
        in_vmem = pl.BlockSpec(memory_space=pltpu.VMEM)
        in_specs = [pl.BlockSpec(memory_space=pltpu.SMEM), anywhere, anywhere, anywhere]
        operands = [dilations, low, middle, high]
        if not first:
            in_specs.append(in_vmem)
            operands.append(prev)
        return pl.pallas_call(
            kernel,
            out_shape=(block, block),
            in_specs=in_specs,
            out_specs=(in_vmem, in_vmem),
            scratch_shapes=[
                pltpu.VMEM((planes + 2 * HALO - 2, band_rows + 2, row_length), jnp.float32),
                pltpu.VMEM((planes, band_rows + 2, row_length), jnp.float32),
                pltpu.SemaphoreType.DMA((3,)),
            ],
            compiler_params=pltpu.CompilerParams(vmem_limit_bytes=56 * 1024 * 1024),
        )(*operands)

    return run


def z_neighbours(block, width):
    count = lax.axis_size("gz")
    forward = [(i, i + 1) for i in range(count - 1)]
    forward.append((count - 1, 0))
    backward = [(target, source) for source, target in forward]
    low = lax.ppermute(lax.slice_in_dim(block, block.shape[0] - width, None, axis=0), "gz", forward)
    high = lax.ppermute(lax.slice_in_dim(block, 0, width, axis=0), "gz", backward)
    return low, high


def invariants(curve_zz, curve_yy, curve_xx, curve_zy, curve_zx, curve_yx):
    trace_sum = curve_xx + curve_yy + curve_zz
    minor_sum = (
        curve_xx * curve_yy
        + curve_xx * curve_zz
        + curve_yy * curve_zz
        - curve_zy * curve_zy
        - curve_zx * curve_zx
        - curve_yx * curve_yx
    )
    return (trace_sum * trace_sum / 3.0 - minor_sum) * jax.nn.sigmoid(-trace_sum)


def signature(smoothed):
    centre = smoothed[1:-1, 1:-1]
    above_z = smoothed[2:, 1:-1]
    below_z = smoothed[:-2, 1:-1]
    above_y = smoothed[1:-1, 2:]
    below_y = smoothed[1:-1, :-2]
    curve_zz = hessian_scale * (above_z - 2.0 * centre + below_z)
    curve_yy = hessian_scale * (above_y - 2.0 * centre + below_y)
    curve_xx = hessian_scale * (jnp.roll(centre, -1, 2) - 2.0 * centre + jnp.roll(centre, 1, 2))
    curve_zy = (
        hessian_scale
        * 0.25
        * (smoothed[2:, 2:] - smoothed[2:, :-2] - smoothed[:-2, 2:] + smoothed[:-2, :-2])
    )
    curve_zx = (
        hessian_scale
        * 0.25
        * (
            jnp.roll(above_z, -1, 2)
            - jnp.roll(above_z, 1, 2)
            - jnp.roll(below_z, -1, 2)
            + jnp.roll(below_z, 1, 2)
        )
    )
    curve_yx = (
        hessian_scale
        * 0.25
        * (
            jnp.roll(above_y, -1, 2)
            - jnp.roll(above_y, 1, 2)
            - jnp.roll(below_y, -1, 2)
            + jnp.roll(below_y, 1, 2)
        )
    )
    return invariants(curve_zz, curve_yy, curve_xx, curve_zy, curve_zx, curve_yx)


def per_device(density, dilations, owner_rank, owner_slot, base_cell, corner_weights):
    slab_depth = density.shape[0]
    band_rows = density.shape[1]
    row_length = density.shape[2]
    banded = with_halo(density, (("gy", 1),), HALO)
    response = None
    features = []
    pending = None

    def finish(pending, response):
        level_index, low, along_y, high = pending
        run = level_kernel(level_index, level_index == 0, slab_depth, band_rows, row_length)
        feature, response = run(dilations, low, along_y, high, response)
        features.append(feature.reshape(slab_depth * band_rows, row_length))
        return response

    for level_index in range(SCALES):
        along_y = smooth_padded(banded, dilations[level_index], 1, band_rows)
        if pending is not None:
            held = (along_y, pending[1], pending[3])
            if response is not None:
                held = held + (response,)
            held = lax.optimization_barrier(held)
            along_y, pending[1], pending[3] = held[:3]
            if response is not None:
                response = held[3]
        low, high = z_neighbours(along_y, HALO)
        if pending is not None:
            response = finish(pending, response)
        pending = [level_index, low, along_y, high]
    response = finish(pending, response)
    plane = (band_rows - 1) * row_length
    z_index = base_cell // plane
    remainder = base_cell % plane
    y_index = remainder // row_length
    x_index = remainder % row_length
    entries = base_cell.shape[0]
    target_x = jnp.concatenate([x_index, (x_index + 1) % row_length])
    pick_x = (
        jnp.arange(row_length, dtype=jnp.int32)[:, None] == target_x[None, :]
    ).astype(jnp.float32)
    cells = jnp.arange(slab_depth * band_rows, dtype=jnp.int32)[:, None]
    weight_grid = None
    for step_z in (0, 1):
        for step_y in (0, 1):
            row = (z_index + step_z) * band_rows + y_index + step_y
            corner = 4 * step_z + 2 * step_y
            weights = jnp.concatenate([corner_weights[corner], corner_weights[corner + 1]])
            term = jnp.where(cells == jnp.concatenate([row, row])[None, :], weights[None, :], 0.0)
            weight_grid = term if weight_grid is None else weight_grid + term
    partials = []
    for feature in features:
        picked = jnp.dot(
            feature, pick_x, precision=lax.Precision.HIGHEST, preferred_element_type=jnp.float32
        )
        per_column = jnp.sum(picked * weight_grid, axis=0)
        partials.append(per_column[:entries] + per_column[entries:])
    partial_value = jnp.stack(partials)
    owner_group = owner_rank[:, 0]
    groups = lax.axis_size("gy")
    column = owner_group * HOWN + owner_slot
    onehot = (column[:, None] == jnp.arange(groups * HOWN, dtype=jnp.int32)[None, :]).astype(
        jnp.float32
    )
    spread = jnp.dot(
        partial_value, onehot, precision=lax.Precision.HIGHEST, preferred_element_type=jnp.float32
    )
    exchanged = lax.all_to_all(
        spread.reshape(SCALES, groups, HOWN), "gy", split_axis=1, concat_axis=1, tiled=True
    )
    catalogue = jnp.sum(exchanged, axis=1)
    return (response, catalogue)


def solution(mesh):
    placed = (
        P("gz", "gy", None),
        P(),
        P(("gz", "gy"), None),
        P(("gz", "gy")),
        P(("gz", "gy")),
        P(None, ("gz", "gy")),
    )
    return jax.shard_map(
        per_device,
        mesh=mesh,
        in_specs=placed,
        out_specs=(P("gz", "gy", None), P(None, ("gz", "gy"))),
        check_vma=False,
    )
```

```python
import jax
import jax.numpy as jnp
from jax import lax
from jax.experimental import pallas as pl
from jax.experimental.pallas import tpu as pltpu
from jax.sharding import PartitionSpec as P

SCALES = 3
HALO = 9
HOWN = 256
DMAX = 4


tap_weights = (0.0625, 0.25, 0.375, 0.25, 0.0625)
hessian_scale = 4.0


def split_ppermute(part, axis, pairs, pieces):
    size = part.shape[0]
    bounds = [size * i // pieces for i in range(pieces + 1)]
    moved = [
        lax.ppermute(lax.slice_in_dim(part, bounds[i], bounds[i + 1], axis=0), axis, pairs)
        for i in range(pieces)
    ]
    return jnp.concatenate(moved, axis=0)


def with_halo(block, sides, width):
    for axis, dim in sides:
        count = lax.axis_size(axis)
        forward = [(i, i + 1) for i in range(count - 1)]
        forward.append((count - 1, 0))
        backward = [(target, source) for source, target in forward]
        low = split_ppermute(
            lax.slice_in_dim(block, block.shape[dim] - width, None, axis=dim), axis, forward, 5
        )
        high = split_ppermute(lax.slice_in_dim(block, 0, width, axis=dim), axis, backward, 5)
        block = jnp.concatenate([low, block, high], axis=dim)
    return block


def smooth_padded(field_data, dilation, along_dim, extent):
    running = None
    for offset in range(5):
        start_at = HALO - 1 + (offset - 2) * dilation
        summand = tap_weights[offset] * lax.dynamic_slice_in_dim(
            field_data, start_at, extent + 2, along_dim
        )
        running = summand if running is None else running + summand
    return running


def smooth_periodic(field_data, dilation):
    running = None
    for offset in range(5):
        summand = tap_weights[offset] * jnp.roll(field_data, -(offset - 2) * dilation, axis=2)
        running = summand if running is None else running + summand
    return running


def level_kernel(level_index, first, slab_depth, band_rows, row_length):
    planes = slab_depth + 2

    def compute(dilation, a_scr, s_scr, feature_ref, prev_ref, best_ref):
        def smooth_plane(plane, carry):
            along_z = None
            for offset in range(5):
                summand = tap_weights[offset] * a_scr[HALO - 1 + plane + (offset - 2) * dilation]
                along_z = summand if along_z is None else along_z + summand
            running = None
            for offset in range(5):
                shift = (-(offset - 2) * dilation) % row_length
                moved = along_z if shift == 0 else pltpu.roll(along_z, shift, 1)
                summand = tap_weights[offset] * moved
                running = summand if running is None else running + summand
            s_scr[plane] = running
            return carry

        lax.fori_loop(0, planes, smooth_plane, 0)

        def feature_plane(z, carry):
            for half in range(band_rows // 8):
                y0 = half * 8

                def at(dz, dy):
                    return s_scr[z + 1 + dz, pl.ds(1 + y0 + dy, 8), :]

                centre = at(0, 0)
                above_z = at(1, 0)
                below_z = at(-1, 0)
                above_y = at(0, 1)
                below_y = at(0, -1)

                def left(v):
                    return pltpu.roll(v, row_length - 1, 1)

                def right(v):
                    return pltpu.roll(v, 1, 1)

                curve_zz = hessian_scale * (above_z - 2.0 * centre + below_z)
                curve_yy = hessian_scale * (above_y - 2.0 * centre + below_y)
                curve_xx = hessian_scale * (left(centre) - 2.0 * centre + right(centre))
                curve_zy = (hessian_scale * 0.25) * (at(1, 1) - at(1, -1) - at(-1, 1) + at(-1, -1))
                curve_zx = (hessian_scale * 0.25) * (
                    left(above_z) - right(above_z) - left(below_z) + right(below_z)
                )
                curve_yx = (hessian_scale * 0.25) * (
                    left(above_y) - right(above_y) - left(below_y) + right(below_y)
                )
                trace_sum = curve_xx + curve_yy + curve_zz
                minor_sum = (
                    curve_xx * curve_yy
                    + curve_xx * curve_zz
                    + curve_yy * curve_zz
                    - curve_zy * curve_zy
                    - curve_zx * curve_zx
                    - curve_yx * curve_yx
                )
                value = (trace_sum * trace_sum / 3.0 - minor_sum) * (1.0 / (1.0 + jnp.exp(trace_sum)))
                feature_ref[z, pl.ds(y0, 8), :] = value
                if first:
                    best_ref[z, pl.ds(y0, 8), :] = value
                else:
                    best_ref[z, pl.ds(y0, 8), :] = jnp.maximum(prev_ref[z, pl.ds(y0, 8), :], value)
            return carry

        lax.fori_loop(0, slab_depth, feature_plane, 0)

    def kernel(*refs):
        if first:
            dil_ref, lo_hbm, mid_hbm, hi_hbm, feature_ref, best_ref, a_scr, s_scr, sems = refs
            prev_ref = None
        else:
            (dil_ref, lo_hbm, mid_hbm, hi_hbm, prev_ref, feature_ref, best_ref,
             a_scr, s_scr, sems) = refs
        copies = [
            pltpu.make_async_copy(lo_hbm, a_scr.at[pl.ds(0, HALO)], sems.at[0]),
            pltpu.make_async_copy(mid_hbm, a_scr.at[pl.ds(HALO, slab_depth)], sems.at[1]),
            pltpu.make_async_copy(hi_hbm, a_scr.at[pl.ds(HALO + slab_depth, HALO)], sems.at[2]),
        ]
        for copy in copies:
            copy.start()
        for copy in copies:
            copy.wait()
        dilation = dil_ref[level_index]
        for value in range(1, DMAX + 1):

            @pl.when(dilation == value)
            def _():
                compute(value, a_scr, s_scr, feature_ref, prev_ref, best_ref)

    def run(dilations, low, middle, high, prev):
        block = jax.ShapeDtypeStruct((slab_depth, band_rows, row_length), jnp.float32)
        anywhere = pl.BlockSpec(memory_space=pl.ANY)
        in_vmem = pl.BlockSpec(memory_space=pltpu.VMEM)
        in_specs = [pl.BlockSpec(memory_space=pltpu.SMEM), anywhere, anywhere, anywhere]
        operands = [dilations, low, middle, high]
        if not first:
            in_specs.append(in_vmem)
            operands.append(prev)
        return pl.pallas_call(
            kernel,
            out_shape=(block, block),
            in_specs=in_specs,
            out_specs=(in_vmem, in_vmem),
            scratch_shapes=[
                pltpu.VMEM((planes + 2 * HALO - 2, band_rows + 2, row_length), jnp.float32),
                pltpu.VMEM((planes, band_rows + 2, row_length), jnp.float32),
                pltpu.SemaphoreType.DMA((3,)),
            ],
            compiler_params=pltpu.CompilerParams(vmem_limit_bytes=56 * 1024 * 1024),
        )(*operands)

    return run


def z_neighbours(block, width):
    count = lax.axis_size("gz")
    forward = [(i, i + 1) for i in range(count - 1)]
    forward.append((count - 1, 0))
    backward = [(target, source) for source, target in forward]
    low = lax.ppermute(lax.slice_in_dim(block, block.shape[0] - width, None, axis=0), "gz", forward)
    high = lax.ppermute(lax.slice_in_dim(block, 0, width, axis=0), "gz", backward)
    return low, high


def invariants(curve_zz, curve_yy, curve_xx, curve_zy, curve_zx, curve_yx):
    trace_sum = curve_xx + curve_yy + curve_zz
    minor_sum = (
        curve_xx * curve_yy
        + curve_xx * curve_zz
        + curve_yy * curve_zz
        - curve_zy * curve_zy
        - curve_zx * curve_zx
        - curve_yx * curve_yx
    )
    return (trace_sum * trace_sum / 3.0 - minor_sum) * jax.nn.sigmoid(-trace_sum)


def signature(smoothed):
    centre = smoothed[1:-1, 1:-1]
    above_z = smoothed[2:, 1:-1]
    below_z = smoothed[:-2, 1:-1]
    above_y = smoothed[1:-1, 2:]
    below_y = smoothed[1:-1, :-2]
    curve_zz = hessian_scale * (above_z - 2.0 * centre + below_z)
    curve_yy = hessian_scale * (above_y - 2.0 * centre + below_y)
    curve_xx = hessian_scale * (jnp.roll(centre, -1, 2) - 2.0 * centre + jnp.roll(centre, 1, 2))
    curve_zy = (
        hessian_scale
        * 0.25
        * (smoothed[2:, 2:] - smoothed[2:, :-2] - smoothed[:-2, 2:] + smoothed[:-2, :-2])
    )
    curve_zx = (
        hessian_scale
        * 0.25
        * (
            jnp.roll(above_z, -1, 2)
            - jnp.roll(above_z, 1, 2)
            - jnp.roll(below_z, -1, 2)
            + jnp.roll(below_z, 1, 2)
        )
    )
    curve_yx = (
        hessian_scale
        * 0.25
        * (
            jnp.roll(above_y, -1, 2)
            - jnp.roll(above_y, 1, 2)
            - jnp.roll(below_y, -1, 2)
            + jnp.roll(below_y, 1, 2)
        )
    )
    return invariants(curve_zz, curve_yy, curve_xx, curve_zy, curve_zx, curve_yx)


def per_device(density, dilations, owner_rank, owner_slot, base_cell, corner_weights):
    slab_depth = density.shape[0]
    band_rows = density.shape[1]
    row_length = density.shape[2]
    banded = with_halo(density, (("gy", 1),), HALO)
    response = None
    features = []
    for level_index in range(SCALES):
        dilation = dilations[level_index]
        along_y = smooth_padded(banded, dilation, 1, band_rows)
        low, high = z_neighbours(along_y, HALO)
        run = level_kernel(level_index, level_index == 0, slab_depth, band_rows, row_length)
        feature, response = run(dilations, low, along_y, high, response)
        features.append(feature.reshape(slab_depth * band_rows, row_length))
    plane = (band_rows - 1) * row_length
    z_index = base_cell // plane
    remainder = base_cell % plane
    y_index = remainder // row_length
    x_index = remainder % row_length
    entries = base_cell.shape[0]
    target_x = jnp.concatenate([x_index, (x_index + 1) % row_length])
    pick_x = (
        jnp.arange(row_length, dtype=jnp.int32)[:, None] == target_x[None, :]
    ).astype(jnp.float32)
    cells = jnp.arange(slab_depth * band_rows, dtype=jnp.int32)[:, None]
    weight_grid = None
    for step_z in (0, 1):
        for step_y in (0, 1):
            row = (z_index + step_z) * band_rows + y_index + step_y
            corner = 4 * step_z + 2 * step_y
            weights = jnp.concatenate([corner_weights[corner], corner_weights[corner + 1]])
            term = jnp.where(cells == jnp.concatenate([row, row])[None, :], weights[None, :], 0.0)
            weight_grid = term if weight_grid is None else weight_grid + term
    partials = []
    for feature in features:
        picked = jnp.dot(
            feature, pick_x, precision=lax.Precision.HIGHEST, preferred_element_type=jnp.float32
        )
        per_column = jnp.sum(picked * weight_grid, axis=0)
        partials.append(per_column[:entries] + per_column[entries:])
    partial_value = jnp.stack(partials)
    owner_group = owner_rank[:, 0]
    groups = lax.axis_size("gy")
    column = owner_group * HOWN + owner_slot
    onehot = (column[:, None] == jnp.arange(groups * HOWN, dtype=jnp.int32)[None, :]).astype(
        jnp.float32
    )
    spread = jnp.dot(
        partial_value, onehot, precision=lax.Precision.HIGHEST, preferred_element_type=jnp.float32
    )
    exchanged = lax.all_to_all(
        spread.reshape(SCALES, groups, HOWN), "gy", split_axis=1, concat_axis=1, tiled=True
    )
    catalogue = jnp.sum(exchanged, axis=1)
    return (response, catalogue)


def solution(mesh):
    placed = (
        P("gz", "gy", None),
        P(),
        P(("gz", "gy"), None),
        P(("gz", "gy")),
        P(("gz", "gy")),
        P(None, ("gz", "gy")),
    )
    return jax.shard_map(
        per_device,
        mesh=mesh,
        in_specs=placed,
        out_specs=(P("gz", "gy", None), P(None, ("gz", "gy"))),
        check_vma=False,
    )
```

```python
import jax
import jax.numpy as jnp
from jax import lax
from jax.experimental import pallas as pl
from jax.experimental.pallas import tpu as pltpu
from jax.sharding import PartitionSpec as P

SCALES = 3
HALO = 9
HOWN = 256
DMAX = 4


tap_weights = (0.0625, 0.25, 0.375, 0.25, 0.0625)
hessian_scale = 4.0


def with_halo(block, sides, width):
    for axis, dim in sides:
        count = lax.axis_size(axis)
        forward = [(i, i + 1) for i in range(count - 1)]
        forward.append((count - 1, 0))
        backward = [(target, source) for source, target in forward]
        low = lax.ppermute(
            lax.slice_in_dim(block, block.shape[dim] - width, None, axis=dim), axis, forward
        )
        high = lax.ppermute(lax.slice_in_dim(block, 0, width, axis=dim), axis, backward)
        block = jnp.concatenate([low, block, high], axis=dim)
    return block


def smooth_padded(field_data, dilation, along_dim, extent):
    running = None
    for offset in range(5):
        start_at = HALO - 1 + (offset - 2) * dilation
        summand = tap_weights[offset] * lax.dynamic_slice_in_dim(
            field_data, start_at, extent + 2, along_dim
        )
        running = summand if running is None else running + summand
    return running


def smooth_periodic(field_data, dilation):
    running = None
    for offset in range(5):
        summand = tap_weights[offset] * jnp.roll(field_data, -(offset - 2) * dilation, axis=2)
        running = summand if running is None else running + summand
    return running


def level_kernel(level_index, first, slab_depth, band_rows, row_length):
    planes = slab_depth + 2

    def compute(dilation, a_scr, s_scr, feature_ref, prev_ref, best_ref):
        def smooth_plane(plane, carry):
            for first_row in range(0, band_rows + 2, 8):
                rows = min(8, band_rows + 2 - first_row)
                along_z = None
                for offset in range(5):
                    source = HALO - 1 + plane + (offset - 2) * dilation
                    summand = tap_weights[offset] * a_scr[source, pl.ds(first_row, rows), :]
                    along_z = summand if along_z is None else along_z + summand
                running = None
                for offset in range(5):
                    shift = (-(offset - 2) * dilation) % row_length
                    moved = along_z if shift == 0 else pltpu.roll(along_z, shift, 1)
                    summand = tap_weights[offset] * moved
                    running = summand if running is None else running + summand
                s_scr[plane, pl.ds(first_row, rows), :] = running
            return carry

        lax.fori_loop(0, planes, smooth_plane, 0)

        def feature_plane(z, carry):
            for half in range(band_rows // 8):
                y0 = half * 8

                def at(dz, dy):
                    return s_scr[z + 1 + dz, pl.ds(1 + y0 + dy, 8), :]

                def left(v):
                    return pltpu.roll(v, row_length - 1, 1)

                def right(v):
                    return pltpu.roll(v, 1, 1)

                centre = at(0, 0)
                above_z = at(1, 0)
                below_z = at(-1, 0)
                curve_zz = hessian_scale * (above_z - 2.0 * centre + below_z)
                across_z = above_z - below_z
                curve_zx = (hessian_scale * 0.25) * (left(across_z) - right(across_z))
                above_y = at(0, 1)
                below_y = at(0, -1)
                curve_yy = hessian_scale * (above_y - 2.0 * centre + below_y)
                across_y = above_y - below_y
                curve_yx = (hessian_scale * 0.25) * (left(across_y) - right(across_y))
                curve_xx = hessian_scale * (left(centre) - 2.0 * centre + right(centre))
                trace_sum = curve_xx + curve_yy + curve_zz
                minor_sum = curve_xx * curve_yy + curve_xx * curve_zz + curve_yy * curve_zz
                minor_sum = minor_sum - curve_zx * curve_zx - curve_yx * curve_yx
                curve_zy = (hessian_scale * 0.25) * (at(1, 1) - at(1, -1) - at(-1, 1) + at(-1, -1))
                minor_sum = minor_sum - curve_zy * curve_zy
                value = (trace_sum * trace_sum / 3.0 - minor_sum) * (1.0 / (1.0 + jnp.exp(trace_sum)))
                feature_ref[z, pl.ds(y0, 8), :] = value
                if first:
                    best_ref[z, pl.ds(y0, 8), :] = value
                else:
                    best_ref[z, pl.ds(y0, 8), :] = jnp.maximum(prev_ref[z, pl.ds(y0, 8), :], value)
            return carry

        lax.fori_loop(0, slab_depth, feature_plane, 0)

    def kernel(*refs):
        if first:
            dil_ref, lo_hbm, mid_hbm, hi_hbm, feature_ref, best_ref, a_scr, s_scr, sems = refs
            prev_ref = None
        else:
            (dil_ref, lo_hbm, mid_hbm, hi_hbm, prev_ref, feature_ref, best_ref,
             a_scr, s_scr, sems) = refs
        copies = [
            pltpu.make_async_copy(lo_hbm, a_scr.at[pl.ds(0, HALO)], sems.at[0]),
            pltpu.make_async_copy(mid_hbm, a_scr.at[pl.ds(HALO, slab_depth)], sems.at[1]),
            pltpu.make_async_copy(hi_hbm, a_scr.at[pl.ds(HALO + slab_depth, HALO)], sems.at[2]),
        ]
        for copy in copies:
            copy.start()
        for copy in copies:
            copy.wait()
        dilation = dil_ref[level_index]
        for value in range(1, DMAX + 1):

            @pl.when(dilation == value)
            def _():
                compute(value, a_scr, s_scr, feature_ref, prev_ref, best_ref)

    def run(dilations, low, middle, high, prev):
        block = jax.ShapeDtypeStruct((slab_depth, band_rows, row_length), jnp.float32)
        anywhere = pl.BlockSpec(memory_space=pl.ANY)
        in_vmem = pl.BlockSpec(memory_space=pltpu.VMEM)
        in_specs = [pl.BlockSpec(memory_space=pltpu.SMEM), anywhere, anywhere, anywhere]
        operands = [dilations, low, middle, high]
        if not first:
            in_specs.append(in_vmem)
            operands.append(prev)
        return pl.pallas_call(
            kernel,
            out_shape=(block, block),
            in_specs=in_specs,
            out_specs=(in_vmem, in_vmem),
            scratch_shapes=[
                pltpu.VMEM((planes + 2 * HALO - 2, band_rows + 2, row_length), jnp.float32),
                pltpu.VMEM((planes, band_rows + 2, row_length), jnp.float32),
                pltpu.SemaphoreType.DMA((3,)),
            ],
            compiler_params=pltpu.CompilerParams(vmem_limit_bytes=56 * 1024 * 1024),
        )(*operands)

    return run


def z_neighbours(block, width):
    count = lax.axis_size("gz")
    forward = [(i, i + 1) for i in range(count - 1)]
    forward.append((count - 1, 0))
    backward = [(target, source) for source, target in forward]
    low = lax.ppermute(lax.slice_in_dim(block, block.shape[0] - width, None, axis=0), "gz", forward)
    high = lax.ppermute(lax.slice_in_dim(block, 0, width, axis=0), "gz", backward)
    return low, high


def invariants(curve_zz, curve_yy, curve_xx, curve_zy, curve_zx, curve_yx):
    trace_sum = curve_xx + curve_yy + curve_zz
    minor_sum = (
        curve_xx * curve_yy
        + curve_xx * curve_zz
        + curve_yy * curve_zz
        - curve_zy * curve_zy
        - curve_zx * curve_zx
        - curve_yx * curve_yx
    )
    return (trace_sum * trace_sum / 3.0 - minor_sum) * jax.nn.sigmoid(-trace_sum)


def signature(smoothed):
    centre = smoothed[1:-1, 1:-1]
    above_z = smoothed[2:, 1:-1]
    below_z = smoothed[:-2, 1:-1]
    above_y = smoothed[1:-1, 2:]
    below_y = smoothed[1:-1, :-2]
    curve_zz = hessian_scale * (above_z - 2.0 * centre + below_z)
    curve_yy = hessian_scale * (above_y - 2.0 * centre + below_y)
    curve_xx = hessian_scale * (jnp.roll(centre, -1, 2) - 2.0 * centre + jnp.roll(centre, 1, 2))
    curve_zy = (
        hessian_scale
        * 0.25
        * (smoothed[2:, 2:] - smoothed[2:, :-2] - smoothed[:-2, 2:] + smoothed[:-2, :-2])
    )
    curve_zx = (
        hessian_scale
        * 0.25
        * (
            jnp.roll(above_z, -1, 2)
            - jnp.roll(above_z, 1, 2)
            - jnp.roll(below_z, -1, 2)
            + jnp.roll(below_z, 1, 2)
        )
    )
    curve_yx = (
        hessian_scale
        * 0.25
        * (
            jnp.roll(above_y, -1, 2)
            - jnp.roll(above_y, 1, 2)
            - jnp.roll(below_y, -1, 2)
            + jnp.roll(below_y, 1, 2)
        )
    )
    return invariants(curve_zz, curve_yy, curve_xx, curve_zy, curve_zx, curve_yx)


def per_device(density, dilations, owner_rank, owner_slot, base_cell, corner_weights):
    slab_depth = density.shape[0]
    band_rows = density.shape[1]
    row_length = density.shape[2]
    banded = with_halo(density, (("gy", 1),), HALO)
    response = None
    features = []
    for level_index in range(SCALES):
        dilation = dilations[level_index]
        along_y = smooth_padded(banded, dilation, 1, band_rows)
        low, high = z_neighbours(along_y, HALO)
        run = level_kernel(level_index, level_index == 0, slab_depth, band_rows, row_length)
        feature, response = run(dilations, low, along_y, high, response)
        features.append(feature.reshape(slab_depth * band_rows, row_length))
    plane = (band_rows - 1) * row_length
    z_index = base_cell // plane
    remainder = base_cell % plane
    y_index = remainder // row_length
    x_index = remainder % row_length
    entries = base_cell.shape[0]
    target_x = jnp.concatenate([x_index, (x_index + 1) % row_length])
    pick_x = (
        jnp.arange(row_length, dtype=jnp.int32)[:, None] == target_x[None, :]
    ).astype(jnp.float32)
    cells = jnp.arange(slab_depth * band_rows, dtype=jnp.int32)[:, None]
    weight_grid = None
    for step_z in (0, 1):
        for step_y in (0, 1):
            row = (z_index + step_z) * band_rows + y_index + step_y
            corner = 4 * step_z + 2 * step_y
            weights = jnp.concatenate([corner_weights[corner], corner_weights[corner + 1]])
            term = jnp.where(cells == jnp.concatenate([row, row])[None, :], weights[None, :], 0.0)
            weight_grid = term if weight_grid is None else weight_grid + term
    partials = []
    for feature in features:
        picked = jnp.dot(
            feature, pick_x, precision=lax.Precision.HIGHEST, preferred_element_type=jnp.float32
        )
        per_column = jnp.sum(picked * weight_grid, axis=0)
        partials.append(per_column[:entries] + per_column[entries:])
    partial_value = jnp.stack(partials)
    owner_group = owner_rank[:, 0]
    groups = lax.axis_size("gy")
    column = owner_group * HOWN + owner_slot
    onehot = (column[:, None] == jnp.arange(groups * HOWN, dtype=jnp.int32)[None, :]).astype(
        jnp.float32
    )
    spread = jnp.dot(
        partial_value, onehot, precision=lax.Precision.HIGHEST, preferred_element_type=jnp.float32
    )
    exchanged = lax.all_to_all(
        spread.reshape(SCALES, groups, HOWN), "gy", split_axis=1, concat_axis=1, tiled=True
    )
    catalogue = jnp.sum(exchanged, axis=1)
    return (response, catalogue)


def solution(mesh):
    placed = (
        P("gz", "gy", None),
        P(),
        P(("gz", "gy"), None),
        P(("gz", "gy")),
        P(("gz", "gy")),
        P(None, ("gz", "gy")),
    )
    return jax.shard_map(
        per_device,
        mesh=mesh,
        in_specs=placed,
        out_specs=(P("gz", "gy", None), P(None, ("gz", "gy"))),
        check_vma=False,
    )
```

```python
import jax
import jax.numpy as jnp
from jax import lax
from jax.experimental import pallas as pl
from jax.experimental.pallas import tpu as pltpu
from jax.sharding import PartitionSpec as P

SCALES = 3
HALO = 9
HOWN = 256
DMAX = 4


tap_weights = (0.0625, 0.25, 0.375, 0.25, 0.0625)
hessian_scale = 4.0


def with_halo(block, sides, width):
    for axis, dim in sides:
        count = lax.axis_size(axis)
        forward = [(i, i + 1) for i in range(count - 1)]
        forward.append((count - 1, 0))
        backward = [(target, source) for source, target in forward]
        low = lax.ppermute(
            lax.slice_in_dim(block, block.shape[dim] - width, None, axis=dim), axis, forward
        )
        high = lax.ppermute(lax.slice_in_dim(block, 0, width, axis=dim), axis, backward)
        block = jnp.concatenate([low, block, high], axis=dim)
    return block


def smooth_padded(field_data, dilation, along_dim, extent):
    running = None
    for offset in range(5):
        start_at = HALO - 1 + (offset - 2) * dilation
        summand = tap_weights[offset] * lax.dynamic_slice_in_dim(
            field_data, start_at, extent + 2, along_dim
        )
        running = summand if running is None else running + summand
    return running


def smooth_periodic(field_data, dilation):
    running = None
    for offset in range(5):
        summand = tap_weights[offset] * jnp.roll(field_data, -(offset - 2) * dilation, axis=2)
        running = summand if running is None else running + summand
    return running


def level_kernel(level_index, first, slab_depth, band_rows, row_length):
    planes = slab_depth + 2

    def compute(dilation, a_scr, s_scr, feature_ref, prev_ref, best_ref, row_wait, prev_copy, out_copy):
        reach = HALO - 1 + 2 * dilation
        for row in range(reach):
            row_wait(row)

        def smooth_plane(plane, carry):
            row_wait(reach + plane)
            for first_row in range(0, band_rows + 2, 8):
                rows = min(8, band_rows + 2 - first_row)
                along_z = None
                for offset in range(5):
                    source = HALO - 1 + plane + (offset - 2) * dilation
                    summand = tap_weights[offset] * a_scr[source, pl.ds(first_row, rows), :]
                    along_z = summand if along_z is None else along_z + summand
                running = None
                for offset in range(5):
                    shift = (-(offset - 2) * dilation) % row_length
                    moved = along_z if shift == 0 else pltpu.roll(along_z, shift, 1)
                    summand = tap_weights[offset] * moved
                    running = summand if running is None else running + summand
                s_scr[plane, pl.ds(first_row, rows), :] = running
            return carry

        lax.fori_loop(0, planes, smooth_plane, 0)
        for row in range(reach + planes, planes + 2 * HALO - 2):
            row_wait(row)
        if prev_copy is not None:
            prev_copy.wait()

        def feature_plane(z, carry):
            for half in range(band_rows // 8):
                y0 = half * 8

                def at(dz, dy):
                    return s_scr[z + 1 + dz, pl.ds(1 + y0 + dy, 8), :]

                def left(v):
                    return pltpu.roll(v, row_length - 1, 1)

                def right(v):
                    return pltpu.roll(v, 1, 1)

                centre = at(0, 0)
                above_z = at(1, 0)
                below_z = at(-1, 0)
                curve_zz = hessian_scale * (above_z - 2.0 * centre + below_z)
                across_z = above_z - below_z
                curve_zx = (hessian_scale * 0.25) * (left(across_z) - right(across_z))
                above_y = at(0, 1)
                below_y = at(0, -1)
                curve_yy = hessian_scale * (above_y - 2.0 * centre + below_y)
                across_y = above_y - below_y
                curve_yx = (hessian_scale * 0.25) * (left(across_y) - right(across_y))
                curve_xx = hessian_scale * (left(centre) - 2.0 * centre + right(centre))
                trace_sum = curve_xx + curve_yy + curve_zz
                minor_sum = curve_xx * curve_yy + curve_xx * curve_zz + curve_yy * curve_zz
                minor_sum = minor_sum - curve_zx * curve_zx - curve_yx * curve_yx
                curve_zy = (hessian_scale * 0.25) * (at(1, 1) - at(1, -1) - at(-1, 1) + at(-1, -1))
                minor_sum = minor_sum - curve_zy * curve_zy
                value = (trace_sum * trace_sum / 3.0 - minor_sum) * (1.0 / (1.0 + jnp.exp(trace_sum)))
                feature_ref[z, pl.ds(y0, 8), :] = value
                if first:
                    best_ref[z, pl.ds(y0, 8), :] = value
                else:
                    best_ref[z, pl.ds(y0, 8), :] = jnp.maximum(prev_ref[z, pl.ds(y0, 8), :], value)
            for copy in out_copy(z):
                copy.start()
            return carry

        lax.fori_loop(0, slab_depth, feature_plane, 0)
        for z in range(slab_depth):
            for copy in out_copy(z):
                copy.wait()

    def kernel(*refs):
        if first:
            (dil_ref, lo_hbm, mid_hbm, hi_hbm, feature_hbm, best_hbm,
             a_scr, s_scr, f_scr, b_scr, p_scr, row_sems, out_sems, prev_sem) = refs
        else:
            (dil_ref, lo_hbm, mid_hbm, hi_hbm, prev_hbm, feature_hbm, best_hbm,
             a_scr, s_scr, f_scr, b_scr, p_scr, row_sems, out_sems, prev_sem) = refs
        pieces = [(lo_hbm, HALO), (mid_hbm, slab_depth), (hi_hbm, HALO)]
        row = 0
        for source, count in pieces:
            for index in range(count):
                pltpu.make_async_copy(source.at[index], a_scr.at[row], row_sems.at[row]).start()
                row += 1
        prev_copy = None
        if not first:
            prev_copy = pltpu.make_async_copy(prev_hbm, p_scr, prev_sem.at[0])
            prev_copy.start()

        def row_wait(row):
            pltpu.make_async_copy(mid_hbm.at[0], a_scr.at[row], row_sems.at[row]).wait()

        def out_copy(z):
            return [
                pltpu.make_async_copy(f_scr.at[z], feature_hbm.at[z], out_sems.at[0, z]),
                pltpu.make_async_copy(b_scr.at[z], best_hbm.at[z], out_sems.at[1, z]),
            ]

        def branch(value):
            def run_branch():
                compute(value, a_scr, s_scr, f_scr, None if first else p_scr, b_scr,
                        row_wait, prev_copy, out_copy)
            return run_branch

        pick = jnp.clip(dil_ref[level_index], 1, DMAX) - 1
        lax.switch(pick, [branch(value) for value in range(1, DMAX + 1)])

    def run(dilations, low, middle, high, prev):
        block = jax.ShapeDtypeStruct((slab_depth, band_rows, row_length), jnp.float32)
        anywhere = pl.BlockSpec(memory_space=pl.ANY)
        in_specs = [pl.BlockSpec(memory_space=pltpu.SMEM), anywhere, anywhere, anywhere]
        operands = [dilations, low, middle, high]
        if not first:
            in_specs.append(anywhere)
            operands.append(prev)
        total_rows = planes + 2 * HALO - 2
        return pl.pallas_call(
            kernel,
            out_shape=(block, block),
            in_specs=in_specs,
            out_specs=(anywhere, anywhere),
            scratch_shapes=[
                pltpu.VMEM((total_rows, band_rows + 2, row_length), jnp.float32),
                pltpu.VMEM((planes, band_rows + 2, row_length), jnp.float32),
                pltpu.VMEM((slab_depth, band_rows, row_length), jnp.float32),
                pltpu.VMEM((slab_depth, band_rows, row_length), jnp.float32),
                pltpu.VMEM((slab_depth, band_rows, row_length), jnp.float32),
                pltpu.SemaphoreType.DMA((total_rows,)),
                pltpu.SemaphoreType.DMA((2, slab_depth)),
                pltpu.SemaphoreType.DMA((1,)),
            ],
            compiler_params=pltpu.CompilerParams(vmem_limit_bytes=56 * 1024 * 1024),
        )(*operands)

    return run


def z_neighbours(block, width):
    count = lax.axis_size("gz")
    forward = [(i, i + 1) for i in range(count - 1)]
    forward.append((count - 1, 0))
    backward = [(target, source) for source, target in forward]
    low = lax.ppermute(lax.slice_in_dim(block, block.shape[0] - width, None, axis=0), "gz", forward)
    high = lax.ppermute(lax.slice_in_dim(block, 0, width, axis=0), "gz", backward)
    return low, high


def invariants(curve_zz, curve_yy, curve_xx, curve_zy, curve_zx, curve_yx):
    trace_sum = curve_xx + curve_yy + curve_zz
    minor_sum = (
        curve_xx * curve_yy
        + curve_xx * curve_zz
        + curve_yy * curve_zz
        - curve_zy * curve_zy
        - curve_zx * curve_zx
        - curve_yx * curve_yx
    )
    return (trace_sum * trace_sum / 3.0 - minor_sum) * jax.nn.sigmoid(-trace_sum)


def signature(smoothed):
    centre = smoothed[1:-1, 1:-1]
    above_z = smoothed[2:, 1:-1]
    below_z = smoothed[:-2, 1:-1]
    above_y = smoothed[1:-1, 2:]
    below_y = smoothed[1:-1, :-2]
    curve_zz = hessian_scale * (above_z - 2.0 * centre + below_z)
    curve_yy = hessian_scale * (above_y - 2.0 * centre + below_y)
    curve_xx = hessian_scale * (jnp.roll(centre, -1, 2) - 2.0 * centre + jnp.roll(centre, 1, 2))
    curve_zy = (
        hessian_scale
        * 0.25
        * (smoothed[2:, 2:] - smoothed[2:, :-2] - smoothed[:-2, 2:] + smoothed[:-2, :-2])
    )
    curve_zx = (
        hessian_scale
        * 0.25
        * (
            jnp.roll(above_z, -1, 2)
            - jnp.roll(above_z, 1, 2)
            - jnp.roll(below_z, -1, 2)
            + jnp.roll(below_z, 1, 2)
        )
    )
    curve_yx = (
        hessian_scale
        * 0.25
        * (
            jnp.roll(above_y, -1, 2)
            - jnp.roll(above_y, 1, 2)
            - jnp.roll(below_y, -1, 2)
            + jnp.roll(below_y, 1, 2)
        )
    )
    return invariants(curve_zz, curve_yy, curve_xx, curve_zy, curve_zx, curve_yx)


def per_device(density, dilations, owner_rank, owner_slot, base_cell, corner_weights):
    slab_depth = density.shape[0]
    band_rows = density.shape[1]
    row_length = density.shape[2]
    banded = with_halo(density, (("gy", 1),), HALO)
    response = None
    features = []
    for level_index in range(SCALES):
        dilation = dilations[level_index]
        along_y = smooth_padded(banded, dilation, 1, band_rows)
        low, high = z_neighbours(along_y, HALO)
        run = level_kernel(level_index, level_index == 0, slab_depth, band_rows, row_length)
        feature, response = run(dilations, low, along_y, high, response)
        features.append(feature.reshape(slab_depth * band_rows, row_length))
    plane = (band_rows - 1) * row_length
    z_index = base_cell // plane
    remainder = base_cell % plane
    y_index = remainder // row_length
    x_index = remainder % row_length
    entries = base_cell.shape[0]
    target_x = jnp.concatenate([x_index, (x_index + 1) % row_length])
    pick_x = (
        jnp.arange(row_length, dtype=jnp.int32)[:, None] == target_x[None, :]
    ).astype(jnp.float32)
    cells = jnp.arange(slab_depth * band_rows, dtype=jnp.int32)[:, None]
    weight_grid = None
    for step_z in (0, 1):
        for step_y in (0, 1):
            row = (z_index + step_z) * band_rows + y_index + step_y
            corner = 4 * step_z + 2 * step_y
            weights = jnp.concatenate([corner_weights[corner], corner_weights[corner + 1]])
            term = jnp.where(cells == jnp.concatenate([row, row])[None, :], weights[None, :], 0.0)
            weight_grid = term if weight_grid is None else weight_grid + term
    partials = []
    for feature in features:
        picked = jnp.dot(
            feature, pick_x, precision=lax.Precision.HIGHEST, preferred_element_type=jnp.float32
        )
        per_column = jnp.sum(picked * weight_grid, axis=0)
        partials.append(per_column[:entries] + per_column[entries:])
    partial_value = jnp.stack(partials)
    owner_group = owner_rank[:, 0]
    groups = lax.axis_size("gy")
    column = owner_group * HOWN + owner_slot
    onehot = (column[:, None] == jnp.arange(groups * HOWN, dtype=jnp.int32)[None, :]).astype(
        jnp.float32
    )
    spread = jnp.dot(
        partial_value, onehot, precision=lax.Precision.HIGHEST, preferred_element_type=jnp.float32
    )
    exchanged = lax.all_to_all(
        spread.reshape(SCALES, groups, HOWN), "gy", split_axis=1, concat_axis=1, tiled=True
    )
    catalogue = jnp.sum(exchanged, axis=1)
    return (response, catalogue)


def solution(mesh):
    placed = (
        P("gz", "gy", None),
        P(),
        P(("gz", "gy"), None),
        P(("gz", "gy")),
        P(("gz", "gy")),
        P(None, ("gz", "gy")),
    )
    return jax.shard_map(
        per_device,
        mesh=mesh,
        in_specs=placed,
        out_specs=(P("gz", "gy", None), P(None, ("gz", "gy"))),
        check_vma=False,
    )
```

```python
import jax
import jax.numpy as jnp
from jax import lax
from jax.experimental import pallas as pl
from jax.experimental.pallas import tpu as pltpu
from jax.sharding import PartitionSpec as P

SCALES = 3
HALO = 9
HOWN = 256
DMAX = 4


tap_weights = (0.0625, 0.25, 0.375, 0.25, 0.0625)
hessian_scale = 4.0


def flat_ppermute(part, axis, pairs):
    rows = part.shape[0] * part.shape[1]
    moved = lax.ppermute(part.reshape(rows, part.shape[2]), axis, pairs)
    return moved.reshape(part.shape)


def with_halo(block, sides, width):
    for axis, dim in sides:
        count = lax.axis_size(axis)
        forward = [(i, i + 1) for i in range(count - 1)]
        forward.append((count - 1, 0))
        backward = [(target, source) for source, target in forward]
        low = flat_ppermute(
            lax.slice_in_dim(block, block.shape[dim] - width, None, axis=dim), axis, forward
        )
        high = flat_ppermute(lax.slice_in_dim(block, 0, width, axis=dim), axis, backward)
        block = jnp.concatenate([low, block, high], axis=dim)
    return block


def smooth_padded(field_data, dilation, along_dim, extent):
    running = None
    for offset in range(5):
        start_at = HALO - 1 + (offset - 2) * dilation
        summand = tap_weights[offset] * lax.dynamic_slice_in_dim(
            field_data, start_at, extent + 2, along_dim
        )
        running = summand if running is None else running + summand
    return running


def smooth_periodic(field_data, dilation):
    running = None
    for offset in range(5):
        summand = tap_weights[offset] * jnp.roll(field_data, -(offset - 2) * dilation, axis=2)
        running = summand if running is None else running + summand
    return running


def level_kernel(level_index, first, slab_depth, band_rows, row_length):
    planes = slab_depth + 2

    def compute(dilation, a_scr, s_scr, feature_ref, prev_ref, best_ref, row_wait, prev_copy, out_copy):
        reach = HALO - 1 + 2 * dilation
        for row in range(reach):
            row_wait(row)

        def smooth_plane(plane, carry):
            row_wait(reach + plane)
            for first_row in range(0, band_rows + 2, 8):
                rows = min(8, band_rows + 2 - first_row)
                along_z = None
                for offset in range(5):
                    source = HALO - 1 + plane + (offset - 2) * dilation
                    summand = tap_weights[offset] * a_scr[source, pl.ds(first_row, rows), :]
                    along_z = summand if along_z is None else along_z + summand
                running = None
                for offset in range(5):
                    shift = (-(offset - 2) * dilation) % row_length
                    moved = along_z if shift == 0 else pltpu.roll(along_z, shift, 1)
                    summand = tap_weights[offset] * moved
                    running = summand if running is None else running + summand
                s_scr[plane, pl.ds(first_row, rows), :] = running
            return carry

        lax.fori_loop(0, planes, smooth_plane, 0)
        for row in range(reach + planes, planes + 2 * HALO - 2):
            row_wait(row)
        if prev_copy is not None:
            prev_copy.wait()

        def feature_plane(z, carry):
            for half in range(band_rows // 8):
                y0 = half * 8

                def at(dz, dy):
                    return s_scr[z + 1 + dz, pl.ds(1 + y0 + dy, 8), :]

                def left(v):
                    return pltpu.roll(v, row_length - 1, 1)

                def right(v):
                    return pltpu.roll(v, 1, 1)

                centre = at(0, 0)
                above_z = at(1, 0)
                below_z = at(-1, 0)
                curve_zz = hessian_scale * (above_z - 2.0 * centre + below_z)
                across_z = above_z - below_z
                curve_zx = (hessian_scale * 0.25) * (left(across_z) - right(across_z))
                above_y = at(0, 1)
                below_y = at(0, -1)
                curve_yy = hessian_scale * (above_y - 2.0 * centre + below_y)
                across_y = above_y - below_y
                curve_yx = (hessian_scale * 0.25) * (left(across_y) - right(across_y))
                curve_xx = hessian_scale * (left(centre) - 2.0 * centre + right(centre))
                trace_sum = curve_xx + curve_yy + curve_zz
                minor_sum = curve_xx * curve_yy + curve_xx * curve_zz + curve_yy * curve_zz
                minor_sum = minor_sum - curve_zx * curve_zx - curve_yx * curve_yx
                curve_zy = (hessian_scale * 0.25) * (at(1, 1) - at(1, -1) - at(-1, 1) + at(-1, -1))
                minor_sum = minor_sum - curve_zy * curve_zy
                value = (trace_sum * trace_sum / 3.0 - minor_sum) * (1.0 / (1.0 + jnp.exp(trace_sum)))
                feature_ref[z, pl.ds(y0, 8), :] = value
                if first:
                    best_ref[z, pl.ds(y0, 8), :] = value
                else:
                    best_ref[z, pl.ds(y0, 8), :] = jnp.maximum(prev_ref[z, pl.ds(y0, 8), :], value)
            for copy in out_copy(z):
                copy.start()
            return carry

        lax.fori_loop(0, slab_depth, feature_plane, 0)
        for z in range(slab_depth):
            for copy in out_copy(z):
                copy.wait()

    def kernel(*refs):
        if first:
            (dil_ref, lo_hbm, mid_hbm, hi_hbm, feature_hbm, best_hbm,
             a_scr, s_scr, f_scr, b_scr, p_scr, row_sems, out_sems, prev_sem) = refs
        else:
            (dil_ref, lo_hbm, mid_hbm, hi_hbm, prev_hbm, feature_hbm, best_hbm,
             a_scr, s_scr, f_scr, b_scr, p_scr, row_sems, out_sems, prev_sem) = refs
        pieces = [(lo_hbm, HALO), (mid_hbm, slab_depth), (hi_hbm, HALO)]
        row = 0
        for source, count in pieces:
            for index in range(count):
                pltpu.make_async_copy(source.at[index], a_scr.at[row], row_sems.at[row]).start()
                row += 1
        prev_copy = None
        if not first:
            prev_copy = pltpu.make_async_copy(prev_hbm, p_scr, prev_sem.at[0])
            prev_copy.start()

        def row_wait(row):
            pltpu.make_async_copy(mid_hbm.at[0], a_scr.at[row], row_sems.at[row]).wait()

        def out_copy(z):
            return [
                pltpu.make_async_copy(f_scr.at[z], feature_hbm.at[z], out_sems.at[0, z]),
                pltpu.make_async_copy(b_scr.at[z], best_hbm.at[z], out_sems.at[1, z]),
            ]

        def branch(value):
            def run_branch():
                compute(value, a_scr, s_scr, f_scr, None if first else p_scr, b_scr,
                        row_wait, prev_copy, out_copy)
            return run_branch

        pick = jnp.clip(dil_ref[level_index], 1, DMAX) - 1
        lax.switch(pick, [branch(value) for value in range(1, DMAX + 1)])

    def run(dilations, low, middle, high, prev):
        block = jax.ShapeDtypeStruct((slab_depth, band_rows, row_length), jnp.float32)
        anywhere = pl.BlockSpec(memory_space=pl.ANY)
        in_specs = [pl.BlockSpec(memory_space=pltpu.SMEM), anywhere, anywhere, anywhere]
        operands = [dilations, low, middle, high]
        if not first:
            in_specs.append(anywhere)
            operands.append(prev)
        total_rows = planes + 2 * HALO - 2
        return pl.pallas_call(
            kernel,
            out_shape=(block, block),
            in_specs=in_specs,
            out_specs=(anywhere, anywhere),
            scratch_shapes=[
                pltpu.VMEM((total_rows, band_rows + 2, row_length), jnp.float32),
                pltpu.VMEM((planes, band_rows + 2, row_length), jnp.float32),
                pltpu.VMEM((slab_depth, band_rows, row_length), jnp.float32),
                pltpu.VMEM((slab_depth, band_rows, row_length), jnp.float32),
                pltpu.VMEM((slab_depth, band_rows, row_length), jnp.float32),
                pltpu.SemaphoreType.DMA((total_rows,)),
                pltpu.SemaphoreType.DMA((2, slab_depth)),
                pltpu.SemaphoreType.DMA((1,)),
            ],
            compiler_params=pltpu.CompilerParams(vmem_limit_bytes=56 * 1024 * 1024),
        )(*operands)

    return run


def z_neighbours(block, width):
    count = lax.axis_size("gz")
    forward = [(i, i + 1) for i in range(count - 1)]
    forward.append((count - 1, 0))
    backward = [(target, source) for source, target in forward]
    low = flat_ppermute(lax.slice_in_dim(block, block.shape[0] - width, None, axis=0), "gz", forward)
    high = flat_ppermute(lax.slice_in_dim(block, 0, width, axis=0), "gz", backward)
    return low, high


def invariants(curve_zz, curve_yy, curve_xx, curve_zy, curve_zx, curve_yx):
    trace_sum = curve_xx + curve_yy + curve_zz
    minor_sum = (
        curve_xx * curve_yy
        + curve_xx * curve_zz
        + curve_yy * curve_zz
        - curve_zy * curve_zy
        - curve_zx * curve_zx
        - curve_yx * curve_yx
    )
    return (trace_sum * trace_sum / 3.0 - minor_sum) * jax.nn.sigmoid(-trace_sum)


def signature(smoothed):
    centre = smoothed[1:-1, 1:-1]
    above_z = smoothed[2:, 1:-1]
    below_z = smoothed[:-2, 1:-1]
    above_y = smoothed[1:-1, 2:]
    below_y = smoothed[1:-1, :-2]
    curve_zz = hessian_scale * (above_z - 2.0 * centre + below_z)
    curve_yy = hessian_scale * (above_y - 2.0 * centre + below_y)
    curve_xx = hessian_scale * (jnp.roll(centre, -1, 2) - 2.0 * centre + jnp.roll(centre, 1, 2))
    curve_zy = (
        hessian_scale
        * 0.25
        * (smoothed[2:, 2:] - smoothed[2:, :-2] - smoothed[:-2, 2:] + smoothed[:-2, :-2])
    )
    curve_zx = (
        hessian_scale
        * 0.25
        * (
            jnp.roll(above_z, -1, 2)
            - jnp.roll(above_z, 1, 2)
            - jnp.roll(below_z, -1, 2)
            + jnp.roll(below_z, 1, 2)
        )
    )
    curve_yx = (
        hessian_scale
        * 0.25
        * (
            jnp.roll(above_y, -1, 2)
            - jnp.roll(above_y, 1, 2)
            - jnp.roll(below_y, -1, 2)
            + jnp.roll(below_y, 1, 2)
        )
    )
    return invariants(curve_zz, curve_yy, curve_xx, curve_zy, curve_zx, curve_yx)


def per_device(density, dilations, owner_rank, owner_slot, base_cell, corner_weights):
    slab_depth = density.shape[0]
    band_rows = density.shape[1]
    row_length = density.shape[2]
    banded = with_halo(density, (("gy", 1),), HALO)
    response = None
    features = []
    for level_index in range(SCALES):
        dilation = dilations[level_index]
        along_y = smooth_padded(banded, dilation, 1, band_rows)
        low, high = z_neighbours(along_y, HALO)
        run = level_kernel(level_index, level_index == 0, slab_depth, band_rows, row_length)
        feature, response = run(dilations, low, along_y, high, response)
        features.append(feature.reshape(slab_depth * band_rows, row_length))
    plane = (band_rows - 1) * row_length
    z_index = base_cell // plane
    remainder = base_cell % plane
    y_index = remainder // row_length
    x_index = remainder % row_length
    entries = base_cell.shape[0]
    target_x = jnp.concatenate([x_index, (x_index + 1) % row_length])
    pick_x = (
        jnp.arange(row_length, dtype=jnp.int32)[:, None] == target_x[None, :]
    ).astype(jnp.float32)
    cells = jnp.arange(slab_depth * band_rows, dtype=jnp.int32)[:, None]
    weight_grid = None
    for step_z in (0, 1):
        for step_y in (0, 1):
            row = (z_index + step_z) * band_rows + y_index + step_y
            corner = 4 * step_z + 2 * step_y
            weights = jnp.concatenate([corner_weights[corner], corner_weights[corner + 1]])
            term = jnp.where(cells == jnp.concatenate([row, row])[None, :], weights[None, :], 0.0)
            weight_grid = term if weight_grid is None else weight_grid + term
    partials = []
    for feature in features:
        picked = jnp.dot(
            feature, pick_x, precision=lax.Precision.HIGHEST, preferred_element_type=jnp.float32
        )
        per_column = jnp.sum(picked * weight_grid, axis=0)
        partials.append(per_column[:entries] + per_column[entries:])
    partial_value = jnp.stack(partials)
    owner_group = owner_rank[:, 0]
    groups = lax.axis_size("gy")
    column = owner_group * HOWN + owner_slot
    onehot = (column[:, None] == jnp.arange(groups * HOWN, dtype=jnp.int32)[None, :]).astype(
        jnp.float32
    )
    spread = jnp.dot(
        partial_value, onehot, precision=lax.Precision.HIGHEST, preferred_element_type=jnp.float32
    )
    exchanged = lax.all_to_all(
        spread.reshape(SCALES, groups, HOWN), "gy", split_axis=1, concat_axis=1, tiled=True
    )
    catalogue = jnp.sum(exchanged, axis=1)
    return (response, catalogue)


def solution(mesh):
    placed = (
        P("gz", "gy", None),
        P(),
        P(("gz", "gy"), None),
        P(("gz", "gy")),
        P(("gz", "gy")),
        P(None, ("gz", "gy")),
    )
    return jax.shard_map(
        per_device,
        mesh=mesh,
        in_specs=placed,
        out_specs=(P("gz", "gy", None), P(None, ("gz", "gy"))),
        check_vma=False,
    )
```

```python
import jax
import jax.numpy as jnp
from jax import lax
from jax.experimental import pallas as pl
from jax.experimental.pallas import tpu as pltpu
from jax.sharding import PartitionSpec as P

SCALES = 3
HALO = 9
HOWN = 256
DMAX = 4


tap_weights = (0.0625, 0.25, 0.375, 0.25, 0.0625)
hessian_scale = 4.0


def flat_ppermute(part, axis, pairs):
    rows = part.shape[0] * part.shape[1]
    moved = lax.ppermute(part.reshape(rows, part.shape[2]), axis, pairs)
    return moved.reshape(part.shape)


def with_halo(block, sides, width):
    for axis, dim in sides:
        count = lax.axis_size(axis)
        forward = [(i, i + 1) for i in range(count - 1)]
        forward.append((count - 1, 0))
        backward = [(target, source) for source, target in forward]
        low = flat_ppermute(
            lax.slice_in_dim(block, block.shape[dim] - width, None, axis=dim), axis, forward
        )
        high = flat_ppermute(lax.slice_in_dim(block, 0, width, axis=dim), axis, backward)
        block = jnp.concatenate([low, block, high], axis=dim)
    return block


def smooth_padded(field_data, dilation, along_dim, extent):
    running = None
    for offset in range(5):
        start_at = HALO - 1 + (offset - 2) * dilation
        summand = tap_weights[offset] * lax.dynamic_slice_in_dim(
            field_data, start_at, extent + 2, along_dim
        )
        running = summand if running is None else running + summand
    return running


def smooth_periodic(field_data, dilation):
    running = None
    for offset in range(5):
        summand = tap_weights[offset] * jnp.roll(field_data, -(offset - 2) * dilation, axis=2)
        running = summand if running is None else running + summand
    return running


def level_kernel(level_index, first, slab_depth, band_rows, row_length):
    planes = slab_depth + 2

    def compute(dilation, a_scr, s_scr, feature_ref, prev_ref, best_ref, row_wait, prev_copy,
                out_copy, edges_in):
        reach = HALO - 1 + 2 * dilation
        last_mid = HALO + slab_depth - 1
        edges_in()
        for row in range(HALO, min(reach, last_mid + 1)):
            row_wait(row)

        def smooth_plane(plane, carry):
            @pl.when(reach + plane <= last_mid)
            def _():
                row_wait(reach + plane)

            for first_row in range(0, band_rows + 2, 8):
                rows = min(8, band_rows + 2 - first_row)
                along_z = None
                for offset in range(5):
                    source = HALO - 1 + plane + (offset - 2) * dilation
                    summand = tap_weights[offset] * a_scr[source, pl.ds(first_row, rows), :]
                    along_z = summand if along_z is None else along_z + summand
                running = None
                for offset in range(5):
                    shift = (-(offset - 2) * dilation) % row_length
                    moved = along_z if shift == 0 else pltpu.roll(along_z, shift, 1)
                    summand = tap_weights[offset] * moved
                    running = summand if running is None else running + summand
                s_scr[plane, pl.ds(first_row, rows), :] = running
            return carry

        lax.fori_loop(0, planes, smooth_plane, 0)
        for row in range(max(reach + planes, HALO), last_mid + 1):
            row_wait(row)
        if prev_copy is not None:
            prev_copy.wait()

        def feature_plane(z, carry):
            for half in range(band_rows // 8):
                y0 = half * 8

                def at(dz, dy):
                    return s_scr[z + 1 + dz, pl.ds(1 + y0 + dy, 8), :]

                def left(v):
                    return pltpu.roll(v, row_length - 1, 1)

                def right(v):
                    return pltpu.roll(v, 1, 1)

                centre = at(0, 0)
                above_z = at(1, 0)
                below_z = at(-1, 0)
                curve_zz = hessian_scale * (above_z - 2.0 * centre + below_z)
                across_z = above_z - below_z
                curve_zx = (hessian_scale * 0.25) * (left(across_z) - right(across_z))
                above_y = at(0, 1)
                below_y = at(0, -1)
                curve_yy = hessian_scale * (above_y - 2.0 * centre + below_y)
                across_y = above_y - below_y
                curve_yx = (hessian_scale * 0.25) * (left(across_y) - right(across_y))
                curve_xx = hessian_scale * (left(centre) - 2.0 * centre + right(centre))
                trace_sum = curve_xx + curve_yy + curve_zz
                minor_sum = curve_xx * curve_yy + curve_xx * curve_zz + curve_yy * curve_zz
                minor_sum = minor_sum - curve_zx * curve_zx - curve_yx * curve_yx
                curve_zy = (hessian_scale * 0.25) * (at(1, 1) - at(1, -1) - at(-1, 1) + at(-1, -1))
                minor_sum = minor_sum - curve_zy * curve_zy
                value = (trace_sum * trace_sum / 3.0 - minor_sum) * (1.0 / (1.0 + jnp.exp(trace_sum)))
                feature_ref[z, pl.ds(y0, 8), :] = value
                if first:
                    best_ref[z, pl.ds(y0, 8), :] = value
                else:
                    best_ref[z, pl.ds(y0, 8), :] = jnp.maximum(prev_ref[z, pl.ds(y0, 8), :], value)
            for copy in out_copy(z):
                copy.start()
            return carry

        lax.fori_loop(0, slab_depth, feature_plane, 0)
        for z in range(slab_depth):
            for copy in out_copy(z):
                copy.wait()

    def kernel(*refs):
        if first:
            (dil_ref, lo_hbm, mid_hbm, hi_hbm, feature_hbm, best_hbm,
             a_scr, s_scr, f_scr, b_scr, p_scr, lo_scr, hi_scr, row_sems, out_sems, prev_sem,
             edge_sems) = refs
        else:
            (dil_ref, lo_hbm, mid_hbm, hi_hbm, prev_hbm, feature_hbm, best_hbm,
             a_scr, s_scr, f_scr, b_scr, p_scr, lo_scr, hi_scr, row_sems, out_sems, prev_sem,
             edge_sems) = refs
        edge_copies = [
            pltpu.make_async_copy(lo_hbm, lo_scr, edge_sems.at[0]),
            pltpu.make_async_copy(hi_hbm, hi_scr, edge_sems.at[1]),
        ]
        for copy in edge_copies:
            copy.start()
        for index in range(slab_depth):
            row = HALO + index
            pltpu.make_async_copy(mid_hbm.at[index], a_scr.at[row], row_sems.at[row]).start()
        prev_copy = None
        if not first:
            prev_copy = pltpu.make_async_copy(prev_hbm, p_scr, prev_sem.at[0])
            prev_copy.start()

        def row_wait(row):
            pltpu.make_async_copy(mid_hbm.at[0], a_scr.at[row], row_sems.at[row]).wait()

        width = band_rows + 2

        def edges_in():
            for copy, flat, first_row in zip(edge_copies, (lo_scr, hi_scr), (0, HALO + slab_depth)):
                copy.wait()
                for index in range(HALO):
                    a_scr[first_row + index] = flat[pl.ds(index * width, width), :]

        def out_copy(z):
            return [
                pltpu.make_async_copy(f_scr.at[z], feature_hbm.at[z], out_sems.at[0, z]),
                pltpu.make_async_copy(b_scr.at[z], best_hbm.at[z], out_sems.at[1, z]),
            ]

        def branch(value):
            def run_branch():
                compute(value, a_scr, s_scr, f_scr, None if first else p_scr, b_scr,
                        row_wait, prev_copy, out_copy, edges_in)
            return run_branch

        pick = jnp.clip(dil_ref[level_index], 1, DMAX) - 1
        lax.switch(pick, [branch(value) for value in range(1, DMAX + 1)])

    def run(dilations, low, middle, high, prev):
        block = jax.ShapeDtypeStruct((slab_depth, band_rows, row_length), jnp.float32)
        anywhere = pl.BlockSpec(memory_space=pl.ANY)
        in_specs = [pl.BlockSpec(memory_space=pltpu.SMEM), anywhere, anywhere, anywhere]
        operands = [dilations, low, middle, high]
        if not first:
            in_specs.append(anywhere)
            operands.append(prev)
        total_rows = planes + 2 * HALO - 2
        return pl.pallas_call(
            kernel,
            out_shape=(block, block),
            in_specs=in_specs,
            out_specs=(anywhere, anywhere),
            scratch_shapes=[
                pltpu.VMEM((total_rows, band_rows + 2, row_length), jnp.float32),
                pltpu.VMEM((planes, band_rows + 2, row_length), jnp.float32),
                pltpu.VMEM((slab_depth, band_rows, row_length), jnp.float32),
                pltpu.VMEM((slab_depth, band_rows, row_length), jnp.float32),
                pltpu.VMEM((slab_depth, band_rows, row_length), jnp.float32),
                pltpu.VMEM((HALO * (band_rows + 2), row_length), jnp.float32),
                pltpu.VMEM((HALO * (band_rows + 2), row_length), jnp.float32),
                pltpu.SemaphoreType.DMA((total_rows,)),
                pltpu.SemaphoreType.DMA((2, slab_depth)),
                pltpu.SemaphoreType.DMA((1,)),
                pltpu.SemaphoreType.DMA((2,)),
            ],
            compiler_params=pltpu.CompilerParams(vmem_limit_bytes=56 * 1024 * 1024),
        )(*operands)

    return run


def z_neighbours(block, width):
    count = lax.axis_size("gz")
    forward = [(i, i + 1) for i in range(count - 1)]
    forward.append((count - 1, 0))
    backward = [(target, source) for source, target in forward]
    def flat(part):
        return part.reshape(part.shape[0] * part.shape[1], part.shape[2])

    low = lax.ppermute(flat(lax.slice_in_dim(block, block.shape[0] - width, None, axis=0)), "gz", forward)
    high = lax.ppermute(flat(lax.slice_in_dim(block, 0, width, axis=0)), "gz", backward)
    return low, high


def invariants(curve_zz, curve_yy, curve_xx, curve_zy, curve_zx, curve_yx):
    trace_sum = curve_xx + curve_yy + curve_zz
    minor_sum = (
        curve_xx * curve_yy
        + curve_xx * curve_zz
        + curve_yy * curve_zz
        - curve_zy * curve_zy
        - curve_zx * curve_zx
        - curve_yx * curve_yx
    )
    return (trace_sum * trace_sum / 3.0 - minor_sum) * jax.nn.sigmoid(-trace_sum)


def signature(smoothed):
    centre = smoothed[1:-1, 1:-1]
    above_z = smoothed[2:, 1:-1]
    below_z = smoothed[:-2, 1:-1]
    above_y = smoothed[1:-1, 2:]
    below_y = smoothed[1:-1, :-2]
    curve_zz = hessian_scale * (above_z - 2.0 * centre + below_z)
    curve_yy = hessian_scale * (above_y - 2.0 * centre + below_y)
    curve_xx = hessian_scale * (jnp.roll(centre, -1, 2) - 2.0 * centre + jnp.roll(centre, 1, 2))
    curve_zy = (
        hessian_scale
        * 0.25
        * (smoothed[2:, 2:] - smoothed[2:, :-2] - smoothed[:-2, 2:] + smoothed[:-2, :-2])
    )
    curve_zx = (
        hessian_scale
        * 0.25
        * (
            jnp.roll(above_z, -1, 2)
            - jnp.roll(above_z, 1, 2)
            - jnp.roll(below_z, -1, 2)
            + jnp.roll(below_z, 1, 2)
        )
    )
    curve_yx = (
        hessian_scale
        * 0.25
        * (
            jnp.roll(above_y, -1, 2)
            - jnp.roll(above_y, 1, 2)
            - jnp.roll(below_y, -1, 2)
            + jnp.roll(below_y, 1, 2)
        )
    )
    return invariants(curve_zz, curve_yy, curve_xx, curve_zy, curve_zx, curve_yx)


def per_device(density, dilations, owner_rank, owner_slot, base_cell, corner_weights):
    slab_depth = density.shape[0]
    band_rows = density.shape[1]
    row_length = density.shape[2]
    banded = with_halo(density, (("gy", 1),), HALO)
    response = None
    features = []
    for level_index in range(SCALES):
        dilation = dilations[level_index]
        along_y = smooth_padded(banded, dilation, 1, band_rows)
        low, high = z_neighbours(along_y, HALO)
        run = level_kernel(level_index, level_index == 0, slab_depth, band_rows, row_length)
        feature, response = run(dilations, low, along_y, high, response)
        features.append(feature.reshape(slab_depth * band_rows, row_length))
    plane = (band_rows - 1) * row_length
    z_index = base_cell // plane
    remainder = base_cell % plane
    y_index = remainder // row_length
    x_index = remainder % row_length
    entries = base_cell.shape[0]
    target_x = jnp.concatenate([x_index, (x_index + 1) % row_length])
    pick_x = (
        jnp.arange(row_length, dtype=jnp.int32)[:, None] == target_x[None, :]
    ).astype(jnp.float32)
    cells = jnp.arange(slab_depth * band_rows, dtype=jnp.int32)[:, None]
    weight_grid = None
    for step_z in (0, 1):
        for step_y in (0, 1):
            row = (z_index + step_z) * band_rows + y_index + step_y
            corner = 4 * step_z + 2 * step_y
            weights = jnp.concatenate([corner_weights[corner], corner_weights[corner + 1]])
            term = jnp.where(cells == jnp.concatenate([row, row])[None, :], weights[None, :], 0.0)
            weight_grid = term if weight_grid is None else weight_grid + term
    partials = []
    for feature in features:
        picked = jnp.dot(
            feature, pick_x, precision=lax.Precision.HIGHEST, preferred_element_type=jnp.float32
        )
        per_column = jnp.sum(picked * weight_grid, axis=0)
        partials.append(per_column[:entries] + per_column[entries:])
    partial_value = jnp.stack(partials)
    owner_group = owner_rank[:, 0]
    groups = lax.axis_size("gy")
    column = owner_group * HOWN + owner_slot
    onehot = (column[:, None] == jnp.arange(groups * HOWN, dtype=jnp.int32)[None, :]).astype(
        jnp.float32
    )
    spread = jnp.dot(
        partial_value, onehot, precision=lax.Precision.HIGHEST, preferred_element_type=jnp.float32
    )
    exchanged = lax.all_to_all(
        spread.reshape(SCALES, groups, HOWN), "gy", split_axis=1, concat_axis=1, tiled=True
    )
    catalogue = jnp.sum(exchanged, axis=1)
    return (response, catalogue)


def solution(mesh):
    placed = (
        P("gz", "gy", None),
        P(),
        P(("gz", "gy"), None),
        P(("gz", "gy")),
        P(("gz", "gy")),
        P(None, ("gz", "gy")),
    )
    return jax.shard_map(
        per_device,
        mesh=mesh,
        in_specs=placed,
        out_specs=(P("gz", "gy", None), P(None, ("gz", "gy"))),
        check_vma=False,
    )
```

```python
import jax
import jax.numpy as jnp
from jax import lax
from jax.experimental import pallas as pl
from jax.experimental.pallas import tpu as pltpu
from jax.sharding import PartitionSpec as P

SCALES = 3
HALO = 9
HOWN = 256
DMAX = 4


tap_weights = (0.0625, 0.25, 0.375, 0.25, 0.0625)
hessian_scale = 4.0


def flat_ppermute(part, axis, pairs):
    rows = part.shape[0] * part.shape[1]
    moved = lax.ppermute(part.reshape(rows, part.shape[2]), axis, pairs)
    return moved.reshape(part.shape)


def with_halo(block, sides, width):
    for axis, dim in sides:
        count = lax.axis_size(axis)
        forward = [(i, i + 1) for i in range(count - 1)]
        forward.append((count - 1, 0))
        backward = [(target, source) for source, target in forward]
        low = flat_ppermute(
            lax.slice_in_dim(block, block.shape[dim] - width, None, axis=dim), axis, forward
        )
        high = flat_ppermute(lax.slice_in_dim(block, 0, width, axis=dim), axis, backward)
        block = jnp.concatenate([low, block, high], axis=dim)
    return block


def smooth_padded(field_data, dilation, along_dim, extent):
    running = None
    for offset in range(5):
        start_at = HALO - 1 + (offset - 2) * dilation
        summand = tap_weights[offset] * lax.dynamic_slice_in_dim(
            field_data, start_at, extent + 2, along_dim
        )
        running = summand if running is None else running + summand
    return running


def smooth_periodic(field_data, dilation):
    running = None
    for offset in range(5):
        summand = tap_weights[offset] * jnp.roll(field_data, -(offset - 2) * dilation, axis=2)
        running = summand if running is None else running + summand
    return running


def level_kernel(level_index, first, slab_depth, band_rows, row_length):
    planes = slab_depth + 2

    def compute(dilation, a_scr, s_scr, feature_ref, prev_ref, best_ref, row_wait, prev_copy,
                out_copy, edges_in):
        reach = HALO - 1 + 2 * dilation
        last_mid = HALO + slab_depth - 1
        edges_in()
        for row in range(HALO, min(reach, last_mid + 1)):
            row_wait(row)

        def smooth_plane(plane, carry):
            @pl.when(reach + plane <= last_mid)
            def _():
                row_wait(reach + plane)

            for first_row in range(0, band_rows + 2, 8):
                rows = min(8, band_rows + 2 - first_row)
                along_z = None
                for offset in range(5):
                    source = HALO - 1 + plane + (offset - 2) * dilation
                    summand = tap_weights[offset] * a_scr[source, pl.ds(first_row, rows), :]
                    along_z = summand if along_z is None else along_z + summand
                running = None
                for offset in range(5):
                    shift = (-(offset - 2) * dilation) % row_length
                    moved = along_z if shift == 0 else pltpu.roll(along_z, shift, 1)
                    summand = tap_weights[offset] * moved
                    running = summand if running is None else running + summand
                s_scr[plane, pl.ds(first_row, rows), :] = running
            return carry

        lax.fori_loop(0, planes, smooth_plane, 0)
        for row in range(max(reach + planes, HALO), last_mid + 1):
            row_wait(row)
        if prev_copy is not None:
            prev_copy.wait()

        def feature_plane(z, carry):
            for half in range(band_rows // 8):
                y0 = half * 8

                def at(dz, dy):
                    return s_scr[z + 1 + dz, pl.ds(1 + y0 + dy, 8), :]

                def left(v):
                    return pltpu.roll(v, row_length - 1, 1)

                def right(v):
                    return pltpu.roll(v, 1, 1)

                centre = at(0, 0)
                above_z = at(1, 0)
                below_z = at(-1, 0)
                curve_zz = hessian_scale * (above_z - 2.0 * centre + below_z)
                across_z = above_z - below_z
                curve_zx = (hessian_scale * 0.25) * (left(across_z) - right(across_z))
                above_y = at(0, 1)
                below_y = at(0, -1)
                curve_yy = hessian_scale * (above_y - 2.0 * centre + below_y)
                across_y = above_y - below_y
                curve_yx = (hessian_scale * 0.25) * (left(across_y) - right(across_y))
                curve_xx = hessian_scale * (left(centre) - 2.0 * centre + right(centre))
                trace_sum = curve_xx + curve_yy + curve_zz
                minor_sum = curve_xx * curve_yy + curve_xx * curve_zz + curve_yy * curve_zz
                minor_sum = minor_sum - curve_zx * curve_zx - curve_yx * curve_yx
                curve_zy = (hessian_scale * 0.25) * (at(1, 1) - at(1, -1) - at(-1, 1) + at(-1, -1))
                minor_sum = minor_sum - curve_zy * curve_zy
                value = (trace_sum * trace_sum / 3.0 - minor_sum) * (1.0 / (1.0 + jnp.exp(trace_sum)))
                feature_ref[z, pl.ds(y0, 8), :] = value
                if first:
                    best_ref[z, pl.ds(y0, 8), :] = value
                else:
                    best_ref[z, pl.ds(y0, 8), :] = jnp.maximum(prev_ref[z, pl.ds(y0, 8), :], value)
            for copy in out_copy(z):
                copy.start()
            return carry

        lax.fori_loop(0, slab_depth, feature_plane, 0)
        for z in range(slab_depth):
            for copy in out_copy(z):
                copy.wait()

    def kernel(*refs):
        if first:
            (dil_ref, lo_hbm, mid_hbm, hi_hbm, feature_hbm, best_hbm,
             a_scr, s_scr, f_scr, b_scr, p_scr, lo_scr, hi_scr, row_sems, out_sems, prev_sem,
             edge_sems) = refs
        else:
            (dil_ref, lo_hbm, mid_hbm, hi_hbm, prev_hbm, feature_hbm, best_hbm,
             a_scr, s_scr, f_scr, b_scr, p_scr, lo_scr, hi_scr, row_sems, out_sems, prev_sem,
             edge_sems) = refs
        edge_copies = [
            pltpu.make_async_copy(lo_hbm, lo_scr, edge_sems.at[0]),
            pltpu.make_async_copy(hi_hbm, hi_scr, edge_sems.at[1]),
        ]
        for copy in edge_copies:
            copy.start()
        for index in range(slab_depth):
            row = HALO + index
            pltpu.make_async_copy(mid_hbm.at[index], a_scr.at[row], row_sems.at[row]).start()
        prev_copy = None
        if not first:
            prev_copy = pltpu.make_async_copy(prev_hbm, p_scr, prev_sem.at[0])
            prev_copy.start()

        def row_wait(row):
            pltpu.make_async_copy(mid_hbm.at[0], a_scr.at[row], row_sems.at[row]).wait()

        width = band_rows + 2

        def edges_in():
            for copy, flat, first_row in zip(edge_copies, (lo_scr, hi_scr), (0, HALO + slab_depth)):
                copy.wait()
                for index in range(HALO):
                    a_scr[first_row + index] = flat[pl.ds(index * width, width), :]

        def out_copy(z):
            return [
                pltpu.make_async_copy(f_scr.at[z], feature_hbm.at[z], out_sems.at[0, z]),
                pltpu.make_async_copy(b_scr.at[z], best_hbm.at[z], out_sems.at[1, z]),
            ]

        def branch(value):
            def run_branch():
                compute(value, a_scr, s_scr, f_scr, None if first else p_scr, b_scr,
                        row_wait, prev_copy, out_copy, edges_in)
            return run_branch

        pick = jnp.clip(dil_ref[level_index], 1, DMAX) - 1
        lax.switch(pick, [branch(value) for value in range(1, DMAX + 1)])

    def run(dilations, low, middle, high, prev):
        block = jax.ShapeDtypeStruct((slab_depth, band_rows, row_length), jnp.float32)
        anywhere = pl.BlockSpec(memory_space=pl.ANY)
        in_specs = [pl.BlockSpec(memory_space=pltpu.SMEM), anywhere, anywhere, anywhere]
        operands = [dilations, low, middle, high]
        if not first:
            in_specs.append(anywhere)
            operands.append(prev)
        total_rows = planes + 2 * HALO - 2
        return pl.pallas_call(
            kernel,
            out_shape=(block, block),
            in_specs=in_specs,
            out_specs=(anywhere, anywhere),
            scratch_shapes=[
                pltpu.VMEM((total_rows, band_rows + 2, row_length), jnp.float32),
                pltpu.VMEM((planes, band_rows + 2, row_length), jnp.float32),
                pltpu.VMEM((slab_depth, band_rows, row_length), jnp.float32),
                pltpu.VMEM((slab_depth, band_rows, row_length), jnp.float32),
                pltpu.VMEM((slab_depth, band_rows, row_length), jnp.float32),
                pltpu.VMEM((HALO * (band_rows + 2), row_length), jnp.float32),
                pltpu.VMEM((HALO * (band_rows + 2), row_length), jnp.float32),
                pltpu.SemaphoreType.DMA((total_rows,)),
                pltpu.SemaphoreType.DMA((2, slab_depth)),
                pltpu.SemaphoreType.DMA((1,)),
                pltpu.SemaphoreType.DMA((2,)),
            ],
            compiler_params=pltpu.CompilerParams(vmem_limit_bytes=56 * 1024 * 1024),
        )(*operands)

    return run


def z_neighbours(block, width):
    count = lax.axis_size("gz")
    forward = [(i, i + 1) for i in range(count - 1)]
    forward.append((count - 1, 0))
    backward = [(target, source) for source, target in forward]
    def flat(part):
        return part.reshape(part.shape[0] * part.shape[1], part.shape[2])

    low = lax.ppermute(flat(lax.slice_in_dim(block, block.shape[0] - width, None, axis=0)), "gz", forward)
    high = lax.ppermute(flat(lax.slice_in_dim(block, 0, width, axis=0)), "gz", backward)
    return low, high


def invariants(curve_zz, curve_yy, curve_xx, curve_zy, curve_zx, curve_yx):
    trace_sum = curve_xx + curve_yy + curve_zz
    minor_sum = (
        curve_xx * curve_yy
        + curve_xx * curve_zz
        + curve_yy * curve_zz
        - curve_zy * curve_zy
        - curve_zx * curve_zx
        - curve_yx * curve_yx
    )
    return (trace_sum * trace_sum / 3.0 - minor_sum) * jax.nn.sigmoid(-trace_sum)


def signature(smoothed):
    centre = smoothed[1:-1, 1:-1]
    above_z = smoothed[2:, 1:-1]
    below_z = smoothed[:-2, 1:-1]
    above_y = smoothed[1:-1, 2:]
    below_y = smoothed[1:-1, :-2]
    curve_zz = hessian_scale * (above_z - 2.0 * centre + below_z)
    curve_yy = hessian_scale * (above_y - 2.0 * centre + below_y)
    curve_xx = hessian_scale * (jnp.roll(centre, -1, 2) - 2.0 * centre + jnp.roll(centre, 1, 2))
    curve_zy = (
        hessian_scale
        * 0.25
        * (smoothed[2:, 2:] - smoothed[2:, :-2] - smoothed[:-2, 2:] + smoothed[:-2, :-2])
    )
    curve_zx = (
        hessian_scale
        * 0.25
        * (
            jnp.roll(above_z, -1, 2)
            - jnp.roll(above_z, 1, 2)
            - jnp.roll(below_z, -1, 2)
            + jnp.roll(below_z, 1, 2)
        )
    )
    curve_yx = (
        hessian_scale
        * 0.25
        * (
            jnp.roll(above_y, -1, 2)
            - jnp.roll(above_y, 1, 2)
            - jnp.roll(below_y, -1, 2)
            + jnp.roll(below_y, 1, 2)
        )
    )
    return invariants(curve_zz, curve_yy, curve_xx, curve_zy, curve_zx, curve_yx)


def per_device(density, dilations, owner_rank, owner_slot, base_cell, corner_weights):
    slab_depth = density.shape[0]
    band_rows = density.shape[1]
    row_length = density.shape[2]
    banded = with_halo(density, (("gy", 1),), HALO)
    response = None
    features = []
    for level_index in range(SCALES):
        dilation = dilations[level_index]
        along_y = smooth_padded(banded, dilation, 1, band_rows)
        low, high = z_neighbours(along_y, HALO)
        run = level_kernel(level_index, level_index == 0, slab_depth, band_rows, row_length)
        feature, response = run(dilations, low, along_y, high, response)
        features.append(feature.reshape(slab_depth * band_rows, row_length))
    plane = (band_rows - 1) * row_length
    z_index = base_cell // plane
    remainder = base_cell % plane
    y_index = remainder // row_length
    x_index = remainder % row_length
    entries = base_cell.shape[0]
    target_x = jnp.concatenate([x_index, (x_index + 1) % row_length])
    pick_x = (
        jnp.arange(row_length, dtype=jnp.int32)[:, None] == target_x[None, :]
    ).astype(jnp.float32)
    cells = jnp.arange(slab_depth * band_rows, dtype=jnp.int32)[:, None]
    weight_grid = None
    for step_z in (0, 1):
        for step_y in (0, 1):
            row = (z_index + step_z) * band_rows + y_index + step_y
            corner = 4 * step_z + 2 * step_y
            weights = jnp.concatenate([corner_weights[corner], corner_weights[corner + 1]])
            term = jnp.where(cells == jnp.concatenate([row, row])[None, :], weights[None, :], 0.0)
            weight_grid = term if weight_grid is None else weight_grid + term
    partials = []
    for feature in features:
        picked = jnp.dot(
            feature, pick_x, precision=lax.Precision.HIGH, preferred_element_type=jnp.float32
        )
        per_column = jnp.sum(picked * weight_grid, axis=0)
        partials.append(per_column[:entries] + per_column[entries:])
    partial_value = jnp.stack(partials)
    owner_group = owner_rank[:, 0]
    groups = lax.axis_size("gy")
    column = owner_group * HOWN + owner_slot
    onehot = (column[:, None] == jnp.arange(groups * HOWN, dtype=jnp.int32)[None, :]).astype(
        jnp.float32
    )
    spread = jnp.dot(
        partial_value, onehot, precision=lax.Precision.HIGH, preferred_element_type=jnp.float32
    )
    exchanged = lax.all_to_all(
        spread.reshape(SCALES, groups, HOWN), "gy", split_axis=1, concat_axis=1, tiled=True
    )
    catalogue = jnp.sum(exchanged, axis=1)
    return (response, catalogue)


def solution(mesh):
    placed = (
        P("gz", "gy", None),
        P(),
        P(("gz", "gy"), None),
        P(("gz", "gy")),
        P(("gz", "gy")),
        P(None, ("gz", "gy")),
    )
    return jax.shard_map(
        per_device,
        mesh=mesh,
        in_specs=placed,
        out_specs=(P("gz", "gy", None), P(None, ("gz", "gy"))),
        check_vma=False,
    )
```

```python
import jax
import jax.numpy as jnp
from jax import lax
from jax.experimental import pallas as pl
from jax.experimental.pallas import tpu as pltpu
from jax.sharding import PartitionSpec as P

SCALES = 3
HALO = 9
HOWN = 256
DMAX = 4


tap_weights = (0.0625, 0.25, 0.375, 0.25, 0.0625)
hessian_scale = 4.0


def flat_ppermute(part, axis, pairs):
    rows = part.shape[0] * part.shape[1]
    moved = lax.ppermute(part.reshape(rows, part.shape[2]), axis, pairs)
    return moved.reshape(part.shape)


def with_halo(block, sides, width):
    for axis, dim in sides:
        count = lax.axis_size(axis)
        forward = [(i, i + 1) for i in range(count - 1)]
        forward.append((count - 1, 0))
        backward = [(target, source) for source, target in forward]
        low = flat_ppermute(
            lax.slice_in_dim(block, block.shape[dim] - width, None, axis=dim), axis, forward
        )
        high = flat_ppermute(lax.slice_in_dim(block, 0, width, axis=dim), axis, backward)
        block = jnp.concatenate([low, block, high], axis=dim)
    return block


def smooth_padded(field_data, dilation, along_dim, extent):
    running = None
    for offset in range(5):
        start_at = HALO - 1 + (offset - 2) * dilation
        summand = tap_weights[offset] * lax.dynamic_slice_in_dim(
            field_data, start_at, extent + 2, along_dim
        )
        running = summand if running is None else running + summand
    return running


def smooth_periodic(field_data, dilation):
    running = None
    for offset in range(5):
        summand = tap_weights[offset] * jnp.roll(field_data, -(offset - 2) * dilation, axis=2)
        running = summand if running is None else running + summand
    return running


def level_kernel(level_index, first, slab_depth, band_rows, row_length):
    planes = slab_depth + 2

    def compute(dilation, a_scr, s_scr, feature_ref, prev_ref, best_ref, row_wait, prev_copy,
                out_copy, edges_in):
        reach = HALO - 1 + 2 * dilation
        last_mid = HALO + slab_depth - 1
        edges_in()
        for row in range(HALO, min(reach, last_mid + 1)):
            row_wait(row)

        def smooth_plane(plane, carry):
            @pl.when(reach + plane <= last_mid)
            def _():
                row_wait(reach + plane)

            for first_row in range(0, band_rows + 2, 8):
                rows = min(8, band_rows + 2 - first_row)
                along_z = None
                for offset in range(5):
                    source = HALO - 1 + plane + (offset - 2) * dilation
                    summand = tap_weights[offset] * a_scr[source, pl.ds(first_row, rows), :]
                    along_z = summand if along_z is None else along_z + summand
                running = None
                for offset in range(5):
                    shift = (-(offset - 2) * dilation) % row_length
                    moved = along_z if shift == 0 else pltpu.roll(along_z, shift, 1)
                    summand = tap_weights[offset] * moved
                    running = summand if running is None else running + summand
                s_scr[plane, pl.ds(first_row, rows), :] = running
            return carry

        lax.fori_loop(0, planes, smooth_plane, 0)
        for row in range(max(reach + planes, HALO), last_mid + 1):
            row_wait(row)
        if prev_copy is not None:
            prev_copy.wait()

        def feature_plane(z, carry):
            for half in range(band_rows // 8):
                y0 = half * 8

                def at(dz, dy):
                    return s_scr[z + 1 + dz, pl.ds(1 + y0 + dy, 8), :]

                def left(v):
                    return pltpu.roll(v, row_length - 1, 1)

                def right(v):
                    return pltpu.roll(v, 1, 1)

                centre = at(0, 0)
                above_z = at(1, 0)
                below_z = at(-1, 0)
                curve_zz = hessian_scale * (above_z - 2.0 * centre + below_z)
                across_z = above_z - below_z
                curve_zx = (hessian_scale * 0.25) * (left(across_z) - right(across_z))
                above_y = at(0, 1)
                below_y = at(0, -1)
                curve_yy = hessian_scale * (above_y - 2.0 * centre + below_y)
                across_y = above_y - below_y
                curve_yx = (hessian_scale * 0.25) * (left(across_y) - right(across_y))
                curve_xx = hessian_scale * (left(centre) - 2.0 * centre + right(centre))
                trace_sum = curve_xx + curve_yy + curve_zz
                minor_sum = curve_xx * curve_yy + curve_xx * curve_zz + curve_yy * curve_zz
                minor_sum = minor_sum - curve_zx * curve_zx - curve_yx * curve_yx
                curve_zy = (hessian_scale * 0.25) * (at(1, 1) - at(1, -1) - at(-1, 1) + at(-1, -1))
                minor_sum = minor_sum - curve_zy * curve_zy
                value = (trace_sum * trace_sum / 3.0 - minor_sum) * (1.0 / (1.0 + jnp.exp(trace_sum)))
                feature_ref[z, pl.ds(y0, 8), :] = value
                if first:
                    best_ref[z, pl.ds(y0, 8), :] = value
                else:
                    best_ref[z, pl.ds(y0, 8), :] = jnp.maximum(prev_ref[z, pl.ds(y0, 8), :], value)
            for copy in out_copy(z):
                copy.start()
            return carry

        lax.fori_loop(0, slab_depth, feature_plane, 0)
        for z in range(slab_depth):
            for copy in out_copy(z):
                copy.wait()

    def kernel(*refs):
        if first:
            (dil_ref, lo_hbm, mid_hbm, hi_hbm, feature_hbm, best_hbm,
             a_scr, s_scr, f_scr, b_scr, p_scr, lo_scr, hi_scr, row_sems, out_sems, prev_sem,
             edge_sems) = refs
        else:
            (dil_ref, lo_hbm, mid_hbm, hi_hbm, prev_hbm, feature_hbm, best_hbm,
             a_scr, s_scr, f_scr, b_scr, p_scr, lo_scr, hi_scr, row_sems, out_sems, prev_sem,
             edge_sems) = refs
        edge_copies = [
            pltpu.make_async_copy(lo_hbm, lo_scr, edge_sems.at[0]),
            pltpu.make_async_copy(hi_hbm, hi_scr, edge_sems.at[1]),
        ]
        for copy in edge_copies:
            copy.start()
        for index in range(slab_depth):
            row = HALO + index
            pltpu.make_async_copy(mid_hbm.at[index], a_scr.at[row], row_sems.at[row]).start()
        prev_copy = None
        if not first:
            prev_copy = pltpu.make_async_copy(prev_hbm, p_scr, prev_sem.at[0])
            prev_copy.start()

        def row_wait(row):
            pltpu.make_async_copy(mid_hbm.at[0], a_scr.at[row], row_sems.at[row]).wait()

        width = band_rows + 2

        def edges_in():
            for copy, flat, first_row in zip(edge_copies, (lo_scr, hi_scr), (0, HALO + slab_depth)):
                copy.wait()
                for index in range(HALO):
                    a_scr[first_row + index] = flat[pl.ds(index * width, width), :]

        def out_copy(z):
            return [
                pltpu.make_async_copy(f_scr.at[z], feature_hbm.at[z], out_sems.at[0, z]),
                pltpu.make_async_copy(b_scr.at[z], best_hbm.at[z], out_sems.at[1, z]),
            ]

        def branch(value):
            def run_branch():
                compute(value, a_scr, s_scr, f_scr, None if first else p_scr, b_scr,
                        row_wait, prev_copy, out_copy, edges_in)
            return run_branch

        pick = jnp.clip(dil_ref[level_index], 1, DMAX) - 1
        lax.switch(pick, [branch(value) for value in range(1, DMAX + 1)])

    def run(dilations, low, middle, high, prev):
        block = jax.ShapeDtypeStruct((slab_depth, band_rows, row_length), jnp.float32)
        anywhere = pl.BlockSpec(memory_space=pl.ANY)
        in_specs = [pl.BlockSpec(memory_space=pltpu.SMEM), anywhere, anywhere, anywhere]
        operands = [dilations, low, middle, high]
        if not first:
            in_specs.append(anywhere)
            operands.append(prev)
        total_rows = planes + 2 * HALO - 2
        return pl.pallas_call(
            kernel,
            out_shape=(block, block),
            in_specs=in_specs,
            out_specs=(anywhere, anywhere),
            scratch_shapes=[
                pltpu.VMEM((total_rows, band_rows + 2, row_length), jnp.float32),
                pltpu.VMEM((planes, band_rows + 2, row_length), jnp.float32),
                pltpu.VMEM((slab_depth, band_rows, row_length), jnp.float32),
                pltpu.VMEM((slab_depth, band_rows, row_length), jnp.float32),
                pltpu.VMEM((slab_depth, band_rows, row_length), jnp.float32),
                pltpu.VMEM((HALO * (band_rows + 2), row_length), jnp.float32),
                pltpu.VMEM((HALO * (band_rows + 2), row_length), jnp.float32),
                pltpu.SemaphoreType.DMA((total_rows,)),
                pltpu.SemaphoreType.DMA((2, slab_depth)),
                pltpu.SemaphoreType.DMA((1,)),
                pltpu.SemaphoreType.DMA((2,)),
            ],
            compiler_params=pltpu.CompilerParams(vmem_limit_bytes=56 * 1024 * 1024),
        )(*operands)

    return run


def z_neighbours(block, width):
    count = lax.axis_size("gz")
    forward = [(i, i + 1) for i in range(count - 1)]
    forward.append((count - 1, 0))
    backward = [(target, source) for source, target in forward]
    def flat(part):
        return part.reshape(part.shape[0] * part.shape[1], part.shape[2])

    low = lax.ppermute(flat(lax.slice_in_dim(block, block.shape[0] - width, None, axis=0)), "gz", forward)
    high = lax.ppermute(flat(lax.slice_in_dim(block, 0, width, axis=0)), "gz", backward)
    return low, high


def invariants(curve_zz, curve_yy, curve_xx, curve_zy, curve_zx, curve_yx):
    trace_sum = curve_xx + curve_yy + curve_zz
    minor_sum = (
        curve_xx * curve_yy
        + curve_xx * curve_zz
        + curve_yy * curve_zz
        - curve_zy * curve_zy
        - curve_zx * curve_zx
        - curve_yx * curve_yx
    )
    return (trace_sum * trace_sum / 3.0 - minor_sum) * jax.nn.sigmoid(-trace_sum)


def signature(smoothed):
    centre = smoothed[1:-1, 1:-1]
    above_z = smoothed[2:, 1:-1]
    below_z = smoothed[:-2, 1:-1]
    above_y = smoothed[1:-1, 2:]
    below_y = smoothed[1:-1, :-2]
    curve_zz = hessian_scale * (above_z - 2.0 * centre + below_z)
    curve_yy = hessian_scale * (above_y - 2.0 * centre + below_y)
    curve_xx = hessian_scale * (jnp.roll(centre, -1, 2) - 2.0 * centre + jnp.roll(centre, 1, 2))
    curve_zy = (
        hessian_scale
        * 0.25
        * (smoothed[2:, 2:] - smoothed[2:, :-2] - smoothed[:-2, 2:] + smoothed[:-2, :-2])
    )
    curve_zx = (
        hessian_scale
        * 0.25
        * (
            jnp.roll(above_z, -1, 2)
            - jnp.roll(above_z, 1, 2)
            - jnp.roll(below_z, -1, 2)
            + jnp.roll(below_z, 1, 2)
        )
    )
    curve_yx = (
        hessian_scale
        * 0.25
        * (
            jnp.roll(above_y, -1, 2)
            - jnp.roll(above_y, 1, 2)
            - jnp.roll(below_y, -1, 2)
            + jnp.roll(below_y, 1, 2)
        )
    )
    return invariants(curve_zz, curve_yy, curve_xx, curve_zy, curve_zx, curve_yx)


def per_device(density, dilations, owner_rank, owner_slot, base_cell, corner_weights):
    slab_depth = density.shape[0]
    band_rows = density.shape[1]
    row_length = density.shape[2]
    banded = with_halo(density, (("gy", 1),), HALO)
    plane = (band_rows - 1) * row_length
    z_index = base_cell // plane
    remainder = base_cell % plane
    y_index = remainder // row_length
    x_index = remainder % row_length
    entries = base_cell.shape[0]
    target_x = jnp.concatenate([x_index, (x_index + 1) % row_length])
    pick_x = (
        jnp.arange(row_length, dtype=jnp.int32)[:, None] == target_x[None, :]
    ).astype(jnp.float32)
    cells = jnp.arange(slab_depth * band_rows, dtype=jnp.int32)[:, None]
    weight_grid = None
    for step_z in (0, 1):
        for step_y in (0, 1):
            row = (z_index + step_z) * band_rows + y_index + step_y
            corner = 4 * step_z + 2 * step_y
            weights = jnp.concatenate([corner_weights[corner], corner_weights[corner + 1]])
            term = jnp.where(cells == jnp.concatenate([row, row])[None, :], weights[None, :], 0.0)
            weight_grid = term if weight_grid is None else weight_grid + term
    partials = []

    def partial_of(feature):
        picked = jnp.dot(
            feature, pick_x, precision=lax.Precision.HIGH, preferred_element_type=jnp.float32
        )
        per_column = jnp.sum(picked * weight_grid, axis=0)
        return per_column[:entries] + per_column[entries:]

    response = None
    for level_index in range(SCALES):
        dilation = dilations[level_index]
        along_y = smooth_padded(banded, dilation, 1, band_rows)
        low, high = z_neighbours(along_y, HALO)
        if partials:
            low, high, partials[-1] = lax.optimization_barrier((low, high, partials[-1]))
        run = level_kernel(level_index, level_index == 0, slab_depth, band_rows, row_length)
        feature, response = run(dilations, low, along_y, high, response)
        partials.append(partial_of(feature.reshape(slab_depth * band_rows, row_length)))
    partial_value = jnp.stack(partials)
    owner_group = owner_rank[:, 0]
    groups = lax.axis_size("gy")
    column = owner_group * HOWN + owner_slot
    onehot = (column[:, None] == jnp.arange(groups * HOWN, dtype=jnp.int32)[None, :]).astype(
        jnp.float32
    )
    spread = jnp.dot(
        partial_value, onehot, precision=lax.Precision.HIGH, preferred_element_type=jnp.float32
    )
    exchanged = lax.all_to_all(
        spread.reshape(SCALES, groups, HOWN), "gy", split_axis=1, concat_axis=1, tiled=True
    )
    catalogue = jnp.sum(exchanged, axis=1)
    return (response, catalogue)


def solution(mesh):
    placed = (
        P("gz", "gy", None),
        P(),
        P(("gz", "gy"), None),
        P(("gz", "gy")),
        P(("gz", "gy")),
        P(None, ("gz", "gy")),
    )
    return jax.shard_map(
        per_device,
        mesh=mesh,
        in_specs=placed,
        out_specs=(P("gz", "gy", None), P(None, ("gz", "gy"))),
        check_vma=False,
    )
```

```python
import jax
import jax.numpy as jnp
from jax import lax
from jax.experimental import pallas as pl
from jax.experimental.pallas import tpu as pltpu
from jax.sharding import PartitionSpec as P

SCALES = 3
HALO = 9
HOWN = 256
DMAX = 4


tap_weights = (0.0625, 0.25, 0.375, 0.25, 0.0625)
hessian_scale = 4.0


def flat_ppermute(part, axis, pairs):
    rows = part.shape[0] * part.shape[1]
    moved = lax.ppermute(part.reshape(rows, part.shape[2]), axis, pairs)
    return moved.reshape(part.shape)


def with_halo(block, sides, width):
    for axis, dim in sides:
        count = lax.axis_size(axis)
        forward = [(i, i + 1) for i in range(count - 1)]
        forward.append((count - 1, 0))
        backward = [(target, source) for source, target in forward]
        low = flat_ppermute(
            lax.slice_in_dim(block, block.shape[dim] - width, None, axis=dim), axis, forward
        )
        high = flat_ppermute(lax.slice_in_dim(block, 0, width, axis=dim), axis, backward)
        block = jnp.concatenate([low, block, high], axis=dim)
    return block


def smooth_padded(field_data, dilation, along_dim, extent):
    running = None
    for offset in range(5):
        start_at = HALO - 1 + (offset - 2) * dilation
        summand = tap_weights[offset] * lax.dynamic_slice_in_dim(
            field_data, start_at, extent + 2, along_dim
        )
        running = summand if running is None else running + summand
    return running


def smooth_periodic(field_data, dilation):
    running = None
    for offset in range(5):
        summand = tap_weights[offset] * jnp.roll(field_data, -(offset - 2) * dilation, axis=2)
        running = summand if running is None else running + summand
    return running


def level_kernel(level_index, first, slab_depth, band_rows, row_length):
    planes = slab_depth + 2

    def compute(dilation, a_scr, s_scr, feature_ref, prev_ref, best_ref, row_wait, prev_copy,
                out_copy, edges_in):
        reach = HALO - 1 + 2 * dilation
        last_mid = HALO + slab_depth - 1
        edges_in()
        for row in range(HALO, min(reach, last_mid + 1)):
            row_wait(row)

        def smooth_plane(plane, carry):
            @pl.when(reach + plane <= last_mid)
            def _():
                row_wait(reach + plane)

            for first_row in range(0, band_rows + 2, 8):
                rows = min(8, band_rows + 2 - first_row)
                along_z = None
                for offset in range(5):
                    source = HALO - 1 + plane + (offset - 2) * dilation
                    summand = tap_weights[offset] * a_scr[source, pl.ds(first_row, rows), :]
                    along_z = summand if along_z is None else along_z + summand
                running = None
                for offset in range(5):
                    shift = (-(offset - 2) * dilation) % row_length
                    moved = along_z if shift == 0 else pltpu.roll(along_z, shift, 1)
                    summand = tap_weights[offset] * moved
                    running = summand if running is None else running + summand
                s_scr[plane, pl.ds(first_row, rows), :] = running
            return carry

        lax.fori_loop(0, planes, smooth_plane, 0)
        for row in range(max(reach + planes, HALO), last_mid + 1):
            row_wait(row)
        if prev_copy is not None:
            prev_copy.wait()

        def feature_plane(z, carry):
            for half in range(band_rows // 8):
                y0 = half * 8

                def at(dz, dy):
                    return s_scr[z + 1 + dz, pl.ds(1 + y0 + dy, 8), :]

                def left(v):
                    return pltpu.roll(v, row_length - 1, 1)

                def right(v):
                    return pltpu.roll(v, 1, 1)

                centre = at(0, 0)
                above_z = at(1, 0)
                below_z = at(-1, 0)
                curve_zz = hessian_scale * (above_z - 2.0 * centre + below_z)
                across_z = above_z - below_z
                curve_zx = (hessian_scale * 0.25) * (left(across_z) - right(across_z))
                above_y = at(0, 1)
                below_y = at(0, -1)
                curve_yy = hessian_scale * (above_y - 2.0 * centre + below_y)
                across_y = above_y - below_y
                curve_yx = (hessian_scale * 0.25) * (left(across_y) - right(across_y))
                curve_xx = hessian_scale * (left(centre) - 2.0 * centre + right(centre))
                trace_sum = curve_xx + curve_yy + curve_zz
                minor_sum = curve_xx * curve_yy + curve_xx * curve_zz + curve_yy * curve_zz
                minor_sum = minor_sum - curve_zx * curve_zx - curve_yx * curve_yx
                curve_zy = (hessian_scale * 0.25) * (at(1, 1) - at(1, -1) - at(-1, 1) + at(-1, -1))
                minor_sum = minor_sum - curve_zy * curve_zy
                value = (trace_sum * trace_sum / 3.0 - minor_sum) * (1.0 / (1.0 + jnp.exp(trace_sum)))
                feature_ref[z, pl.ds(y0, 8), :] = value
                if first:
                    best_ref[z, pl.ds(y0, 8), :] = value
                else:
                    best_ref[z, pl.ds(y0, 8), :] = jnp.maximum(prev_ref[z, pl.ds(y0, 8), :], value)
            for copy in out_copy(z):
                copy.start()
            return carry

        lax.fori_loop(0, slab_depth, feature_plane, 0)
        for z in range(slab_depth):
            for copy in out_copy(z):
                copy.wait()

    def kernel(*refs):
        if first:
            (dil_ref, lo_hbm, mid_hbm, hi_hbm, feature_hbm, best_hbm,
             a_scr, s_scr, f_scr, b_scr, p_scr, lo_scr, hi_scr, row_sems, out_sems, prev_sem,
             edge_sems) = refs
        else:
            (dil_ref, lo_hbm, mid_hbm, hi_hbm, prev_hbm, feature_hbm, best_hbm,
             a_scr, s_scr, f_scr, b_scr, p_scr, lo_scr, hi_scr, row_sems, out_sems, prev_sem,
             edge_sems) = refs
        edge_copies = [
            pltpu.make_async_copy(lo_hbm, lo_scr, edge_sems.at[0]),
            pltpu.make_async_copy(hi_hbm, hi_scr, edge_sems.at[1]),
        ]
        for copy in edge_copies:
            copy.start()
        for index in range(slab_depth):
            row = HALO + index
            pltpu.make_async_copy(mid_hbm.at[index], a_scr.at[row], row_sems.at[row]).start()
        prev_copy = None
        if not first:
            prev_copy = pltpu.make_async_copy(prev_hbm, p_scr, prev_sem.at[0])
            prev_copy.start()

        def row_wait(row):
            pltpu.make_async_copy(mid_hbm.at[0], a_scr.at[row], row_sems.at[row]).wait()

        width = -(-(band_rows + 2) // 8) * 8

        def edges_in():
            for copy, flat, first_row in zip(edge_copies, (lo_scr, hi_scr), (0, HALO + slab_depth)):
                copy.wait()
                for index in range(HALO):
                    a_scr[first_row + index] = flat[pl.ds(index * width, width), :]

        def out_copy(z):
            return [
                pltpu.make_async_copy(f_scr.at[z], feature_hbm.at[z], out_sems.at[0, z]),
                pltpu.make_async_copy(b_scr.at[z], best_hbm.at[z], out_sems.at[1, z]),
            ]

        def branch(value):
            def run_branch():
                compute(value, a_scr, s_scr, f_scr, None if first else p_scr, b_scr,
                        row_wait, prev_copy, out_copy, edges_in)
            return run_branch

        pick = jnp.clip(dil_ref[level_index], 1, DMAX) - 1
        lax.switch(pick, [branch(value) for value in range(1, DMAX + 1)])

    def run(dilations, low, middle, high, prev):
        block = jax.ShapeDtypeStruct((slab_depth, band_rows, row_length), jnp.float32)
        anywhere = pl.BlockSpec(memory_space=pl.ANY)
        in_specs = [pl.BlockSpec(memory_space=pltpu.SMEM), anywhere, anywhere, anywhere]
        operands = [dilations, low, middle, high]
        if not first:
            in_specs.append(anywhere)
            operands.append(prev)
        total_rows = planes + 2 * HALO - 2
        return pl.pallas_call(
            kernel,
            out_shape=(block, block),
            in_specs=in_specs,
            out_specs=(anywhere, anywhere),
            scratch_shapes=[
                pltpu.VMEM((total_rows, -(-(band_rows + 2) // 8) * 8, row_length), jnp.float32),
                pltpu.VMEM((planes, band_rows + 2, row_length), jnp.float32),
                pltpu.VMEM((slab_depth, band_rows, row_length), jnp.float32),
                pltpu.VMEM((slab_depth, band_rows, row_length), jnp.float32),
                pltpu.VMEM((slab_depth, band_rows, row_length), jnp.float32),
                pltpu.VMEM((HALO * -(-(band_rows + 2) // 8) * 8, row_length), jnp.float32),
                pltpu.VMEM((HALO * -(-(band_rows + 2) // 8) * 8, row_length), jnp.float32),
                pltpu.SemaphoreType.DMA((total_rows,)),
                pltpu.SemaphoreType.DMA((2, slab_depth)),
                pltpu.SemaphoreType.DMA((1,)),
                pltpu.SemaphoreType.DMA((2,)),
            ],
            compiler_params=pltpu.CompilerParams(vmem_limit_bytes=56 * 1024 * 1024),
        )(*operands)

    return run


def z_neighbours(block, width):
    count = lax.axis_size("gz")
    forward = [(i, i + 1) for i in range(count - 1)]
    forward.append((count - 1, 0))
    backward = [(target, source) for source, target in forward]
    def flat(part):
        return part.reshape(part.shape[0] * part.shape[1], part.shape[2])

    low = lax.ppermute(flat(lax.slice_in_dim(block, block.shape[0] - width, None, axis=0)), "gz", forward)
    high = lax.ppermute(flat(lax.slice_in_dim(block, 0, width, axis=0)), "gz", backward)
    return low, high


def invariants(curve_zz, curve_yy, curve_xx, curve_zy, curve_zx, curve_yx):
    trace_sum = curve_xx + curve_yy + curve_zz
    minor_sum = (
        curve_xx * curve_yy
        + curve_xx * curve_zz
        + curve_yy * curve_zz
        - curve_zy * curve_zy
        - curve_zx * curve_zx
        - curve_yx * curve_yx
    )
    return (trace_sum * trace_sum / 3.0 - minor_sum) * jax.nn.sigmoid(-trace_sum)


def signature(smoothed):
    centre = smoothed[1:-1, 1:-1]
    above_z = smoothed[2:, 1:-1]
    below_z = smoothed[:-2, 1:-1]
    above_y = smoothed[1:-1, 2:]
    below_y = smoothed[1:-1, :-2]
    curve_zz = hessian_scale * (above_z - 2.0 * centre + below_z)
    curve_yy = hessian_scale * (above_y - 2.0 * centre + below_y)
    curve_xx = hessian_scale * (jnp.roll(centre, -1, 2) - 2.0 * centre + jnp.roll(centre, 1, 2))
    curve_zy = (
        hessian_scale
        * 0.25
        * (smoothed[2:, 2:] - smoothed[2:, :-2] - smoothed[:-2, 2:] + smoothed[:-2, :-2])
    )
    curve_zx = (
        hessian_scale
        * 0.25
        * (
            jnp.roll(above_z, -1, 2)
            - jnp.roll(above_z, 1, 2)
            - jnp.roll(below_z, -1, 2)
            + jnp.roll(below_z, 1, 2)
        )
    )
    curve_yx = (
        hessian_scale
        * 0.25
        * (
            jnp.roll(above_y, -1, 2)
            - jnp.roll(above_y, 1, 2)
            - jnp.roll(below_y, -1, 2)
            + jnp.roll(below_y, 1, 2)
        )
    )
    return invariants(curve_zz, curve_yy, curve_xx, curve_zy, curve_zx, curve_yx)


def per_device(density, dilations, owner_rank, owner_slot, base_cell, corner_weights):
    slab_depth = density.shape[0]
    band_rows = density.shape[1]
    row_length = density.shape[2]
    banded = with_halo(density, (("gy", 1),), HALO)
    aligned_rows = -(-(band_rows + 2) // 8) * 8
    spare = jnp.zeros((slab_depth, aligned_rows - band_rows - 2, row_length), jnp.float32)
    banded = jnp.concatenate([banded, spare], axis=1)
    response = None
    features = []
    for level_index in range(SCALES):
        dilation = dilations[level_index]
        along_y = smooth_padded(banded, dilation, 1, aligned_rows - 2)
        low, high = z_neighbours(along_y, HALO)
        run = level_kernel(level_index, level_index == 0, slab_depth, band_rows, row_length)
        feature, response = run(dilations, low, along_y, high, response)
        features.append(feature.reshape(slab_depth * band_rows, row_length))
    plane = (band_rows - 1) * row_length
    z_index = base_cell // plane
    remainder = base_cell % plane
    y_index = remainder // row_length
    x_index = remainder % row_length
    entries = base_cell.shape[0]
    target_x = jnp.concatenate([x_index, (x_index + 1) % row_length])
    pick_x = (
        jnp.arange(row_length, dtype=jnp.int32)[:, None] == target_x[None, :]
    ).astype(jnp.float32)
    cells = jnp.arange(slab_depth * band_rows, dtype=jnp.int32)[:, None]
    weight_grid = None
    for step_z in (0, 1):
        for step_y in (0, 1):
            row = (z_index + step_z) * band_rows + y_index + step_y
            corner = 4 * step_z + 2 * step_y
            weights = jnp.concatenate([corner_weights[corner], corner_weights[corner + 1]])
            term = jnp.where(cells == jnp.concatenate([row, row])[None, :], weights[None, :], 0.0)
            weight_grid = term if weight_grid is None else weight_grid + term
    partials = []
    for feature in features:
        picked = jnp.dot(
            feature, pick_x, precision=lax.Precision.HIGH, preferred_element_type=jnp.float32
        )
        per_column = jnp.sum(picked * weight_grid, axis=0)
        partials.append(per_column[:entries] + per_column[entries:])
    partial_value = jnp.stack(partials)
    owner_group = owner_rank[:, 0]
    groups = lax.axis_size("gy")
    column = owner_group * HOWN + owner_slot
    onehot = (column[:, None] == jnp.arange(groups * HOWN, dtype=jnp.int32)[None, :]).astype(
        jnp.float32
    )
    spread = jnp.dot(
        partial_value, onehot, precision=lax.Precision.HIGH, preferred_element_type=jnp.float32
    )
    exchanged = lax.all_to_all(
        spread.reshape(SCALES, groups, HOWN), "gy", split_axis=1, concat_axis=1, tiled=True
    )
    catalogue = jnp.sum(exchanged, axis=1)
    return (response, catalogue)


def solution(mesh):
    placed = (
        P("gz", "gy", None),
        P(),
        P(("gz", "gy"), None),
        P(("gz", "gy")),
        P(("gz", "gy")),
        P(None, ("gz", "gy")),
    )
    return jax.shard_map(
        per_device,
        mesh=mesh,
        in_specs=placed,
        out_specs=(P("gz", "gy", None), P(None, ("gz", "gy"))),
        check_vma=False,
    )
```

```python
import jax
import jax.numpy as jnp
from jax import lax
from jax.experimental import pallas as pl
from jax.experimental.pallas import tpu as pltpu
from jax.sharding import PartitionSpec as P

SCALES = 3
HALO = 9
HOWN = 256
DMAX = 4


tap_weights = (0.0625, 0.25, 0.375, 0.25, 0.0625)
hessian_scale = 4.0


def flat_ppermute(part, axis, pairs):
    rows = part.shape[0] * part.shape[1]
    moved = lax.ppermute(part.reshape(rows, part.shape[2]), axis, pairs)
    return moved.reshape(part.shape)


def with_halo(block, sides, width):
    for axis, dim in sides:
        count = lax.axis_size(axis)
        forward = [(i, i + 1) for i in range(count - 1)]
        forward.append((count - 1, 0))
        backward = [(target, source) for source, target in forward]
        low = flat_ppermute(
            lax.slice_in_dim(block, block.shape[dim] - width, None, axis=dim), axis, forward
        )
        high = flat_ppermute(lax.slice_in_dim(block, 0, width, axis=dim), axis, backward)
        block = jnp.concatenate([low, block, high], axis=dim)
    return block


def smooth_padded(field_data, dilation, along_dim, extent):
    running = None
    for offset in range(5):
        start_at = HALO - 1 + (offset - 2) * dilation
        summand = tap_weights[offset] * lax.dynamic_slice_in_dim(
            field_data, start_at, extent + 2, along_dim
        )
        running = summand if running is None else running + summand
    return running


def smooth_periodic(field_data, dilation):
    running = None
    for offset in range(5):
        summand = tap_weights[offset] * jnp.roll(field_data, -(offset - 2) * dilation, axis=2)
        running = summand if running is None else running + summand
    return running


def level_kernel(level_index, first, slab_depth, band_rows, row_length):
    planes = slab_depth + 2

    def compute(dilation, a_scr, s_scr, feature_ref, prev_ref, best_ref, row_wait, prev_copy,
                out_copy, edges_in):
        reach = HALO - 1 + 2 * dilation
        last_mid = HALO + slab_depth - 1
        edges_in()
        for row in range(HALO, min(reach, last_mid + 1)):
            row_wait(row)

        def smooth_plane(plane, carry):
            @pl.when(reach + plane <= last_mid)
            def _():
                row_wait(reach + plane)

            for first_row in range(0, band_rows + 2, 8):
                rows = min(8, band_rows + 2 - first_row)
                def tap(offset):
                    source = HALO - 1 + plane + (offset - 2) * dilation
                    return a_scr[source, pl.ds(first_row, rows), :]

                along_z = (
                    tap_weights[0] * (tap(0) + tap(4))
                    + tap_weights[1] * (tap(1) + tap(3))
                    + tap_weights[2] * tap(2)
                )

                def moved(offset):
                    return pltpu.roll(along_z, (-(offset - 2) * dilation) % row_length, 1)

                running = (
                    tap_weights[0] * (moved(0) + moved(4))
                    + tap_weights[1] * (moved(1) + moved(3))
                    + tap_weights[2] * along_z
                )
                s_scr[plane, pl.ds(first_row, rows), :] = running
            return carry

        lax.fori_loop(0, planes, smooth_plane, 0)
        for row in range(max(reach + planes, HALO), last_mid + 1):
            row_wait(row)
        if prev_copy is not None:
            prev_copy.wait()

        def feature_plane(z, carry):
            for half in range(band_rows // 8):
                y0 = half * 8

                def at(dz, dy):
                    return s_scr[z + 1 + dz, pl.ds(1 + y0 + dy, 8), :]

                def left(v):
                    return pltpu.roll(v, row_length - 1, 1)

                def right(v):
                    return pltpu.roll(v, 1, 1)

                centre = at(0, 0)
                above_z = at(1, 0)
                below_z = at(-1, 0)
                curve_zz = hessian_scale * (above_z - 2.0 * centre + below_z)
                across_z = above_z - below_z
                curve_zx = (hessian_scale * 0.25) * (left(across_z) - right(across_z))
                above_y = at(0, 1)
                below_y = at(0, -1)
                curve_yy = hessian_scale * (above_y - 2.0 * centre + below_y)
                across_y = above_y - below_y
                curve_yx = (hessian_scale * 0.25) * (left(across_y) - right(across_y))
                curve_xx = hessian_scale * (left(centre) - 2.0 * centre + right(centre))
                trace_sum = curve_xx + curve_yy + curve_zz
                minor_sum = curve_xx * curve_yy + curve_xx * curve_zz + curve_yy * curve_zz
                minor_sum = minor_sum - curve_zx * curve_zx - curve_yx * curve_yx
                curve_zy = (hessian_scale * 0.25) * (at(1, 1) - at(1, -1) - at(-1, 1) + at(-1, -1))
                minor_sum = minor_sum - curve_zy * curve_zy
                value = (trace_sum * trace_sum / 3.0 - minor_sum) * (1.0 / (1.0 + jnp.exp(trace_sum)))
                feature_ref[z, pl.ds(y0, 8), :] = value
                if first:
                    best_ref[z, pl.ds(y0, 8), :] = value
                else:
                    best_ref[z, pl.ds(y0, 8), :] = jnp.maximum(prev_ref[z, pl.ds(y0, 8), :], value)
            for copy in out_copy(z):
                copy.start()
            return carry

        lax.fori_loop(0, slab_depth, feature_plane, 0)
        for z in range(slab_depth):
            for copy in out_copy(z):
                copy.wait()

    def kernel(*refs):
        if first:
            (dil_ref, lo_hbm, mid_hbm, hi_hbm, feature_hbm, best_hbm,
             a_scr, s_scr, f_scr, b_scr, p_scr, lo_scr, hi_scr, row_sems, out_sems, prev_sem,
             edge_sems) = refs
        else:
            (dil_ref, lo_hbm, mid_hbm, hi_hbm, prev_hbm, feature_hbm, best_hbm,
             a_scr, s_scr, f_scr, b_scr, p_scr, lo_scr, hi_scr, row_sems, out_sems, prev_sem,
             edge_sems) = refs
        edge_copies = [
            pltpu.make_async_copy(lo_hbm, lo_scr, edge_sems.at[0]),
            pltpu.make_async_copy(hi_hbm, hi_scr, edge_sems.at[1]),
        ]
        for copy in edge_copies:
            copy.start()
        for index in range(slab_depth):
            row = HALO + index
            pltpu.make_async_copy(mid_hbm.at[index], a_scr.at[row], row_sems.at[row]).start()
        prev_copy = None
        if not first:
            prev_copy = pltpu.make_async_copy(prev_hbm, p_scr, prev_sem.at[0])
            prev_copy.start()

        def row_wait(row):
            pltpu.make_async_copy(mid_hbm.at[0], a_scr.at[row], row_sems.at[row]).wait()

        width = band_rows + 2

        def edges_in():
            for copy, flat, first_row in zip(edge_copies, (lo_scr, hi_scr), (0, HALO + slab_depth)):
                copy.wait()
                for index in range(HALO):
                    a_scr[first_row + index] = flat[pl.ds(index * width, width), :]

        def out_copy(z):
            return [
                pltpu.make_async_copy(f_scr.at[z], feature_hbm.at[z], out_sems.at[0, z]),
                pltpu.make_async_copy(b_scr.at[z], best_hbm.at[z], out_sems.at[1, z]),
            ]

        def branch(value):
            def run_branch():
                compute(value, a_scr, s_scr, f_scr, None if first else p_scr, b_scr,
                        row_wait, prev_copy, out_copy, edges_in)
            return run_branch

        pick = jnp.clip(dil_ref[level_index], 1, DMAX) - 1
        lax.switch(pick, [branch(value) for value in range(1, DMAX + 1)])

    def run(dilations, low, middle, high, prev):
        block = jax.ShapeDtypeStruct((slab_depth, band_rows, row_length), jnp.float32)
        anywhere = pl.BlockSpec(memory_space=pl.ANY)
        in_specs = [pl.BlockSpec(memory_space=pltpu.SMEM), anywhere, anywhere, anywhere]
        operands = [dilations, low, middle, high]
        if not first:
            in_specs.append(anywhere)
            operands.append(prev)
        total_rows = planes + 2 * HALO - 2
        return pl.pallas_call(
            kernel,
            out_shape=(block, block),
            in_specs=in_specs,
            out_specs=(anywhere, anywhere),
            scratch_shapes=[
                pltpu.VMEM((total_rows, band_rows + 2, row_length), jnp.float32),
                pltpu.VMEM((planes, band_rows + 2, row_length), jnp.float32),
                pltpu.VMEM((slab_depth, band_rows, row_length), jnp.float32),
                pltpu.VMEM((slab_depth, band_rows, row_length), jnp.float32),
                pltpu.VMEM((slab_depth, band_rows, row_length), jnp.float32),
                pltpu.VMEM((HALO * (band_rows + 2), row_length), jnp.float32),
                pltpu.VMEM((HALO * (band_rows + 2), row_length), jnp.float32),
                pltpu.SemaphoreType.DMA((total_rows,)),
                pltpu.SemaphoreType.DMA((2, slab_depth)),
                pltpu.SemaphoreType.DMA((1,)),
                pltpu.SemaphoreType.DMA((2,)),
            ],
            compiler_params=pltpu.CompilerParams(vmem_limit_bytes=56 * 1024 * 1024),
        )(*operands)

    return run


def z_neighbours(block, width):
    count = lax.axis_size("gz")
    forward = [(i, i + 1) for i in range(count - 1)]
    forward.append((count - 1, 0))
    backward = [(target, source) for source, target in forward]
    def flat(part):
        return part.reshape(part.shape[0] * part.shape[1], part.shape[2])

    low = lax.ppermute(flat(lax.slice_in_dim(block, block.shape[0] - width, None, axis=0)), "gz", forward)
    high = lax.ppermute(flat(lax.slice_in_dim(block, 0, width, axis=0)), "gz", backward)
    return low, high


def invariants(curve_zz, curve_yy, curve_xx, curve_zy, curve_zx, curve_yx):
    trace_sum = curve_xx + curve_yy + curve_zz
    minor_sum = (
        curve_xx * curve_yy
        + curve_xx * curve_zz
        + curve_yy * curve_zz
        - curve_zy * curve_zy
        - curve_zx * curve_zx
        - curve_yx * curve_yx
    )
    return (trace_sum * trace_sum / 3.0 - minor_sum) * jax.nn.sigmoid(-trace_sum)


def signature(smoothed):
    centre = smoothed[1:-1, 1:-1]
    above_z = smoothed[2:, 1:-1]
    below_z = smoothed[:-2, 1:-1]
    above_y = smoothed[1:-1, 2:]
    below_y = smoothed[1:-1, :-2]
    curve_zz = hessian_scale * (above_z - 2.0 * centre + below_z)
    curve_yy = hessian_scale * (above_y - 2.0 * centre + below_y)
    curve_xx = hessian_scale * (jnp.roll(centre, -1, 2) - 2.0 * centre + jnp.roll(centre, 1, 2))
    curve_zy = (
        hessian_scale
        * 0.25
        * (smoothed[2:, 2:] - smoothed[2:, :-2] - smoothed[:-2, 2:] + smoothed[:-2, :-2])
    )
    curve_zx = (
        hessian_scale
        * 0.25
        * (
            jnp.roll(above_z, -1, 2)
            - jnp.roll(above_z, 1, 2)
            - jnp.roll(below_z, -1, 2)
            + jnp.roll(below_z, 1, 2)
        )
    )
    curve_yx = (
        hessian_scale
        * 0.25
        * (
            jnp.roll(above_y, -1, 2)
            - jnp.roll(above_y, 1, 2)
            - jnp.roll(below_y, -1, 2)
            + jnp.roll(below_y, 1, 2)
        )
    )
    return invariants(curve_zz, curve_yy, curve_xx, curve_zy, curve_zx, curve_yx)


def per_device(density, dilations, owner_rank, owner_slot, base_cell, corner_weights):
    slab_depth = density.shape[0]
    band_rows = density.shape[1]
    row_length = density.shape[2]
    banded = with_halo(density, (("gy", 1),), HALO)
    response = None
    features = []
    for level_index in range(SCALES):
        dilation = dilations[level_index]
        along_y = smooth_padded(banded, dilation, 1, band_rows)
        low, high = z_neighbours(along_y, HALO)
        run = level_kernel(level_index, level_index == 0, slab_depth, band_rows, row_length)
        feature, response = run(dilations, low, along_y, high, response)
        features.append(feature.reshape(slab_depth * band_rows, row_length))
    plane = (band_rows - 1) * row_length
    z_index = base_cell // plane
    remainder = base_cell % plane
    y_index = remainder // row_length
    x_index = remainder % row_length
    entries = base_cell.shape[0]
    target_x = jnp.concatenate([x_index, (x_index + 1) % row_length])
    pick_x = (
        jnp.arange(row_length, dtype=jnp.int32)[:, None] == target_x[None, :]
    ).astype(jnp.float32)
    cells = jnp.arange(slab_depth * band_rows, dtype=jnp.int32)[:, None]
    weight_grid = None
    for step_z in (0, 1):
        for step_y in (0, 1):
            row = (z_index + step_z) * band_rows + y_index + step_y
            corner = 4 * step_z + 2 * step_y
            weights = jnp.concatenate([corner_weights[corner], corner_weights[corner + 1]])
            term = jnp.where(cells == jnp.concatenate([row, row])[None, :], weights[None, :], 0.0)
            weight_grid = term if weight_grid is None else weight_grid + term
    partials = []
    for feature in features:
        picked = jnp.dot(
            feature, pick_x, precision=lax.Precision.HIGH, preferred_element_type=jnp.float32
        )
        per_column = jnp.sum(picked * weight_grid, axis=0)
        partials.append(per_column[:entries] + per_column[entries:])
    partial_value = jnp.stack(partials)
    owner_group = owner_rank[:, 0]
    groups = lax.axis_size("gy")
    column = owner_group * HOWN + owner_slot
    onehot = (column[:, None] == jnp.arange(groups * HOWN, dtype=jnp.int32)[None, :]).astype(
        jnp.float32
    )
    spread = jnp.dot(
        partial_value, onehot, precision=lax.Precision.HIGH, preferred_element_type=jnp.float32
    )
    exchanged = lax.all_to_all(
        spread.reshape(SCALES, groups, HOWN), "gy", split_axis=1, concat_axis=1, tiled=True
    )
    catalogue = jnp.sum(exchanged, axis=1)
    return (response, catalogue)


def solution(mesh):
    placed = (
        P("gz", "gy", None),
        P(),
        P(("gz", "gy"), None),
        P(("gz", "gy")),
        P(("gz", "gy")),
        P(None, ("gz", "gy")),
    )
    return jax.shard_map(
        per_device,
        mesh=mesh,
        in_specs=placed,
        out_specs=(P("gz", "gy", None), P(None, ("gz", "gy"))),
        check_vma=False,
    )
```
